32 devices in a mesh: grp: 2 (over x), limb: 8 (over z, y), coef: 2 (over core).
Axes of the slice: x: 2, y: 2, z: 4, core: 2. Of those that a mesh axis runs over, the one named last changes fastest.
Arguments:
- cipher: bfloat16 [16, 48, 128, 256], P(('grp', 'limb'), None, None, 'coef'), parts along dimension 0, may hold values from -6 to 6
- switch_key: bfloat16 [1, 3, 64, 128, 256], P(None, None, 'limb', None, 'coef'), may hold values from -3 to 3
- raise_table: bfloat16 [3, 48, 16], replicated, may hold values from -1.5 to 1.5
- lower_table: bfloat16 [48, 16], replicated, may hold values from -1.5 to 1.5
- special_inverse: float32 [48], replicated, may hold values from 0.5 to 2
Outputs:
- switched: bfloat16 [1, 16, 48, 128, 256], P(None, ('grp', 'limb'), None, None, 'coef'), parts along dimension 1
The draws below stay inside these ranges and needn't reach their ends.
There are 2 independent parts, one for each index of `grp`. The reference program is written for one: setup_inputs(seed, part) draws one part's arguments, and reference() takes and returns one part's arrays. A program takes and returns all parts, laid end to end along the dimension named above; an argument that names none is the same for every part. Nothing has to cross between parts.
All inputs are finite; a program needn't handle non-finite values.
Results may differ from the reference program's by a relative error of at most 0.018.
Values may be sent and summed in bfloat16 or wider, within the bound.
No kernel may reach another device: no remote copies, remote signals or barrier semaphores. Data moves between devices by JAX's collectives and lax.ppermute only.
A program may use at most 128 MiB of HBM per device.

```python
import math
import jax
import jax.numpy as jnp
from jax import lax

LIMBS = 48
SPECIAL = 16
DIGITS = 3
ROWS = 128
COLS = 256
KEYS = 1
DIGIT_LIMBS = 16
EXTENDED = 64
CYCLE = 32768
CIPHERS = 8


def block_levels(own_key, shape, shards, smallest, top_value):
    def one(dim, parts):
        steps = jax.random.uniform(jax.random.fold_in(jax.random.fold_in(own_key, 6), dim), (parts,), jnp.float32, smallest / len(shards), top_value / len(shards))
        return jnp.repeat(jnp.exp(steps), shape[dim] // parts).reshape((-1,) + (1,) * (len(shape) - dim - 1))

    factor_of = one(*shards[0])
    for cut in shards[1:]:
        factor_of = factor_of * one(*cut)
    return factor_of


def gaussian(stream_key, extent, width, reach, pieces=(), kind=jnp.bfloat16):
    gain = block_levels(stream_key, extent, pieces, -0.22, 0.18) if pieces else 1.0
    array = jax.random.normal(stream_key, extent, jnp.float32) * width * gain
    return jnp.minimum(jnp.maximum(array, -reach), reach).astype(kind)


def setup_inputs(seed: int = 0, part: int = 0) -> dict:
    seeds = jax.random.split(jax.random.key(seed), 6)
    own_keys = jax.random.split(jax.random.fold_in(seeds[5], part), 6)
    cipher = gaussian(own_keys[0], (CIPHERS, LIMBS, ROWS, COLS), 1.0, 6.0, ((0, 8), (3, 2)))
    switch_key = gaussian(seeds[1], (KEYS, DIGITS, EXTENDED, ROWS, COLS), 0.5, 3.0, ((2, 8), (4, 2)))
    raise_table = gaussian(seeds[2], (DIGITS, EXTENDED - DIGIT_LIMBS, DIGIT_LIMBS), DIGIT_LIMBS ** -0.5, 1.5)
    lower_table = gaussian(seeds[3], (LIMBS, SPECIAL), SPECIAL ** -0.5, 1.5)
    special_inverse = jnp.clip(jnp.exp(jax.random.uniform(seeds[4], (LIMBS,), jnp.float32, math.log(0.5), math.log(2.0))), 0.5, 2.0)
    return dict(cipher=cipher, switch_key=switch_key, raise_table=raise_table, lower_table=lower_table, special_inverse=special_inverse)


def cosine_table(size):
    freq = jnp.arange(size, dtype=jnp.float32)[:, None]
    place = jnp.arange(size, dtype=jnp.float32)[None, :]
    norm = jnp.where(freq == 0, math.sqrt(1.0 / size), math.sqrt(2.0 / size))
    return (norm * jnp.cos(math.pi * (2.0 * place + 1.0) * freq / (2.0 * size))).astype(jnp.bfloat16)

def twiddles(limbs, rows, cols):
    product = rows[:, None] * cols[None, :] % CYCLE
    scaled = product[None, :, :] * (2 * limbs + 1)[:, None, None] % CYCLE
    return 1.0 + 0.5 * jnp.cos(2.0 * math.pi / CYCLE * scaled.astype(jnp.float32))

def twists(limbs, rows, cols):
    position = rows[:, None] * COLS + cols[None, :]
    scaled = position[None, :, :] * (2 * limbs + 1)[:, None, None] % CYCLE
    return 1.0 + 0.5 * jnp.cos(2.0 * math.pi / CYCLE * scaled.astype(jnp.float32))

def forward(values, weights, twist, row_table, column_table):
    sectioned = (values.astype(jnp.float32) * twist).astype(jnp.bfloat16)
    half = jnp.einsum('...ab,kb->...ak', sectioned.astype(jnp.float32), column_table.astype(jnp.float32))
    half = (half * weights).astype(jnp.bfloat16)
    whole = jnp.einsum('ka,...ab->...kb', row_table.astype(jnp.float32), half.astype(jnp.float32))
    return whole.astype(jnp.bfloat16)

def inverse(values, weights, twist, row_table, column_table):
    half = jnp.einsum('ka,...kb->...ab', row_table.astype(jnp.float32), values.astype(jnp.float32))
    half = (half / weights).astype(jnp.bfloat16)
    whole = jnp.einsum('...ab,bn->...an', half.astype(jnp.float32), column_table.astype(jnp.float32))
    return (whole / twist).astype(jnp.bfloat16)

def reference(cipher, switch_key, raise_table, lower_table, special_inverse):
    row_table = cosine_table(ROWS)
    column_table = cosine_table(COLS)
    every_limb = jnp.arange(EXTENDED, dtype=jnp.int32)
    all_rows = jnp.arange(ROWS, dtype=jnp.int32)
    all_cols = jnp.arange(COLS, dtype=jnp.int32)
    weights = twiddles(every_limb, all_rows, all_cols)
    twist = twists(every_limb, all_rows, all_cols)

    def switch_one(single):
        coeffs = inverse(single, weights[:LIMBS], twist[:LIMBS], row_table, column_table)
        stacked = []
        for digit in range(DIGITS):
            first = digit * DIGIT_LIMBS
            block = coeffs[first:first + DIGIT_LIMBS]
            raised = jnp.einsum('ti,iab->tab', raise_table[digit].astype(jnp.float32), block.astype(jnp.float32)).astype(jnp.bfloat16)
            target_weights = jnp.concatenate([weights[:first], weights[first + DIGIT_LIMBS:]], axis=0)
            target_twist = jnp.concatenate([twist[:first], twist[first + DIGIT_LIMBS:]], axis=0)
            lifted = forward(raised, target_weights, target_twist, row_table, column_table)
            stacked.append(jnp.concatenate([lifted[:first], single[first:first + DIGIT_LIMBS], lifted[first:]], axis=0))
        extended = jnp.stack(stacked, axis=0)
        product = lax.optimization_barrier(jnp.sum(extended[None].astype(jnp.float32) * switch_key.astype(jnp.float32), axis=1)).astype(jnp.bfloat16)
        special = inverse(product[:, LIMBS:], weights[LIMBS:], twist[LIMBS:], row_table, column_table)
        lowered = jnp.einsum('ls,ksab->klab', lower_table.astype(jnp.float32), special.astype(jnp.float32)).astype(jnp.bfloat16)
        lowered_eval = forward(lowered, weights[:LIMBS], twist[:LIMBS], row_table, column_table)
        result = (product[:, :LIMBS].astype(jnp.float32) - lowered_eval.astype(jnp.float32)) * special_inverse[None, :, None, None]
        return result.astype(jnp.bfloat16)
    switched = lax.map(switch_one, cipher)
    return jnp.moveaxis(switched, 0, 1)
```

```python
import math

import jax
import jax.numpy as jnp
from jax import lax
from jax.experimental import pallas as pl
from jax.experimental.pallas import tpu as pltpu
from jax.sharding import PartitionSpec as P

LIMBS = 48
DIGITS = 3
DIGIT_LIMBS = 16
EXTENDED = 64
CYCLE = 32768
BLK = 16

F32 = jnp.float32
BF16 = jnp.bfloat16
I32 = jnp.int32


def cosine_table(size):
    freq = jnp.arange(size, dtype=jnp.float32)[:, None]
    place = jnp.arange(size, dtype=jnp.float32)[None, :]
    norm = jnp.where(freq == 0, math.sqrt(1.0 / size), math.sqrt(2.0 / size))
    return (norm * jnp.cos(math.pi * (2.0 * place + 1.0) * freq / (2.0 * size))).astype(
        jnp.bfloat16
    )


def _angle(phase):
    ang = (2.0 * math.pi / CYCLE) * phase.astype(F32)
    return jnp.cos(ang), jnp.sin(ang)


def _twiddle(p, q):
    cp, sp = _angle(p)
    cq, sq = _angle(q)
    cp, sp, cq, sq = lax.optimization_barrier((cp, sp, cq, sq))
    return 1.0 + 0.5 * (cp * cq - sp * sq)


def twiddle_tables(me, rows, cols, nc):
    rows_l, cols_l = rows // nc, cols // nc
    m = (2 * jnp.arange(EXTENDED, dtype=I32) + 1)[:, None, None, None]
    fine = jnp.arange(8, dtype=I32)[None, None, :, None]
    coarse = (8 * jnp.arange(rows // 8, dtype=I32))[None, :, None, None]
    bcol = (me * cols_l + jnp.arange(cols_l, dtype=I32))[None, None, None, :]
    w_col = _twiddle(
        (coarse * bcol) % CYCLE * m % CYCLE, (fine * bcol) % CYCLE * m % CYCLE
    ).reshape(EXTENDED, rows, cols_l)
    coarse = (me * rows_l + 8 * jnp.arange(rows_l // 8, dtype=I32))[None, :, None, None]
    ball = jnp.arange(cols, dtype=I32)[None, None, None, :]
    w_row = _twiddle(
        (coarse * ball) % CYCLE * m % CYCLE, (fine * ball) % CYCLE * m % CYCLE
    ).reshape(EXTENDED, rows_l, cols)
    v_row = _twiddle(
        (coarse * cols + ball) * m % CYCLE, (fine * cols) * m % CYCLE
    ).reshape(EXTENDED, rows_l, cols)
    return w_col, w_row, v_row


SMEM_SPEC = pl.BlockSpec(memory_space=pltpu.SMEM)


def _split_store(me_ref, first, second, own_ref, send_ref):
    top = me_ref[0] == 0

    @pl.when(top)
    def _():
        own_ref[...] = first
        send_ref[...] = second

    @pl.when(jnp.logical_not(top))
    def _():
        own_ref[...] = second
        send_ref[...] = first


def _inv_row_kernel(me_ref, y_ref, w_ref, ft_ref, own_ref, send_ref, h_ref):
    ft = ft_ref[...]
    n, rows, _ = y_ref.shape
    for l in range(n):
        h = jnp.dot(ft, y_ref[l], preferred_element_type=F32)
        h_ref[l] = (h / w_ref[l]).astype(BF16)
    half = rows // 2
    _split_store(me_ref, h_ref[:, :half, :], h_ref[:, half:, :], own_ref, send_ref)


def inv_row(me_arr, y, w_col, ft, e0):
    n, rows, cols_l = y.shape
    eb0 = e0 // BLK
    blk = pl.BlockSpec((BLK, rows, cols_l), lambda i: (i, 0, 0))
    out = pl.BlockSpec((BLK, rows // 2, cols_l), lambda i: (i, 0, 0))
    return pl.pallas_call(
        _inv_row_kernel,
        grid=(n // BLK,),
        in_specs=[
            SMEM_SPEC,
            blk,
            pl.BlockSpec((BLK, rows, cols_l), lambda i: (i + eb0, 0, 0)),
            pl.BlockSpec((rows, rows), lambda i: (0, 0)),
        ],
        out_specs=[out, out],
        out_shape=[jax.ShapeDtypeStruct((n, rows // 2, cols_l), BF16)] * 2,
        scratch_shapes=[pltpu.VMEM((BLK, rows, cols_l), BF16)],
    )(me_arr, y, w_col, ft)


def _inv_col_kernel(own_ref, recv_ref, v_ref, fo_ref, fr_ref, out_ref):
    n, rows_l, half = own_ref.shape
    a = own_ref[...].reshape(n * rows_l, half)
    b = recv_ref[...].reshape(n * rows_l, half)
    x = jnp.dot(a, fo_ref[...], preferred_element_type=F32)
    x = x + jnp.dot(b, fr_ref[...], preferred_element_type=F32)
    x = x.reshape(n, rows_l, -1)
    out_ref[...] = (x / v_ref[...]).astype(BF16)


def inv_col(own, recv, v_row, f_own, f_oth, e0):
    n, rows_l, half = own.shape
    cols = 2 * half
    eb0 = e0 // BLK
    blk = pl.BlockSpec((BLK, rows_l, half), lambda i: (i, 0, 0))
    return pl.pallas_call(
        _inv_col_kernel,
        grid=(n // BLK,),
        in_specs=[
            blk,
            blk,
            pl.BlockSpec((BLK, rows_l, cols), lambda i: (i + eb0, 0, 0)),
            pl.BlockSpec((half, cols), lambda i: (0, 0)),
            pl.BlockSpec((half, cols), lambda i: (0, 0)),
        ],
        out_specs=pl.BlockSpec((BLK, rows_l, cols), lambda i: (i, 0, 0)),
        out_shape=jax.ShapeDtypeStruct((n, rows_l, cols), BF16),
    )(own, recv, v_row, f_own, f_oth)


def _fwd_col_kernel(me_ref, x_ref, v_ref, w_ref, ft_ref, own_ref, send_ref):
    n, rows_l, cols = x_ref.shape
    g = (x_ref[...].astype(F32) * v_ref[...]).astype(BF16)
    h = jnp.dot(g.reshape(n * rows_l, cols), ft_ref[...], preferred_element_type=F32)
    h = (h.reshape(n, rows_l, cols) * w_ref[...]).astype(BF16)
    half = cols // 2
    _split_store(me_ref, h[:, :, :half], h[:, :, half:], own_ref, send_ref)


def fwd_col(me_arr, x, v_row, w_row, ft, table_block):
    groups, n, rows_l, cols = x.shape
    half = cols // 2
    xs = pl.BlockSpec((None, BLK, rows_l, cols), lambda j, t: (j, t, 0, 0))
    ts = pl.BlockSpec((BLK, rows_l, cols), lambda j, t: (table_block(j, t), 0, 0))
    os = pl.BlockSpec((None, BLK, rows_l, half), lambda j, t: (j, t, 0, 0))
    return pl.pallas_call(
        _fwd_col_kernel,
        grid=(groups, n // BLK),
        in_specs=[SMEM_SPEC, xs, ts, ts, pl.BlockSpec((cols, cols), lambda j, t: (0, 0))],
        out_specs=[os, os],
        out_shape=[jax.ShapeDtypeStruct((groups, n, rows_l, half), BF16)] * 2,
    )(me_arr, x, v_row, w_row, ft)


def _product_kernel(eb0, fo_ref, fr_ref, cip_ref, key_ref, *rest):
    halves = rest[: 2 * DIGITS]
    out_ref, acc_ref = rest[2 * DIGITS :]
    eb = pl.program_id(0) + eb0
    fo = fo_ref[...]
    fr = fr_ref[...]
    acc_ref[...] = jnp.zeros_like(acc_ref)
    n = acc_ref.shape[0]
    for j in range(DIGITS):
        own_ref, recv_ref = halves[2 * j], halves[2 * j + 1]

        @pl.when(eb == j)
        def _():
            acc_ref[...] += cip_ref[...].astype(F32) * key_ref[j].astype(F32)

        @pl.when(eb != j)
        def _():
            for l in range(n):
                y = jnp.dot(fo, own_ref[l], preferred_element_type=F32)
                y = (y + jnp.dot(fr, recv_ref[l], preferred_element_type=F32)).astype(BF16)
                acc_ref[l] += y.astype(F32) * key_ref[j, l].astype(F32)

    out_ref[...] = acc_ref[...].astype(BF16)


def product(cip, key, own2, recv2, f_own, f_oth, eb0, nblocks):
    _, rows, cols_l = cip.shape
    rows_l = rows // 2

    def lifted_block(j):
        def index(i):
            eb = i + eb0
            tb = jnp.where(eb < j, eb, eb - 1)
            return (j, jnp.clip(tb, 0, DIGITS - 1), 0, 0)

        return pl.BlockSpec((None, BLK, rows_l, cols_l), index)

    half_specs = []
    half_args = []
    for j in range(DIGITS):
        half_specs += [lifted_block(j), lifted_block(j)]
        half_args += [own2, recv2]
    return pl.pallas_call(
        lambda *refs: _product_kernel(eb0, *refs),
        grid=(nblocks,),
        in_specs=[
            pl.BlockSpec((rows, rows_l), lambda i: (0, 0)),
            pl.BlockSpec((rows, rows_l), lambda i: (0, 0)),
            pl.BlockSpec(
                (BLK, rows, cols_l), lambda i: (jnp.minimum(i + eb0, DIGITS - 1), 0, 0)
            ),
            pl.BlockSpec((DIGITS, BLK, rows, cols_l), lambda i: (0, i + eb0, 0, 0)),
        ]
        + half_specs,
        out_specs=pl.BlockSpec((BLK, rows, cols_l), lambda i: (i, 0, 0)),
        out_shape=jax.ShapeDtypeStruct((nblocks * BLK, rows, cols_l), BF16),
        scratch_shapes=[pltpu.VMEM((BLK, rows, cols_l), F32)],
    )(f_own, f_oth, cip, key, *half_args)


def _final_kernel(fo_ref, fr_ref, own_ref, recv_ref, prod_ref, s_ref, out_ref):
    fo = fo_ref[...]
    fr = fr_ref[...]
    for l in range(own_ref.shape[0]):
        y = jnp.dot(fo, own_ref[l], preferred_element_type=F32)
        y = (y + jnp.dot(fr, recv_ref[l], preferred_element_type=F32)).astype(BF16)
        diff = prod_ref[l].astype(F32) - y.astype(F32)
        out_ref[l] = (diff * s_ref[l]).astype(BF16)


def final(own4, recv4, prod, scale, f_own, f_oth):
    n, rows, cols_l = prod.shape
    rows_l = rows // 2
    hs = pl.BlockSpec((BLK, rows_l, cols_l), lambda i: (i, 0, 0))
    return pl.pallas_call(
        _final_kernel,
        grid=(n // BLK,),
        in_specs=[
            pl.BlockSpec((rows, rows_l), lambda i: (0, 0)),
            pl.BlockSpec((rows, rows_l), lambda i: (0, 0)),
            hs,
            hs,
            pl.BlockSpec((BLK, rows, cols_l), lambda i: (i, 0, 0)),
            pl.BlockSpec((BLK, 1, cols_l), lambda i: (i, 0, 0)),
        ],
        out_specs=pl.BlockSpec((BLK, rows, cols_l), lambda i: (i, 0, 0)),
        out_shape=jax.ShapeDtypeStruct((n, rows, cols_l), BF16),
    )(f_own, f_oth, own4, recv4, prod, scale)


def swap(x):
    return lax.ppermute(x, "coef", perm=[(0, 1), (1, 0)])


def body(cipher, switch_key, raise_table, lower_table, special_inverse):
    nc = lax.axis_size("coef")
    me = lax.axis_index("coef")
    me_arr = jnp.reshape(me, (1,)).astype(I32)
    other = 1 - me
    _, limbs, rows, cols_l = cipher.shape
    cols = cols_l * nc
    rows_l = rows // nc

    key = lax.all_gather(switch_key, "limb", axis=2, tiled=True)[0]

    f_rows = cosine_table(rows)
    f_cols = cosine_table(cols)
    ft_rows = f_rows.T
    ft_cols = f_cols.T
    fc_own = lax.dynamic_slice_in_dim(f_cols, me * cols_l, cols_l, axis=0)
    fc_oth = lax.dynamic_slice_in_dim(f_cols, other * cols_l, cols_l, axis=0)
    fr_own = lax.dynamic_slice_in_dim(f_rows, me * rows_l, rows_l, axis=1)
    fr_oth = lax.dynamic_slice_in_dim(f_rows, other * rows_l, rows_l, axis=1)
    w_col, w_row, v_row = twiddle_tables(me, rows, cols, nc)

    ct = cipher[0]
    own1, send1 = inv_row(me_arr, ct, w_col, ft_rows, 0)
    coeffs = inv_col(own1, swap(send1), v_row, fc_own, fc_oth, 0)

    blocks = coeffs.reshape(DIGITS, DIGIT_LIMBS, rows_l * cols)
    raised = lax.dot_general(
        raise_table, blocks, (((2,), (1,)), ((0,), (0,))), preferred_element_type=F32
    )
    raised = raised.astype(BF16).reshape(DIGITS, limbs, rows_l, cols)

    own2, send2 = fwd_col(
        me_arr, raised, v_row, w_row, ft_cols, lambda j, t: jnp.where(t >= j, t + 1, t)
    )
    recv2 = swap(send2)

    prod_special = product(ct, key, own2, recv2, fr_own, fr_oth, DIGITS, 1)
    prod_cipher = product(ct, key, own2, recv2, fr_own, fr_oth, 0, DIGITS)

    own3, send3 = inv_row(me_arr, prod_special, w_col, ft_rows, limbs)
    special = inv_col(own3, swap(send3), v_row, fc_own, fc_oth, limbs)
    lowered = jnp.dot(
        lower_table, special.reshape(DIGIT_LIMBS, rows_l * cols), preferred_element_type=F32
    )
    lowered = lowered.astype(BF16).reshape(1, limbs, rows_l, cols)
    own4, send4 = fwd_col(me_arr, lowered, v_row, w_row, ft_cols, lambda j, t: t)
    scale = jnp.broadcast_to(special_inverse[:, None, None], (limbs, 1, cols_l))
    result = final(own4[0], swap(send4)[0], prod_cipher, scale, fr_own, fr_oth)
    return result[None, None]


def solution(mesh):
    in_specs = (
        P(("grp", "limb"), None, None, "coef"),
        P(None, None, "limb", None, "coef"),
        P(),
        P(),
        P(),
    )
    out_specs = P(None, ("grp", "limb"), None, None, "coef")
    return jax.shard_map(body, mesh=mesh, in_specs=in_specs, out_specs=out_specs, check_vma=False)
```

```python
import math

import jax
import jax.numpy as jnp
from jax import lax
from jax.experimental import pallas as pl
from jax.experimental.pallas import tpu as pltpu
from jax.sharding import PartitionSpec as P

LIMBS = 48
DIGITS = 3
DIGIT_LIMBS = 16
EXTENDED = 64
CYCLE = 32768
BLK = 16

F32 = jnp.float32
BF16 = jnp.bfloat16
I32 = jnp.int32


def cosine_table(size):
    freq = jnp.arange(size, dtype=jnp.float32)[:, None]
    place = jnp.arange(size, dtype=jnp.float32)[None, :]
    norm = jnp.where(freq == 0, math.sqrt(1.0 / size), math.sqrt(2.0 / size))
    return (norm * jnp.cos(math.pi * (2.0 * place + 1.0) * freq / (2.0 * size))).astype(
        jnp.bfloat16
    )


def _angle(phase):
    ang = (2.0 * math.pi / CYCLE) * phase.astype(F32)
    return jnp.cos(ang), jnp.sin(ang)


def _twiddle(p, q):
    cp, sp = _angle(p)
    cq, sq = _angle(q)
    cp, sp, cq, sq = lax.optimization_barrier((cp, sp, cq, sq))
    return 1.0 + 0.5 * (cp * cq - sp * sq)


def twiddle_tables(me, rows, cols, nc):
    rows_l, cols_l = rows // nc, cols // nc
    m = (2 * jnp.arange(EXTENDED, dtype=I32) + 1)[:, None, None, None]
    fine = jnp.arange(8, dtype=I32)[None, None, :, None]
    coarse = (8 * jnp.arange(rows // 8, dtype=I32))[None, :, None, None]
    bcol = (me * cols_l + jnp.arange(cols_l, dtype=I32))[None, None, None, :]
    w_col = _twiddle(
        (coarse * bcol) % CYCLE * m % CYCLE, (fine * bcol) % CYCLE * m % CYCLE
    ).reshape(EXTENDED, rows, cols_l)
    coarse = (me * rows_l + 8 * jnp.arange(rows_l // 8, dtype=I32))[None, :, None, None]
    ball = jnp.arange(cols, dtype=I32)[None, None, None, :]
    w_row = _twiddle(
        (coarse * ball) % CYCLE * m % CYCLE, (fine * ball) % CYCLE * m % CYCLE
    ).reshape(EXTENDED, rows_l, cols)
    v_row = _twiddle(
        (coarse * cols + ball) * m % CYCLE, (fine * cols) * m % CYCLE
    ).reshape(EXTENDED, rows_l, cols)
    return w_col, w_row, v_row


SMEM_SPEC = pl.BlockSpec(memory_space=pltpu.SMEM)


def _split_store(me_ref, first, second, own_ref, send_ref):
    top = me_ref[0] == 0

    @pl.when(top)
    def _():
        own_ref[...] = first
        send_ref[...] = second

    @pl.when(jnp.logical_not(top))
    def _():
        own_ref[...] = second
        send_ref[...] = first


def _inv_row_kernel(me_ref, y_ref, w_ref, ft_ref, own_ref, send_ref, h_ref):
    ft = ft_ref[...]
    n, rows, _ = y_ref.shape
    for l in range(n):
        h = jnp.dot(ft, y_ref[l], preferred_element_type=F32)
        h_ref[l] = (h / w_ref[l]).astype(BF16)
    half = rows // 2
    _split_store(me_ref, h_ref[:, :half, :], h_ref[:, half:, :], own_ref, send_ref)


def inv_row(me_arr, y, w_col, ft, e0):
    n, rows, cols_l = y.shape
    eb0 = e0 // BLK
    blk = pl.BlockSpec((BLK, rows, cols_l), lambda i: (i, 0, 0))
    out = pl.BlockSpec((BLK, rows // 2, cols_l), lambda i: (i, 0, 0))
    return pl.pallas_call(
        _inv_row_kernel,
        grid=(n // BLK,),
        in_specs=[
            SMEM_SPEC,
            blk,
            pl.BlockSpec((BLK, rows, cols_l), lambda i: (i + eb0, 0, 0)),
            pl.BlockSpec((rows, rows), lambda i: (0, 0)),
        ],
        out_specs=[out, out],
        out_shape=[jax.ShapeDtypeStruct((n, rows // 2, cols_l), BF16)] * 2,
        scratch_shapes=[pltpu.VMEM((BLK, rows, cols_l), BF16)],
    )(me_arr, y, w_col, ft)


def _inv_col_kernel(own_ref, recv_ref, v_ref, fo_ref, fr_ref, out_ref):
    n, rows_l, half = own_ref.shape
    a = own_ref[...].reshape(n * rows_l, half)
    b = recv_ref[...].reshape(n * rows_l, half)
    x = jnp.dot(a, fo_ref[...], preferred_element_type=F32)
    x = x + jnp.dot(b, fr_ref[...], preferred_element_type=F32)
    x = x.reshape(n, rows_l, -1)
    out_ref[...] = (x / v_ref[...]).astype(BF16)


def inv_col(own, recv, v_row, f_own, f_oth, e0):
    n, rows_l, half = own.shape
    cols = 2 * half
    eb0 = e0 // BLK
    blk = pl.BlockSpec((BLK, rows_l, half), lambda i: (i, 0, 0))
    return pl.pallas_call(
        _inv_col_kernel,
        grid=(n // BLK,),
        in_specs=[
            blk,
            blk,
            pl.BlockSpec((BLK, rows_l, cols), lambda i: (i + eb0, 0, 0)),
            pl.BlockSpec((half, cols), lambda i: (0, 0)),
            pl.BlockSpec((half, cols), lambda i: (0, 0)),
        ],
        out_specs=pl.BlockSpec((BLK, rows_l, cols), lambda i: (i, 0, 0)),
        out_shape=jax.ShapeDtypeStruct((n, rows_l, cols), BF16),
    )(own, recv, v_row, f_own, f_oth)


def _fwd_col_kernel(me_ref, x_ref, v_ref, w_ref, ft_ref, own_ref, send_ref):
    n, rows_l, cols = x_ref.shape
    g = (x_ref[...].astype(F32) * v_ref[...]).astype(BF16)
    h = jnp.dot(g.reshape(n * rows_l, cols), ft_ref[...], preferred_element_type=F32)
    h = (h.reshape(n, rows_l, cols) * w_ref[...]).astype(BF16)
    half = cols // 2
    _split_store(me_ref, h[:, :, :half], h[:, :, half:], own_ref, send_ref)


def fwd_col(me_arr, x, v_row, w_row, ft, table_block):
    groups, n, rows_l, cols = x.shape
    half = cols // 2
    xs = pl.BlockSpec((None, BLK, rows_l, cols), lambda j, t: (j, t, 0, 0))
    ts = pl.BlockSpec((BLK, rows_l, cols), lambda j, t: (table_block(j, t), 0, 0))
    os = pl.BlockSpec((None, BLK, rows_l, half), lambda j, t: (j, t, 0, 0))
    return pl.pallas_call(
        _fwd_col_kernel,
        grid=(groups, n // BLK),
        in_specs=[SMEM_SPEC, xs, ts, ts, pl.BlockSpec((cols, cols), lambda j, t: (0, 0))],
        out_specs=[os, os],
        out_shape=[jax.ShapeDtypeStruct((groups, n, rows_l, half), BF16)] * 2,
    )(me_arr, x, v_row, w_row, ft)


def _product_kernel(eb0, fo_ref, fr_ref, cip_ref, key_ref, *rest):
    halves = rest[: 2 * DIGITS]
    out_ref, acc_ref = rest[2 * DIGITS :]
    eb = pl.program_id(0) + eb0
    fo = fo_ref[...]
    fr = fr_ref[...]
    acc_ref[...] = jnp.zeros_like(acc_ref)
    n = acc_ref.shape[0]
    for j in range(DIGITS):
        own_ref, recv_ref = halves[2 * j], halves[2 * j + 1]

        @pl.when(eb == j)
        def _():
            acc_ref[...] += cip_ref[...].astype(F32) * key_ref[j].astype(F32)

        @pl.when(eb != j)
        def _():
            for l in range(n):
                y = jnp.dot(fo, own_ref[l], preferred_element_type=F32)
                y = (y + jnp.dot(fr, recv_ref[l], preferred_element_type=F32)).astype(BF16)
                acc_ref[l] += y.astype(F32) * key_ref[j, l].astype(F32)

    out_ref[...] = acc_ref[...].astype(BF16)


def product(cip, key, own2, recv2, f_own, f_oth, eb0, nblocks):
    _, rows, cols_l = cip.shape
    rows_l = rows // 2

    def lifted_block(j):
        def index(i):
            eb = i + eb0
            tb = jnp.where(eb < j, eb, eb - 1)
            return (j, jnp.clip(tb, 0, DIGITS - 1), 0, 0)

        return pl.BlockSpec((None, BLK, rows_l, cols_l), index)

    half_specs = []
    half_args = []
    for j in range(DIGITS):
        half_specs += [lifted_block(j), lifted_block(j)]
        half_args += [own2, recv2]
    return pl.pallas_call(
        lambda *refs: _product_kernel(eb0, *refs),
        grid=(nblocks,),
        in_specs=[
            pl.BlockSpec((rows, rows_l), lambda i: (0, 0)),
            pl.BlockSpec((rows, rows_l), lambda i: (0, 0)),
            pl.BlockSpec(
                (BLK, rows, cols_l), lambda i: (jnp.minimum(i + eb0, DIGITS - 1), 0, 0)
            ),
            pl.BlockSpec((DIGITS, BLK, rows, cols_l), lambda i: (0, i + eb0, 0, 0)),
        ]
        + half_specs,
        out_specs=pl.BlockSpec((BLK, rows, cols_l), lambda i: (i, 0, 0)),
        out_shape=jax.ShapeDtypeStruct((nblocks * BLK, rows, cols_l), BF16),
        scratch_shapes=[pltpu.VMEM((BLK, rows, cols_l), F32)],
    )(f_own, f_oth, cip, key, *half_args)


def _final_kernel(fo_ref, fr_ref, own_ref, recv_ref, prod_ref, s_ref, out_ref):
    fo = fo_ref[...]
    fr = fr_ref[...]
    for l in range(own_ref.shape[0]):
        y = jnp.dot(fo, own_ref[l], preferred_element_type=F32)
        y = (y + jnp.dot(fr, recv_ref[l], preferred_element_type=F32)).astype(BF16)
        diff = prod_ref[l].astype(F32) - y.astype(F32)
        out_ref[l] = (diff * s_ref[l]).astype(BF16)


def final(own4, recv4, prod, scale, f_own, f_oth):
    n, rows, cols_l = prod.shape
    rows_l = rows // 2
    hs = pl.BlockSpec((BLK, rows_l, cols_l), lambda i: (i, 0, 0))
    return pl.pallas_call(
        _final_kernel,
        grid=(n // BLK,),
        in_specs=[
            pl.BlockSpec((rows, rows_l), lambda i: (0, 0)),
            pl.BlockSpec((rows, rows_l), lambda i: (0, 0)),
            hs,
            hs,
            pl.BlockSpec((BLK, rows, cols_l), lambda i: (i, 0, 0)),
            pl.BlockSpec((BLK, 1, cols_l), lambda i: (i, 0, 0)),
        ],
        out_specs=pl.BlockSpec((BLK, rows, cols_l), lambda i: (i, 0, 0)),
        out_shape=jax.ShapeDtypeStruct((n, rows, cols_l), BF16),
    )(f_own, f_oth, own4, recv4, prod, scale)


def snake_ring(n):
    if n % 2:
        return list(range(n))
    outer = n // 2
    return [2 * a for a in range(outer)] + [2 * a + 1 for a in reversed(range(outer))]


def ring_setup(shard):
    n = lax.axis_size("limb")
    me_l = lax.axis_index("limb")
    order = snake_ring(n)
    pos = [0] * n
    for i, l in enumerate(order):
        pos[l] = i
    width = shard.shape[1]
    full = jnp.zeros((shard.shape[0], n * width) + shard.shape[2:], shard.dtype)
    full = lax.dynamic_update_slice_in_dim(full, shard, me_l * width, axis=1)
    return dict(
        n=n,
        order=jnp.array(order, I32),
        p=jnp.array(pos, I32)[me_l],
        cw=[(order[i], order[(i + 1) % n]) for i in range(n)],
        ccw=[(order[i], order[(i - 1) % n]) for i in range(n)],
        width=width,
        full=full,
        a=shard,
        b=shard,
        s=0,
    )


def ring_steps(st):
    return st["n"] // 2


def ring_step(st):
    n, width, order, p = st["n"], st["width"], st["order"], st["p"]
    st["s"] += 1
    s = st["s"]
    if 2 * s < n:
        st["a"] = lax.ppermute(st["a"], "limb", st["cw"])
        st["b"] = lax.ppermute(st["b"], "limb", st["ccw"])
        st["full"] = lax.dynamic_update_slice_in_dim(
            st["full"], st["a"], order[(p - s) % n] * width, axis=1
        )
        st["full"] = lax.dynamic_update_slice_in_dim(
            st["full"], st["b"], order[(p + s) % n] * width, axis=1
        )
    else:
        h = st["a"].shape[2] // 2
        a = lax.ppermute(st["a"][:, :, :h], "limb", st["cw"])
        b = lax.ppermute(st["b"][:, :, h:], "limb", st["ccw"])
        src = order[(p + s) % n] * width
        st["full"] = lax.dynamic_update_slice_in_dim(
            st["full"], jnp.concatenate([a, b], axis=2), src, axis=1
        )


def ring_hold(st, x):
    if st["s"] >= ring_steps(st):
        return x
    st["a"], st["b"], x = lax.optimization_barrier((st["a"], st["b"], x))
    ring_step(st)
    return x


def ring_finish(st):
    while st["s"] < ring_steps(st):
        ring_step(st)
    return st["full"]

def swap(x):
    return lax.ppermute(x, "coef", perm=[(0, 1), (1, 0)])


def body(cipher, switch_key, raise_table, lower_table, special_inverse):
    nc = lax.axis_size("coef")
    me = lax.axis_index("coef")
    me_arr = jnp.reshape(me, (1,)).astype(I32)
    other = 1 - me
    _, limbs, rows, cols_l = cipher.shape
    cols = cols_l * nc
    rows_l = rows // nc

    ring = ring_setup(switch_key[0])
    if ring_steps(ring):
        ring_step(ring)

    f_rows = cosine_table(rows)
    f_cols = cosine_table(cols)
    ft_rows = f_rows.T
    ft_cols = f_cols.T
    fc_own = lax.dynamic_slice_in_dim(f_cols, me * cols_l, cols_l, axis=0)
    fc_oth = lax.dynamic_slice_in_dim(f_cols, other * cols_l, cols_l, axis=0)
    fr_own = lax.dynamic_slice_in_dim(f_rows, me * rows_l, rows_l, axis=1)
    fr_oth = lax.dynamic_slice_in_dim(f_rows, other * rows_l, rows_l, axis=1)
    w_col, w_row, v_row = twiddle_tables(me, rows, cols, nc)

    ct = cipher[0]
    own1, send1 = inv_row(me_arr, ct, w_col, ft_rows, 0)
    own1 = ring_hold(ring, own1)
    coeffs = inv_col(own1, swap(send1), v_row, fc_own, fc_oth, 0)

    blocks = coeffs.reshape(DIGITS, DIGIT_LIMBS, rows_l * cols)
    raised = lax.dot_general(
        raise_table, blocks, (((2,), (1,)), ((0,), (0,))), preferred_element_type=F32
    )
    raised = raised.astype(BF16).reshape(DIGITS, limbs, rows_l, cols)

    raised = ring_hold(ring, raised)
    own2, send2 = fwd_col(
        me_arr, raised, v_row, w_row, ft_cols, lambda j, t: jnp.where(t >= j, t + 1, t)
    )
    own2, send2 = ring_hold(ring, (own2, send2))
    recv2 = swap(send2)
    key = ring_finish(ring)

    prod_special = product(ct, key, own2, recv2, fr_own, fr_oth, DIGITS, 1)
    prod_cipher = product(ct, key, own2, recv2, fr_own, fr_oth, 0, DIGITS)

    own3, send3 = inv_row(me_arr, prod_special, w_col, ft_rows, limbs)
    special = inv_col(own3, swap(send3), v_row, fc_own, fc_oth, limbs)
    lowered = jnp.dot(
        lower_table, special.reshape(DIGIT_LIMBS, rows_l * cols), preferred_element_type=F32
    )
    lowered = lowered.astype(BF16).reshape(1, limbs, rows_l, cols)
    own4, send4 = fwd_col(me_arr, lowered, v_row, w_row, ft_cols, lambda j, t: t)
    scale = jnp.broadcast_to(special_inverse[:, None, None], (limbs, 1, cols_l))
    result = final(own4[0], swap(send4)[0], prod_cipher, scale, fr_own, fr_oth)
    return result[None, None]


def solution(mesh):
    in_specs = (
        P(("grp", "limb"), None, None, "coef"),
        P(None, None, "limb", None, "coef"),
        P(),
        P(),
        P(),
    )
    out_specs = P(None, ("grp", "limb"), None, None, "coef")
    return jax.shard_map(body, mesh=mesh, in_specs=in_specs, out_specs=out_specs, check_vma=False)
```

```python
import math

import jax
import ml_dtypes
import numpy as np
import jax.numpy as jnp
from jax import lax
from jax.experimental import pallas as pl
from jax.experimental.pallas import tpu as pltpu
from jax.sharding import PartitionSpec as P

LIMBS = 48
DIGITS = 3
DIGIT_LIMBS = 16
EXTENDED = 64
CYCLE = 32768
BLK = 16

F32 = jnp.float32
BF16 = jnp.bfloat16
I32 = jnp.int32


def cosine_table(size):
    freq = np.arange(size, dtype=np.float64)[:, None]
    place = np.arange(size, dtype=np.float64)[None, :]
    norm = np.where(freq == 0, math.sqrt(1.0 / size), math.sqrt(2.0 / size))
    return (norm * np.cos(math.pi * (2.0 * place + 1.0) * freq / (2.0 * size))).astype(
        ml_dtypes.bfloat16
    )


def _angle(phase):
    ang = (2.0 * math.pi / CYCLE) * phase.astype(F32)
    return jnp.cos(ang), jnp.sin(ang)


def _limb_angle(c):
    shape = (-1,) + (1,) * c.ndim
    hi = jnp.arange(EXTENDED // 8, dtype=I32).reshape(shape)
    lo = (2 * jnp.arange(8, dtype=I32) + 1).reshape(shape)
    ch, sh = _angle((16 * hi * c[None]) % CYCLE)
    cl, sl = _angle((lo * c[None]) % CYCLE)
    cos = ch[:, None] * cl[None] - sh[:, None] * sl[None]
    sin = sh[:, None] * cl[None] + ch[:, None] * sl[None]
    return cos.reshape((EXTENDED,) + c.shape), sin.reshape((EXTENDED,) + c.shape)


def _twiddle(p, q):
    cp, sp = _limb_angle(p % CYCLE)
    cq, sq = _limb_angle(q % CYCLE)
    cp, sp, cq, sq = lax.optimization_barrier((cp, sp, cq, sq))
    return 1.0 + 0.5 * (cp * cq - sp * sq)


def twiddle_tables(me, rows, cols, nc):
    rows_l, cols_l = rows // nc, cols // nc
    fine = jnp.arange(8, dtype=I32)[None, :, None]
    coarse = (8 * jnp.arange(rows // 8, dtype=I32))[:, None, None]
    bcol = (me * cols_l + jnp.arange(cols_l, dtype=I32))[None, None, :]
    w_col = _twiddle(coarse * bcol, fine * bcol).reshape(EXTENDED, rows, cols_l)
    coarse = (me * rows_l + 8 * jnp.arange(rows_l // 8, dtype=I32))[:, None, None]
    ball = jnp.arange(cols, dtype=I32)[None, None, :]
    w_row = _twiddle(coarse * ball, fine * ball).reshape(EXTENDED, rows_l, cols)
    v_row = _twiddle(coarse * cols + ball, fine * cols).reshape(EXTENDED, rows_l, cols)
    return w_col, w_row, v_row


SMEM_SPEC = pl.BlockSpec(memory_space=pltpu.SMEM)


def _split_store(me_ref, first, second, own_ref, send_ref):
    top = me_ref[0] == 0

    @pl.when(top)
    def _():
        own_ref[...] = first
        send_ref[...] = second

    @pl.when(jnp.logical_not(top))
    def _():
        own_ref[...] = second
        send_ref[...] = first


def _inv_row_kernel(me_ref, y_ref, w_ref, ft_ref, own_ref, send_ref, h_ref):
    ft = ft_ref[...]
    n, rows, _ = y_ref.shape
    for l in range(n):
        h = jnp.dot(ft, y_ref[l], preferred_element_type=F32)
        h_ref[l] = (h / w_ref[l]).astype(BF16)
    half = rows // 2
    _split_store(me_ref, h_ref[:, :half, :], h_ref[:, half:, :], own_ref, send_ref)


def inv_row(me_arr, y, w_col, ft, e0):
    n, rows, cols_l = y.shape
    eb0 = e0 // BLK
    blk = pl.BlockSpec((BLK, rows, cols_l), lambda i: (i, 0, 0))
    out = pl.BlockSpec((BLK, rows // 2, cols_l), lambda i: (i, 0, 0))
    return pl.pallas_call(
        _inv_row_kernel,
        grid=(n // BLK,),
        in_specs=[
            SMEM_SPEC,
            blk,
            pl.BlockSpec((BLK, rows, cols_l), lambda i: (i + eb0, 0, 0)),
            pl.BlockSpec((rows, rows), lambda i: (0, 0)),
        ],
        out_specs=[out, out],
        out_shape=[jax.ShapeDtypeStruct((n, rows // 2, cols_l), BF16)] * 2,
        scratch_shapes=[pltpu.VMEM((BLK, rows, cols_l), BF16)],
    )(me_arr, y, w_col, ft)


def _inv_col_kernel(own_ref, recv_ref, v_ref, fo_ref, fr_ref, out_ref):
    n, rows_l, half = own_ref.shape
    a = own_ref[...].reshape(n * rows_l, half)
    b = recv_ref[...].reshape(n * rows_l, half)
    x = jnp.dot(a, fo_ref[...], preferred_element_type=F32)
    x = x + jnp.dot(b, fr_ref[...], preferred_element_type=F32)
    x = x.reshape(n, rows_l, -1)
    out_ref[...] = (x / v_ref[...]).astype(BF16)


def inv_col(own, recv, v_row, f_own, f_oth, e0):
    n, rows_l, half = own.shape
    cols = 2 * half
    eb0 = e0 // BLK
    blk = pl.BlockSpec((BLK, rows_l, half), lambda i: (i, 0, 0))
    return pl.pallas_call(
        _inv_col_kernel,
        grid=(n // BLK,),
        in_specs=[
            blk,
            blk,
            pl.BlockSpec((BLK, rows_l, cols), lambda i: (i + eb0, 0, 0)),
            pl.BlockSpec((half, cols), lambda i: (0, 0)),
            pl.BlockSpec((half, cols), lambda i: (0, 0)),
        ],
        out_specs=pl.BlockSpec((BLK, rows_l, cols), lambda i: (i, 0, 0)),
        out_shape=jax.ShapeDtypeStruct((n, rows_l, cols), BF16),
    )(own, recv, v_row, f_own, f_oth)


def _fwd_col_kernel(me_ref, x_ref, v_ref, w_ref, ft_ref, own_ref, send_ref):
    n, rows_l, cols = x_ref.shape
    g = (x_ref[...].astype(F32) * v_ref[...]).astype(BF16)
    h = jnp.dot(g.reshape(n * rows_l, cols), ft_ref[...], preferred_element_type=F32)
    h = (h.reshape(n, rows_l, cols) * w_ref[...]).astype(BF16)
    half = cols // 2
    _split_store(me_ref, h[:, :, :half], h[:, :, half:], own_ref, send_ref)


def fwd_col(me_arr, x, v_row, w_row, ft, table_block):
    groups, n, rows_l, cols = x.shape
    half = cols // 2
    xs = pl.BlockSpec((None, BLK, rows_l, cols), lambda j, t: (j, t, 0, 0))
    ts = pl.BlockSpec((BLK, rows_l, cols), lambda j, t: (table_block(j, t), 0, 0))
    os = pl.BlockSpec((None, BLK, rows_l, half), lambda j, t: (j, t, 0, 0))
    return pl.pallas_call(
        _fwd_col_kernel,
        grid=(groups, n // BLK),
        in_specs=[SMEM_SPEC, xs, ts, ts, pl.BlockSpec((cols, cols), lambda j, t: (0, 0))],
        out_specs=[os, os],
        out_shape=[jax.ShapeDtypeStruct((groups, n, rows_l, half), BF16)] * 2,
    )(me_arr, x, v_row, w_row, ft)


def _product_kernel(eb0, fo_ref, fr_ref, cip_ref, key_ref, *rest):
    halves = rest[: 2 * DIGITS]
    out_ref, acc_ref = rest[2 * DIGITS :]
    eb = pl.program_id(0) + eb0
    fo = fo_ref[...]
    fr = fr_ref[...]
    acc_ref[...] = jnp.zeros_like(acc_ref)
    n = acc_ref.shape[0]
    for j in range(DIGITS):
        own_ref, recv_ref = halves[2 * j], halves[2 * j + 1]

        @pl.when(eb == j)
        def _():
            acc_ref[...] += cip_ref[...].astype(F32) * key_ref[j].astype(F32)

        @pl.when(eb != j)
        def _():
            for l in range(n):
                y = jnp.dot(fo, own_ref[l], preferred_element_type=F32)
                y = (y + jnp.dot(fr, recv_ref[l], preferred_element_type=F32)).astype(BF16)
                acc_ref[l] += y.astype(F32) * key_ref[j, l].astype(F32)

    out_ref[...] = acc_ref[...].astype(BF16)


def product(cip, key, own2, recv2, f_own, f_oth, eb0, nblocks):
    _, rows, cols_l = cip.shape
    rows_l = rows // 2

    def lifted_block(j):
        def index(i):
            eb = i + eb0
            tb = jnp.where(eb < j, eb, eb - 1)
            return (j, jnp.clip(tb, 0, DIGITS - 1), 0, 0)

        return pl.BlockSpec((None, BLK, rows_l, cols_l), index)

    half_specs = []
    half_args = []
    for j in range(DIGITS):
        half_specs += [lifted_block(j), lifted_block(j)]
        half_args += [own2, recv2]
    return pl.pallas_call(
        lambda *refs: _product_kernel(eb0, *refs),
        grid=(nblocks,),
        in_specs=[
            pl.BlockSpec((rows, rows_l), lambda i: (0, 0)),
            pl.BlockSpec((rows, rows_l), lambda i: (0, 0)),
            pl.BlockSpec(
                (BLK, rows, cols_l), lambda i: (jnp.minimum(i + eb0, DIGITS - 1), 0, 0)
            ),
            pl.BlockSpec((DIGITS, BLK, rows, cols_l), lambda i: (0, i + eb0, 0, 0)),
        ]
        + half_specs,
        out_specs=pl.BlockSpec((BLK, rows, cols_l), lambda i: (i, 0, 0)),
        out_shape=jax.ShapeDtypeStruct((nblocks * BLK, rows, cols_l), BF16),
        scratch_shapes=[pltpu.VMEM((BLK, rows, cols_l), F32)],
    )(f_own, f_oth, cip, key, *half_args)


def _final_kernel(fo_ref, fr_ref, own_ref, recv_ref, prod_ref, s_ref, out_ref):
    fo = fo_ref[...]
    fr = fr_ref[...]
    for l in range(own_ref.shape[0]):
        y = jnp.dot(fo, own_ref[l], preferred_element_type=F32)
        y = (y + jnp.dot(fr, recv_ref[l], preferred_element_type=F32)).astype(BF16)
        diff = prod_ref[l].astype(F32) - y.astype(F32)
        out_ref[l] = (diff * s_ref[l]).astype(BF16)


def final(own4, recv4, prod, scale, f_own, f_oth):
    n, rows, cols_l = prod.shape
    rows_l = rows // 2
    hs = pl.BlockSpec((BLK, rows_l, cols_l), lambda i: (i, 0, 0))
    return pl.pallas_call(
        _final_kernel,
        grid=(n // BLK,),
        in_specs=[
            pl.BlockSpec((rows, rows_l), lambda i: (0, 0)),
            pl.BlockSpec((rows, rows_l), lambda i: (0, 0)),
            hs,
            hs,
            pl.BlockSpec((BLK, rows, cols_l), lambda i: (i, 0, 0)),
            pl.BlockSpec((BLK, 1, cols_l), lambda i: (i, 0, 0)),
        ],
        out_specs=pl.BlockSpec((BLK, rows, cols_l), lambda i: (i, 0, 0)),
        out_shape=jax.ShapeDtypeStruct((n, rows, cols_l), BF16),
    )(f_own, f_oth, own4, recv4, prod, scale)


def snake_ring(n):
    if n % 2:
        return list(range(n))
    outer = n // 2
    return [2 * a for a in range(outer)] + [2 * a + 1 for a in reversed(range(outer))]


def ring_setup(shard):
    n = lax.axis_size("limb")
    me_l = lax.axis_index("limb")
    order = snake_ring(n)
    pos = [0] * n
    for i, l in enumerate(order):
        pos[l] = i
    width = shard.shape[1]
    full = jnp.zeros((shard.shape[0], n * width) + shard.shape[2:], shard.dtype)
    full = lax.dynamic_update_slice_in_dim(full, shard, me_l * width, axis=1)
    return dict(
        n=n,
        order=jnp.array(order, I32),
        p=jnp.array(pos, I32)[me_l],
        cw=[(order[i], order[(i + 1) % n]) for i in range(n)],
        ccw=[(order[i], order[(i - 1) % n]) for i in range(n)],
        width=width,
        full=full,
        a=shard,
        b=shard,
        s=0,
    )


def ring_steps(st):
    return st["n"] // 2


def ring_step(st):
    n, width, order, p = st["n"], st["width"], st["order"], st["p"]
    st["s"] += 1
    s = st["s"]
    if 2 * s < n:
        st["a"] = lax.ppermute(st["a"], "limb", st["cw"])
        st["b"] = lax.ppermute(st["b"], "limb", st["ccw"])
        st["full"] = lax.dynamic_update_slice_in_dim(
            st["full"], st["a"], order[(p - s) % n] * width, axis=1
        )
        st["full"] = lax.dynamic_update_slice_in_dim(
            st["full"], st["b"], order[(p + s) % n] * width, axis=1
        )
    else:
        h = st["a"].shape[2] // 2
        a = lax.ppermute(st["a"][:, :, :h], "limb", st["cw"])
        b = lax.ppermute(st["b"][:, :, h:], "limb", st["ccw"])
        src = order[(p + s) % n] * width
        st["full"] = lax.dynamic_update_slice_in_dim(
            st["full"], jnp.concatenate([a, b], axis=2), src, axis=1
        )


def ring_hold(st, x):
    if st["s"] >= ring_steps(st):
        return x
    st["a"], st["b"], x = lax.optimization_barrier((st["a"], st["b"], x))
    ring_step(st)
    return x


def ring_finish(st):
    while st["s"] < ring_steps(st):
        ring_step(st)
    return st["full"]

def swap(x):
    return lax.ppermute(x, "coef", perm=[(0, 1), (1, 0)])


def body(cipher, switch_key, raise_table, lower_table, special_inverse):
    nc = lax.axis_size("coef")
    me = lax.axis_index("coef")
    me_arr = jnp.reshape(me, (1,)).astype(I32)
    other = 1 - me
    _, limbs, rows, cols_l = cipher.shape
    cols = cols_l * nc
    rows_l = rows // nc

    ring = ring_setup(switch_key[0])
    if ring_steps(ring):
        ring_step(ring)

    f_rows = cosine_table(rows)
    f_cols = cosine_table(cols)
    ft_rows = f_rows.T
    ft_cols = f_cols.T
    fc_own = lax.dynamic_slice_in_dim(f_cols, me * cols_l, cols_l, axis=0)
    fc_oth = lax.dynamic_slice_in_dim(f_cols, other * cols_l, cols_l, axis=0)
    fr_own = lax.dynamic_slice_in_dim(f_rows, me * rows_l, rows_l, axis=1)
    fr_oth = lax.dynamic_slice_in_dim(f_rows, other * rows_l, rows_l, axis=1)
    w_col, w_row, v_row = twiddle_tables(me, rows, cols, nc)

    ct = cipher[0]
    own1, send1 = inv_row(me_arr, ct, w_col, ft_rows, 0)
    own1 = ring_hold(ring, own1)
    coeffs = inv_col(own1, swap(send1), v_row, fc_own, fc_oth, 0)

    blocks = coeffs.reshape(DIGITS, DIGIT_LIMBS, rows_l, cols)
    raised = lax.dot_general(
        raise_table, blocks, (((2,), (1,)), ((0,), (0,))), preferred_element_type=F32
    ).astype(BF16)

    raised = ring_hold(ring, raised)
    own2, send2 = fwd_col(
        me_arr, raised, v_row, w_row, ft_cols, lambda j, t: jnp.where(t >= j, t + 1, t)
    )
    own2, send2 = ring_hold(ring, (own2, send2))
    recv2 = swap(send2)
    key = ring_finish(ring)

    prod_special = product(ct, key, own2, recv2, fr_own, fr_oth, DIGITS, 1)
    prod_cipher = product(ct, key, own2, recv2, fr_own, fr_oth, 0, DIGITS)

    own3, send3 = inv_row(me_arr, prod_special, w_col, ft_rows, limbs)
    special = inv_col(own3, swap(send3), v_row, fc_own, fc_oth, limbs)
    lowered = lax.dot_general(
        lower_table, special, (((1,), (0,)), ((), ())), preferred_element_type=F32
    )
    lowered = lowered.astype(BF16)[None]
    own4, send4 = fwd_col(me_arr, lowered, v_row, w_row, ft_cols, lambda j, t: t)
    scale = jnp.broadcast_to(special_inverse[:, None, None], (limbs, 1, cols_l))
    result = final(own4[0], swap(send4)[0], prod_cipher, scale, fr_own, fr_oth)
    return result[None, None]


def solution(mesh):
    in_specs = (
        P(("grp", "limb"), None, None, "coef"),
        P(None, None, "limb", None, "coef"),
        P(),
        P(),
        P(),
    )
    out_specs = P(None, ("grp", "limb"), None, None, "coef")
    return jax.shard_map(body, mesh=mesh, in_specs=in_specs, out_specs=out_specs, check_vma=False)
```

```python
import math

import jax
import ml_dtypes
import numpy as np
import jax.numpy as jnp
from jax import lax
from jax.experimental import pallas as pl
from jax.experimental.pallas import tpu as pltpu
from jax.sharding import PartitionSpec as P

LIMBS = 48
DIGITS = 3
DIGIT_LIMBS = 16
EXTENDED = 64
CYCLE = 32768
BLK = 16

F32 = jnp.float32
BF16 = jnp.bfloat16
I32 = jnp.int32


def cosine_table(size):
    freq = np.arange(size, dtype=np.float64)[:, None]
    place = np.arange(size, dtype=np.float64)[None, :]
    norm = np.where(freq == 0, math.sqrt(1.0 / size), math.sqrt(2.0 / size))
    return (norm * np.cos(math.pi * (2.0 * place + 1.0) * freq / (2.0 * size))).astype(
        ml_dtypes.bfloat16
    )


def _angle(phase):
    ang = (2.0 * math.pi / CYCLE) * phase.astype(F32)
    return jnp.cos(ang), jnp.sin(ang)


def _limb_angle(c):
    shape = (-1,) + (1,) * c.ndim
    hi = jnp.arange(EXTENDED // 8, dtype=I32).reshape(shape)
    lo = (2 * jnp.arange(8, dtype=I32) + 1).reshape(shape)
    ch, sh = _angle((16 * hi * c[None]) % CYCLE)
    cl, sl = _angle((lo * c[None]) % CYCLE)
    cos = ch[:, None] * cl[None] - sh[:, None] * sl[None]
    sin = sh[:, None] * cl[None] + ch[:, None] * sl[None]
    return cos.reshape((EXTENDED,) + c.shape), sin.reshape((EXTENDED,) + c.shape)


def _twiddle(p, q):
    cp, sp = _limb_angle(p % CYCLE)
    cq, sq = _limb_angle(q % CYCLE)
    cp, sp, cq, sq = lax.optimization_barrier((cp, sp, cq, sq))
    return 1.0 + 0.5 * (cp * cq - sp * sq)


def twiddle_tables(me, rows, cols, nc):
    rows_l, cols_l = rows // nc, cols // nc
    fine = jnp.arange(8, dtype=I32)[None, :, None]
    coarse = (8 * jnp.arange(rows // 8, dtype=I32))[:, None, None]
    bcol = (me * cols_l + jnp.arange(cols_l, dtype=I32))[None, None, :]
    w_col = _twiddle(coarse * bcol, fine * bcol).reshape(EXTENDED, rows, cols_l)
    coarse = (me * rows_l + 8 * jnp.arange(rows_l // 8, dtype=I32))[:, None, None]
    ball = jnp.arange(cols, dtype=I32)[None, None, :]
    w_row = _twiddle(coarse * ball, fine * ball).reshape(EXTENDED, rows_l, cols)
    v_row = _twiddle(coarse * cols + ball, fine * cols).reshape(EXTENDED, rows_l, cols)
    return w_col, w_row, v_row


SMEM_SPEC = pl.BlockSpec(memory_space=pltpu.SMEM)


def _split_store(me_ref, first, second, own_ref, send_ref):
    top = me_ref[0] == 0

    @pl.when(top)
    def _():
        own_ref[...] = first
        send_ref[...] = second

    @pl.when(jnp.logical_not(top))
    def _():
        own_ref[...] = second
        send_ref[...] = first


def _inv_row_kernel(me_ref, y_ref, w_ref, ft_ref, own_ref, send_ref, h_ref):
    ft = ft_ref[...]
    n, rows, _ = y_ref.shape
    for l in range(n):
        h = jnp.dot(ft, y_ref[l], preferred_element_type=F32)
        h_ref[l] = (h / w_ref[l]).astype(BF16)
    half = rows // 2
    _split_store(me_ref, h_ref[:, :half, :], h_ref[:, half:, :], own_ref, send_ref)


def inv_row(me_arr, y, w_col, ft, e0):
    n, rows, cols_l = y.shape
    eb0 = e0 // BLK
    blk = pl.BlockSpec((BLK, rows, cols_l), lambda i: (i, 0, 0))
    out = pl.BlockSpec((BLK, rows // 2, cols_l), lambda i: (i, 0, 0))
    return pl.pallas_call(
        _inv_row_kernel,
        grid=(n // BLK,),
        in_specs=[
            SMEM_SPEC,
            blk,
            pl.BlockSpec((BLK, rows, cols_l), lambda i: (i + eb0, 0, 0)),
            pl.BlockSpec((rows, rows), lambda i: (0, 0)),
        ],
        out_specs=[out, out],
        out_shape=[jax.ShapeDtypeStruct((n, rows // 2, cols_l), BF16)] * 2,
        scratch_shapes=[pltpu.VMEM((BLK, rows, cols_l), BF16)],
    )(me_arr, y, w_col, ft)


def _inv_col_kernel(own_ref, recv_ref, v_ref, fo_ref, fr_ref, out_ref):
    n, rows_l, half = own_ref.shape
    a = own_ref[...].reshape(n * rows_l, half)
    b = recv_ref[...].reshape(n * rows_l, half)
    x = jnp.dot(a, fo_ref[...], preferred_element_type=F32)
    x = x + jnp.dot(b, fr_ref[...], preferred_element_type=F32)
    x = x.reshape(n, rows_l, -1)
    out_ref[...] = (x / v_ref[...]).astype(BF16)


def inv_col(own, recv, v_row, f_own, f_oth, e0):
    n, rows_l, half = own.shape
    cols = 2 * half
    eb0 = e0 // BLK
    blk = pl.BlockSpec((BLK, rows_l, half), lambda i: (i, 0, 0))
    return pl.pallas_call(
        _inv_col_kernel,
        grid=(n // BLK,),
        in_specs=[
            blk,
            blk,
            pl.BlockSpec((BLK, rows_l, cols), lambda i: (i + eb0, 0, 0)),
            pl.BlockSpec((half, cols), lambda i: (0, 0)),
            pl.BlockSpec((half, cols), lambda i: (0, 0)),
        ],
        out_specs=pl.BlockSpec((BLK, rows_l, cols), lambda i: (i, 0, 0)),
        out_shape=jax.ShapeDtypeStruct((n, rows_l, cols), BF16),
    )(own, recv, v_row, f_own, f_oth)


def _fwd_col_kernel(me_ref, x_ref, v_ref, w_ref, ft_ref, own_ref, send_ref):
    n, rows_l, cols = x_ref.shape
    g = (x_ref[...].astype(F32) * v_ref[...]).astype(BF16)
    h = jnp.dot(g.reshape(n * rows_l, cols), ft_ref[...], preferred_element_type=F32)
    h = (h.reshape(n, rows_l, cols) * w_ref[...]).astype(BF16)
    half = cols // 2
    _split_store(me_ref, h[:, :, :half], h[:, :, half:], own_ref, send_ref)


def fwd_col(me_arr, x, v_row, w_row, ft, table_block):
    groups, n, rows_l, cols = x.shape
    half = cols // 2
    xs = pl.BlockSpec((None, BLK, rows_l, cols), lambda j, t: (j, t, 0, 0))
    ts = pl.BlockSpec((BLK, rows_l, cols), lambda j, t: (table_block(j, t), 0, 0))
    os = pl.BlockSpec((None, BLK, rows_l, half), lambda j, t: (j, t, 0, 0))
    return pl.pallas_call(
        _fwd_col_kernel,
        grid=(groups, n // BLK),
        in_specs=[SMEM_SPEC, xs, ts, ts, pl.BlockSpec((cols, cols), lambda j, t: (0, 0))],
        out_specs=[os, os],
        out_shape=[jax.ShapeDtypeStruct((groups, n, rows_l, half), BF16)] * 2,
    )(me_arr, x, v_row, w_row, ft)


def _product_kernel(eb0, spb, slot_ref, g_ref, fo_ref, fr_ref, cip_ref, *rest):
    ring_refs = rest[:spb]
    side_refs = rest[spb : 2 * spb]
    halves = rest[2 * spb : 2 * spb + 2 * DIGITS]
    out_ref, acc_ref = rest[2 * spb + 2 * DIGITS :]
    width = ring_refs[0].shape[1]
    eb = pl.program_id(0) + eb0
    fo = fo_ref[...]
    fr = fr_ref[...]
    acc_ref[...] = jnp.zeros_like(acc_ref)
    n = acc_ref.shape[0]

    def key(gv, j, l):
        kd = (j - gv) % DIGITS
        if kd < 2:
            return ring_refs[l // width][kd, l % width]
        return side_refs[l // width][0, l % width]

    for gv in range(2):
        for j in range(DIGITS):
            own_ref, recv_ref = halves[2 * j], halves[2 * j + 1]

            @pl.when(jnp.logical_and(g_ref[0] == gv, eb == j))
            def _():
                for l in range(n):
                    acc_ref[l] += cip_ref[l].astype(F32) * key(gv, j, l).astype(F32)

            @pl.when(jnp.logical_and(g_ref[0] == gv, eb != j))
            def _():
                for l in range(n):
                    y = jnp.dot(fo, own_ref[l], preferred_element_type=F32)
                    y = (y + jnp.dot(fr, recv_ref[l], preferred_element_type=F32)).astype(BF16)
                    acc_ref[l] += y.astype(F32) * key(gv, j, l).astype(F32)

    out_ref[...] = acc_ref[...].astype(BF16)


def product(cip, ring_key, side_key, slot, g_arr, own2, recv2, f_own, f_oth, eb0, nblocks):
    _, rows, cols_l = cip.shape
    rows_l = rows // 2
    width = ring_key.shape[1] // slot.shape[0]
    spb = BLK // width

    def lifted_block(j):
        def index(i, slot_ref):
            eb = i + eb0
            tb = jnp.where(eb < j, eb, eb - 1)
            return (j, jnp.clip(tb, 0, DIGITS - 1), 0, 0)

        return pl.BlockSpec((None, BLK, rows_l, cols_l), index)

    def key_block(r, depth):
        return pl.BlockSpec(
            (depth, width, rows, cols_l),
            lambda i, slot_ref: (0, slot_ref[(i + eb0) * spb + r], 0, 0),
        )

    half_specs = []
    half_args = []
    for j in range(DIGITS):
        half_specs += [lifted_block(j), lifted_block(j)]
        half_args += [own2, recv2]
    grid_spec = pltpu.PrefetchScalarGridSpec(
        num_scalar_prefetch=1,
        grid=(nblocks,),
        in_specs=[
            SMEM_SPEC,
            pl.BlockSpec((rows, rows_l), lambda i, slot_ref: (0, 0)),
            pl.BlockSpec((rows, rows_l), lambda i, slot_ref: (0, 0)),
            pl.BlockSpec(
                (BLK, rows, cols_l),
                lambda i, slot_ref: (jnp.minimum(i + eb0, DIGITS - 1), 0, 0),
            ),
        ]
        + [key_block(r, 2) for r in range(spb)]
        + [key_block(r, 1) for r in range(spb)]
        + half_specs,
        out_specs=pl.BlockSpec((BLK, rows, cols_l), lambda i, slot_ref: (i, 0, 0)),
        scratch_shapes=[pltpu.VMEM((BLK, rows, cols_l), F32)],
    )
    return pl.pallas_call(
        lambda *refs: _product_kernel(eb0, spb, *refs),
        grid_spec=grid_spec,
        out_shape=jax.ShapeDtypeStruct((nblocks * BLK, rows, cols_l), BF16),
    )(slot, g_arr, f_own, f_oth, cip, *([ring_key] * spb), *([side_key] * spb), *half_args)


def _final_kernel(fo_ref, fr_ref, own_ref, recv_ref, prod_ref, s_ref, out_ref):
    fo = fo_ref[...]
    fr = fr_ref[...]
    for l in range(own_ref.shape[0]):
        y = jnp.dot(fo, own_ref[l], preferred_element_type=F32)
        y = (y + jnp.dot(fr, recv_ref[l], preferred_element_type=F32)).astype(BF16)
        diff = prod_ref[l].astype(F32) - y.astype(F32)
        out_ref[l] = (diff * s_ref[l]).astype(BF16)


def final(own4, recv4, prod, scale, f_own, f_oth):
    n, rows, cols_l = prod.shape
    rows_l = rows // 2
    hs = pl.BlockSpec((BLK, rows_l, cols_l), lambda i: (i, 0, 0))
    return pl.pallas_call(
        _final_kernel,
        grid=(n // BLK,),
        in_specs=[
            pl.BlockSpec((rows, rows_l), lambda i: (0, 0)),
            pl.BlockSpec((rows, rows_l), lambda i: (0, 0)),
            hs,
            hs,
            pl.BlockSpec((BLK, rows, cols_l), lambda i: (i, 0, 0)),
            pl.BlockSpec((BLK, 1, cols_l), lambda i: (i, 0, 0)),
        ],
        out_specs=pl.BlockSpec((BLK, rows, cols_l), lambda i: (i, 0, 0)),
        out_shape=jax.ShapeDtypeStruct((n, rows, cols_l), BF16),
    )(f_own, f_oth, own4, recv4, prod, scale)


def snake_ring(n):
    if n % 2:
        return list(range(n))
    outer = n // 2
    return [2 * a for a in range(outer)] + [2 * a + 1 for a in reversed(range(outer))]


def ring_setup(shard):
    n = lax.axis_size("limb")
    me_l = lax.axis_index("limb")
    g = lax.axis_index("grp")
    order = snake_ring(n)
    pos = [0] * n
    for i, l in enumerate(order):
        pos[l] = i
    pos_arr = jnp.array(pos, I32)
    p = pos_arr[me_l]
    d = (pos_arr - p) % n
    half = (n - 1) // 2
    slot = jnp.where(d == 0, 0, jnp.where(d <= half, 2 * d, 2 * (n - d) - 1))
    if n % 2 == 0:
        slot = jnp.where(d == n // 2, n - 1, slot)
    piece = lax.dynamic_slice_in_dim(shard, g, 2, axis=0)
    return dict(
        n=n,
        g=g,
        slot=slot.astype(I32),
        cw=[(order[i], order[(i + 1) % n]) for i in range(n)],
        ccw=[(order[i], order[(i - 1) % n]) for i in range(n)],
        ring=[piece],
        side=[lax.dynamic_slice_in_dim(shard, 2 - 2 * g, 1, axis=0)],
        a=piece,
        b=piece,
        s=0,
        fresh=[],
        pending=[],
    )


def ring_steps(st):
    return st["n"] // 2


def _to_partner(x, g):
    return lax.ppermute(lax.dynamic_slice_in_dim(x, g, 1, axis=0), "grp", [(0, 1), (1, 0)])


def ring_step(st):
    n = st["n"]
    st["s"] += 1
    if 2 * st["s"] < n:
        st["a"] = lax.ppermute(st["a"], "limb", st["cw"])
        st["b"] = lax.ppermute(st["b"], "limb", st["ccw"])
        st["fresh"] = [st["a"], st["b"]]
    else:
        h = st["a"].shape[2] // 2
        a = lax.ppermute(st["a"][:, :, :h], "limb", st["cw"])
        b = lax.ppermute(st["b"][:, :, h:], "limb", st["ccw"])
        st["fresh"] = [jnp.concatenate([a, b], axis=2)]


def _settle(st, x):
    fresh, pending = st["fresh"], st["pending"]
    fresh, pending, x = lax.optimization_barrier((fresh, pending, x))
    st["side"] += pending
    st["ring"] += fresh
    if len(fresh) == 2:
        st["a"], st["b"] = fresh
    st["pending"] = [_to_partner(jnp.concatenate(fresh, axis=1), st["g"])]
    st["fresh"] = []
    return x


def ring_hold(st, x):
    if st["s"] >= ring_steps(st):
        return x
    x = _settle(st, x)
    ring_step(st)
    return x


def ring_finish(st, x):
    while st["s"] < ring_steps(st):
        x = _settle(st, x)
        ring_step(st)
    if st["fresh"]:
        x = _settle(st, x)
    st["side"] += st["pending"]
    return jnp.concatenate(st["ring"], axis=1), jnp.concatenate(st["side"], axis=1), x

def swap(x):
    return lax.ppermute(x, "coef", perm=[(0, 1), (1, 0)])


def body(cipher, switch_key, raise_table, lower_table, special_inverse):
    nc = lax.axis_size("coef")
    me = lax.axis_index("coef")
    me_arr = jnp.reshape(me, (1,)).astype(I32)
    other = 1 - me
    _, limbs, rows, cols_l = cipher.shape
    cols = cols_l * nc
    rows_l = rows // nc

    ring = ring_setup(switch_key[0])
    if ring_steps(ring):
        ring_step(ring)

    f_rows = cosine_table(rows)
    f_cols = cosine_table(cols)
    ft_rows = f_rows.T
    ft_cols = f_cols.T
    fc_own = lax.dynamic_slice_in_dim(f_cols, me * cols_l, cols_l, axis=0)
    fc_oth = lax.dynamic_slice_in_dim(f_cols, other * cols_l, cols_l, axis=0)
    fr_own = lax.dynamic_slice_in_dim(f_rows, me * rows_l, rows_l, axis=1)
    fr_oth = lax.dynamic_slice_in_dim(f_rows, other * rows_l, rows_l, axis=1)
    w_col, w_row, v_row = twiddle_tables(me, rows, cols, nc)

    ct = cipher[0]
    own1, send1 = inv_row(me_arr, ct, w_col, ft_rows, 0)
    own1 = ring_hold(ring, own1)
    coeffs = inv_col(own1, swap(send1), v_row, fc_own, fc_oth, 0)

    coeffs = ring_hold(ring, coeffs)
    blocks = coeffs.reshape(DIGITS, DIGIT_LIMBS, rows_l, cols)
    raised = lax.dot_general(
        raise_table, blocks, (((2,), (1,)), ((0,), (0,))), preferred_element_type=F32
    ).astype(BF16)

    raised = ring_hold(ring, raised)
    own2, send2 = fwd_col(
        me_arr, raised, v_row, w_row, ft_cols, lambda j, t: jnp.where(t >= j, t + 1, t)
    )
    ring_key, side_key, (own2, send2) = ring_finish(ring, (own2, send2))
    recv2 = swap(send2)
    slot = ring["slot"]
    g_arr = jnp.reshape(ring["g"], (1,)).astype(I32)

    prod_special = product(
        ct, ring_key, side_key, slot, g_arr, own2, recv2, fr_own, fr_oth, DIGITS, 1
    )
    prod_cipher = product(
        ct, ring_key, side_key, slot, g_arr, own2, recv2, fr_own, fr_oth, 0, DIGITS
    )

    own3, send3 = inv_row(me_arr, prod_special, w_col, ft_rows, limbs)
    special = inv_col(own3, swap(send3), v_row, fc_own, fc_oth, limbs)
    lowered = lax.dot_general(
        lower_table, special, (((1,), (0,)), ((), ())), preferred_element_type=F32
    )
    lowered = lowered.astype(BF16)[None]
    own4, send4 = fwd_col(me_arr, lowered, v_row, w_row, ft_cols, lambda j, t: t)
    scale = jnp.broadcast_to(special_inverse[:, None, None], (limbs, 1, cols_l))
    result = final(own4[0], swap(send4)[0], prod_cipher, scale, fr_own, fr_oth)
    return result[None, None]


def solution(mesh):
    in_specs = (
        P(("grp", "limb"), None, None, "coef"),
        P(None, None, "limb", None, "coef"),
        P(),
        P(),
        P(),
    )
    out_specs = P(None, ("grp", "limb"), None, None, "coef")
    return jax.shard_map(body, mesh=mesh, in_specs=in_specs, out_specs=out_specs, check_vma=False)
```

```python
import math

import jax
import ml_dtypes
import numpy as np
import jax.numpy as jnp
from jax import lax
from jax.experimental import pallas as pl
from jax.experimental.pallas import tpu as pltpu
from jax.sharding import PartitionSpec as P

LIMBS = 48
DIGITS = 3
DIGIT_LIMBS = 16
EXTENDED = 64
CYCLE = 32768
BLK = 16

F32 = jnp.float32
BF16 = jnp.bfloat16
I32 = jnp.int32


def cosine_table(size):
    freq = np.arange(size, dtype=np.float64)[:, None]
    place = np.arange(size, dtype=np.float64)[None, :]
    norm = np.where(freq == 0, math.sqrt(1.0 / size), math.sqrt(2.0 / size))
    return (norm * np.cos(math.pi * (2.0 * place + 1.0) * freq / (2.0 * size))).astype(
        ml_dtypes.bfloat16
    )


def _angle(phase):
    ang = (2.0 * math.pi / CYCLE) * phase.astype(F32)
    return jnp.cos(ang), jnp.sin(ang)


def _limb_angle(c):
    shape = (-1,) + (1,) * c.ndim
    hi = jnp.arange(EXTENDED // 8, dtype=I32).reshape(shape)
    lo = (2 * jnp.arange(8, dtype=I32) + 1).reshape(shape)
    ch, sh = _angle((16 * hi * c[None]) % CYCLE)
    cl, sl = _angle((lo * c[None]) % CYCLE)
    cos = ch[:, None] * cl[None] - sh[:, None] * sl[None]
    sin = sh[:, None] * cl[None] + ch[:, None] * sl[None]
    return cos.reshape((EXTENDED,) + c.shape), sin.reshape((EXTENDED,) + c.shape)


def _twiddle(p, q):
    cp, sp = _limb_angle(p % CYCLE)
    cq, sq = _limb_angle(q % CYCLE)
    cp, sp, cq, sq = lax.optimization_barrier((cp, sp, cq, sq))
    return 1.0 + 0.5 * (cp * cq - sp * sq)


def twiddle_tables(me, rows, cols, nc):
    rows_l, cols_l = rows // nc, cols // nc
    fine = jnp.arange(8, dtype=I32)[None, :, None]
    coarse = (8 * jnp.arange(rows // 8, dtype=I32))[:, None, None]
    bcol = (me * cols_l + jnp.arange(cols_l, dtype=I32))[None, None, :]
    w_col = _twiddle(coarse * bcol, fine * bcol).reshape(EXTENDED, rows, cols_l)
    coarse = (me * rows_l + 8 * jnp.arange(rows_l // 8, dtype=I32))[:, None, None]
    ball = jnp.arange(cols, dtype=I32)[None, None, :]
    w_row = _twiddle(coarse * ball, fine * ball).reshape(EXTENDED, rows_l, cols)
    v_row = _twiddle(coarse * cols + ball, fine * cols).reshape(EXTENDED, rows_l, cols)
    return w_col, w_row, v_row


SMEM_SPEC = pl.BlockSpec(memory_space=pltpu.SMEM)


def _split_store(me_ref, first, second, own_ref, send_ref):
    top = me_ref[0] == 0

    @pl.when(top)
    def _():
        own_ref[...] = first
        send_ref[...] = second

    @pl.when(jnp.logical_not(top))
    def _():
        own_ref[...] = second
        send_ref[...] = first


def _inv_row_kernel(me_ref, y_ref, w_ref, ft_ref, own_ref, send_ref, h_ref):
    ft = ft_ref[...]
    n, rows, _ = y_ref.shape
    for l in range(n):
        h = jnp.dot(ft, y_ref[l], preferred_element_type=F32)
        h_ref[l] = (h / w_ref[l]).astype(BF16)
    half = rows // 2
    _split_store(me_ref, h_ref[:, :half, :], h_ref[:, half:, :], own_ref, send_ref)


def inv_row(me_arr, y, w_col, ft, e0):
    n, rows, cols_l = y.shape
    eb0 = e0 // BLK
    blk = pl.BlockSpec((BLK, rows, cols_l), lambda i: (i, 0, 0))
    out = pl.BlockSpec((BLK, rows // 2, cols_l), lambda i: (i, 0, 0))
    return pl.pallas_call(
        _inv_row_kernel,
        grid=(n // BLK,),
        in_specs=[
            SMEM_SPEC,
            blk,
            pl.BlockSpec((BLK, rows, cols_l), lambda i: (i + eb0, 0, 0)),
            pl.BlockSpec((rows, rows), lambda i: (0, 0)),
        ],
        out_specs=[out, out],
        out_shape=[jax.ShapeDtypeStruct((n, rows // 2, cols_l), BF16)] * 2,
        scratch_shapes=[pltpu.VMEM((BLK, rows, cols_l), BF16)],
    )(me_arr, y, w_col, ft)


def _inv_col_kernel(own_ref, recv_ref, v_ref, fo_ref, fr_ref, out_ref):
    n, rows_l, half = own_ref.shape
    a = own_ref[...].reshape(n * rows_l, half)
    b = recv_ref[...].reshape(n * rows_l, half)
    x = jnp.dot(a, fo_ref[...], preferred_element_type=F32)
    x = x + jnp.dot(b, fr_ref[...], preferred_element_type=F32)
    x = x.reshape(n, rows_l, -1)
    out_ref[...] = (x / v_ref[...]).astype(BF16)


def inv_col(own, recv, v_row, f_own, f_oth, e0):
    n, rows_l, half = own.shape
    cols = 2 * half
    eb0 = e0 // BLK
    blk = pl.BlockSpec((BLK, rows_l, half), lambda i: (i, 0, 0))
    return pl.pallas_call(
        _inv_col_kernel,
        grid=(n // BLK,),
        in_specs=[
            blk,
            blk,
            pl.BlockSpec((BLK, rows_l, cols), lambda i: (i + eb0, 0, 0)),
            pl.BlockSpec((half, cols), lambda i: (0, 0)),
            pl.BlockSpec((half, cols), lambda i: (0, 0)),
        ],
        out_specs=pl.BlockSpec((BLK, rows_l, cols), lambda i: (i, 0, 0)),
        out_shape=jax.ShapeDtypeStruct((n, rows_l, cols), BF16),
    )(own, recv, v_row, f_own, f_oth)


def _fwd_col_kernel(me_ref, x_ref, v_ref, w_ref, ft_ref, own_ref, send_ref):
    n, rows_l, cols = x_ref.shape
    g = (x_ref[...].astype(F32) * v_ref[...]).astype(BF16)
    h = jnp.dot(g.reshape(n * rows_l, cols), ft_ref[...], preferred_element_type=F32)
    h = (h.reshape(n, rows_l, cols) * w_ref[...]).astype(BF16)
    half = cols // 2
    _split_store(me_ref, h[:, :, :half], h[:, :, half:], own_ref, send_ref)


def fwd_col(me_arr, x, v_row, w_row, ft, table_block):
    groups, n, rows_l, cols = x.shape
    half = cols // 2
    xs = pl.BlockSpec((None, BLK, rows_l, cols), lambda j, t: (j, t, 0, 0))
    ts = pl.BlockSpec((BLK, rows_l, cols), lambda j, t: (table_block(j, t), 0, 0))
    os = pl.BlockSpec((None, BLK, rows_l, half), lambda j, t: (j, t, 0, 0))
    return pl.pallas_call(
        _fwd_col_kernel,
        grid=(groups, n // BLK),
        in_specs=[SMEM_SPEC, xs, ts, ts, pl.BlockSpec((cols, cols), lambda j, t: (0, 0))],
        out_specs=[os, os],
        out_shape=[jax.ShapeDtypeStruct((groups, n, rows_l, half), BF16)] * 2,
    )(me_arr, x, v_row, w_row, ft)


def _product_kernel(eb0, spb, ring_map, side_map, slot_ref, g_ref, fo_ref, fr_ref, cip_ref, *rest):
    nr, ns = len(ring_map), len(set(i for i, _ in side_map))
    ring_refs = rest[:nr]
    side_refs = rest[nr : nr + ns]
    halves = rest[nr + ns : nr + ns + 2 * DIGITS]
    out_ref, acc_ref, kring, kside = rest[nr + ns + 2 * DIGITS :]
    width = kring.shape[2]
    eb = pl.program_id(0) + eb0
    for r in range(spb):
        where = slot_ref[eb * spb + r]
        for k in range(nr):
            ai, off = side_map[k]

            @pl.when(where == k)
            def _():
                pltpu.sync_copy(ring_refs[k], kring.at[r])
                pltpu.sync_copy(side_refs[ai].at[:, pl.ds(off * width, width)], kside.at[r])

    fo = fo_ref[...]
    fr = fr_ref[...]
    acc_ref[...] = jnp.zeros_like(acc_ref)
    n = acc_ref.shape[0]

    def key(gv, j, l):
        kd = (j - gv) % DIGITS
        if kd < 2:
            return kring[l // width, kd, l % width]
        return kside[l // width, 0, l % width]

    for gv in range(2):
        for j in range(DIGITS):
            own_ref, recv_ref = halves[2 * j], halves[2 * j + 1]

            @pl.when(jnp.logical_and(g_ref[0] == gv, eb == j))
            def _():
                for l in range(n):
                    acc_ref[l] += cip_ref[l].astype(F32) * key(gv, j, l).astype(F32)

            @pl.when(jnp.logical_and(g_ref[0] == gv, eb != j))
            def _():
                for l in range(n):
                    y = jnp.dot(fo, own_ref[l], preferred_element_type=F32)
                    y = (y + jnp.dot(fr, recv_ref[l], preferred_element_type=F32)).astype(BF16)
                    acc_ref[l] += y.astype(F32) * key(gv, j, l).astype(F32)

    out_ref[...] = acc_ref[...].astype(BF16)


def product(cip, ring_pieces, side_pieces, slot, g_arr, own2, recv2, f_own, f_oth, eb0, nblocks):
    _, rows, cols_l = cip.shape
    rows_l = rows // 2
    width = ring_pieces[0].shape[1]
    spb = BLK // width
    side_map = []
    for i, piece in enumerate(side_pieces):
        side_map += [(i, off) for off in range(piece.shape[1] // width)]
    ring_map = list(range(len(ring_pieces)))

    def lifted_block(j):
        def index(i, slot_ref):
            eb = i + eb0
            tb = jnp.where(eb < j, eb, eb - 1)
            return (j, jnp.clip(tb, 0, DIGITS - 1), 0, 0)

        return pl.BlockSpec((None, BLK, rows_l, cols_l), index)

    any_spec = pl.BlockSpec(memory_space=pl.ANY)
    half_specs = []
    half_args = []
    for j in range(DIGITS):
        half_specs += [lifted_block(j), lifted_block(j)]
        half_args += [own2, recv2]
    grid_spec = pltpu.PrefetchScalarGridSpec(
        num_scalar_prefetch=1,
        grid=(nblocks,),
        in_specs=[
            SMEM_SPEC,
            pl.BlockSpec((rows, rows_l), lambda i, slot_ref: (0, 0)),
            pl.BlockSpec((rows, rows_l), lambda i, slot_ref: (0, 0)),
            pl.BlockSpec(
                (BLK, rows, cols_l),
                lambda i, slot_ref: (jnp.minimum(i + eb0, DIGITS - 1), 0, 0),
            ),
        ]
        + [any_spec] * (len(ring_pieces) + len(side_pieces))
        + half_specs,
        out_specs=pl.BlockSpec((BLK, rows, cols_l), lambda i, slot_ref: (i, 0, 0)),
        scratch_shapes=[
            pltpu.VMEM((BLK, rows, cols_l), F32),
            pltpu.VMEM((spb, 2, width, rows, cols_l), BF16),
            pltpu.VMEM((spb, 1, width, rows, cols_l), BF16),
        ],
    )
    return pl.pallas_call(
        lambda *refs: _product_kernel(eb0, spb, ring_map, side_map, *refs),
        grid_spec=grid_spec,
        out_shape=jax.ShapeDtypeStruct((nblocks * BLK, rows, cols_l), BF16),
    )(slot, g_arr, f_own, f_oth, cip, *ring_pieces, *side_pieces, *half_args)


def _final_kernel(fo_ref, fr_ref, own_ref, recv_ref, prod_ref, s_ref, out_ref):
    fo = fo_ref[...]
    fr = fr_ref[...]
    for l in range(own_ref.shape[0]):
        y = jnp.dot(fo, own_ref[l], preferred_element_type=F32)
        y = (y + jnp.dot(fr, recv_ref[l], preferred_element_type=F32)).astype(BF16)
        diff = prod_ref[l].astype(F32) - y.astype(F32)
        out_ref[l] = (diff * s_ref[l]).astype(BF16)


def final(own4, recv4, prod, scale, f_own, f_oth):
    n, rows, cols_l = prod.shape
    rows_l = rows // 2
    hs = pl.BlockSpec((BLK, rows_l, cols_l), lambda i: (i, 0, 0))
    return pl.pallas_call(
        _final_kernel,
        grid=(n // BLK,),
        in_specs=[
            pl.BlockSpec((rows, rows_l), lambda i: (0, 0)),
            pl.BlockSpec((rows, rows_l), lambda i: (0, 0)),
            hs,
            hs,
            pl.BlockSpec((BLK, rows, cols_l), lambda i: (i, 0, 0)),
            pl.BlockSpec((BLK, 1, cols_l), lambda i: (i, 0, 0)),
        ],
        out_specs=pl.BlockSpec((BLK, rows, cols_l), lambda i: (i, 0, 0)),
        out_shape=jax.ShapeDtypeStruct((n, rows, cols_l), BF16),
    )(f_own, f_oth, own4, recv4, prod, scale)


def snake_ring(n):
    if n % 2:
        return list(range(n))
    outer = n // 2
    return [2 * a for a in range(outer)] + [2 * a + 1 for a in reversed(range(outer))]


def ring_setup(shard):
    n = lax.axis_size("limb")
    me_l = lax.axis_index("limb")
    g = lax.axis_index("grp")
    order = snake_ring(n)
    pos = [0] * n
    for i, l in enumerate(order):
        pos[l] = i
    pos_arr = jnp.array(pos, I32)
    p = pos_arr[me_l]
    d = (pos_arr - p) % n
    half = (n - 1) // 2
    slot = jnp.where(d == 0, 0, jnp.where(d <= half, 2 * d, 2 * (n - d) - 1))
    if n % 2 == 0:
        slot = jnp.where(d == n // 2, n - 1, slot)
    piece = lax.dynamic_slice_in_dim(shard, g, 2, axis=0)
    return dict(
        n=n,
        g=g,
        slot=slot.astype(I32),
        cw=[(order[i], order[(i + 1) % n]) for i in range(n)],
        ccw=[(order[i], order[(i - 1) % n]) for i in range(n)],
        ring=[piece],
        side=[lax.dynamic_slice_in_dim(shard, 2 - 2 * g, 1, axis=0)],
        a=piece,
        b=piece,
        s=0,
        fresh=[],
        pending=[],
    )


def ring_steps(st):
    return st["n"] // 2


def _to_partner(x, g):
    return lax.ppermute(lax.dynamic_slice_in_dim(x, g, 1, axis=0), "grp", [(0, 1), (1, 0)])


def ring_step(st):
    n = st["n"]
    st["s"] += 1
    if 2 * st["s"] < n:
        st["a"] = lax.ppermute(st["a"], "limb", st["cw"])
        st["b"] = lax.ppermute(st["b"], "limb", st["ccw"])
        st["fresh"] = [st["a"], st["b"]]
    else:
        h = st["a"].shape[2] // 2
        a = lax.ppermute(st["a"][:, :, :h], "limb", st["cw"])
        b = lax.ppermute(st["b"][:, :, h:], "limb", st["ccw"])
        st["fresh"] = [jnp.concatenate([a, b], axis=2)]


def _settle(st, x):
    fresh, pending = st["fresh"], st["pending"]
    fresh, pending, x = lax.optimization_barrier((fresh, pending, x))
    st["side"] += pending
    st["ring"] += fresh
    if len(fresh) == 2:
        st["a"], st["b"] = fresh
    st["pending"] = [_to_partner(jnp.concatenate(fresh, axis=1), st["g"])]
    st["fresh"] = []
    return x


def ring_hold(st, x):
    if st["s"] >= ring_steps(st):
        return x
    x = _settle(st, x)
    ring_step(st)
    return x


def ring_finish(st, x):
    while st["s"] < ring_steps(st):
        x = _settle(st, x)
        ring_step(st)
    if st["fresh"]:
        x = _settle(st, x)
    st["side"] += st["pending"]
    return st["ring"], st["side"], x

def swap(x):
    return lax.ppermute(x, "coef", perm=[(0, 1), (1, 0)])


def body(cipher, switch_key, raise_table, lower_table, special_inverse):
    nc = lax.axis_size("coef")
    me = lax.axis_index("coef")
    me_arr = jnp.reshape(me, (1,)).astype(I32)
    other = 1 - me
    _, limbs, rows, cols_l = cipher.shape
    cols = cols_l * nc
    rows_l = rows // nc

    ring = ring_setup(switch_key[0])
    if ring_steps(ring):
        ring_step(ring)

    f_rows = cosine_table(rows)
    f_cols = cosine_table(cols)
    ft_rows = f_rows.T
    ft_cols = f_cols.T
    fc_own = lax.dynamic_slice_in_dim(f_cols, me * cols_l, cols_l, axis=0)
    fc_oth = lax.dynamic_slice_in_dim(f_cols, other * cols_l, cols_l, axis=0)
    fr_own = lax.dynamic_slice_in_dim(f_rows, me * rows_l, rows_l, axis=1)
    fr_oth = lax.dynamic_slice_in_dim(f_rows, other * rows_l, rows_l, axis=1)
    w_col, w_row, v_row = twiddle_tables(me, rows, cols, nc)

    ct = cipher[0]
    own1, send1 = inv_row(me_arr, ct, w_col, ft_rows, 0)
    own1 = ring_hold(ring, own1)
    coeffs = inv_col(own1, swap(send1), v_row, fc_own, fc_oth, 0)

    coeffs = ring_hold(ring, coeffs)
    blocks = coeffs.reshape(DIGITS, DIGIT_LIMBS, rows_l, cols)
    raised = lax.dot_general(
        raise_table, blocks, (((2,), (1,)), ((0,), (0,))), preferred_element_type=F32
    ).astype(BF16)

    raised = ring_hold(ring, raised)
    own2, send2 = fwd_col(
        me_arr, raised, v_row, w_row, ft_cols, lambda j, t: jnp.where(t >= j, t + 1, t)
    )
    ring_key, side_key, (own2, send2) = ring_finish(ring, (own2, send2))
    recv2 = swap(send2)
    slot = ring["slot"]
    g_arr = jnp.reshape(ring["g"], (1,)).astype(I32)

    prod_special = product(
        ct, ring_key, side_key, slot, g_arr, own2, recv2, fr_own, fr_oth, DIGITS, 1
    )
    prod_cipher = product(
        ct, ring_key, side_key, slot, g_arr, own2, recv2, fr_own, fr_oth, 0, DIGITS
    )

    own3, send3 = inv_row(me_arr, prod_special, w_col, ft_rows, limbs)
    special = inv_col(own3, swap(send3), v_row, fc_own, fc_oth, limbs)
    lowered = lax.dot_general(
        lower_table, special, (((1,), (0,)), ((), ())), preferred_element_type=F32
    )
    lowered = lowered.astype(BF16)[None]
    own4, send4 = fwd_col(me_arr, lowered, v_row, w_row, ft_cols, lambda j, t: t)
    scale = jnp.broadcast_to(special_inverse[:, None, None], (limbs, 1, cols_l))
    result = final(own4[0], swap(send4)[0], prod_cipher, scale, fr_own, fr_oth)
    return result[None, None]


def solution(mesh):
    in_specs = (
        P(("grp", "limb"), None, None, "coef"),
        P(None, None, "limb", None, "coef"),
        P(),
        P(),
        P(),
    )
    out_specs = P(None, ("grp", "limb"), None, None, "coef")
    return jax.shard_map(body, mesh=mesh, in_specs=in_specs, out_specs=out_specs, check_vma=False)
```

```python
import math

import jax
import ml_dtypes
import numpy as np
import jax.numpy as jnp
from jax import lax
from jax.experimental import pallas as pl
from jax.experimental.pallas import tpu as pltpu
from jax.sharding import PartitionSpec as P

LIMBS = 48
DIGITS = 3
DIGIT_LIMBS = 16
EXTENDED = 64
CYCLE = 32768
BLK = 16

F32 = jnp.float32
BF16 = jnp.bfloat16
I32 = jnp.int32


def cosine_table(size):
    freq = np.arange(size, dtype=np.float64)[:, None]
    place = np.arange(size, dtype=np.float64)[None, :]
    norm = np.where(freq == 0, math.sqrt(1.0 / size), math.sqrt(2.0 / size))
    return (norm * np.cos(math.pi * (2.0 * place + 1.0) * freq / (2.0 * size))).astype(
        ml_dtypes.bfloat16
    )


def _angle(phase):
    ang = (2.0 * math.pi / CYCLE) * phase.astype(F32)
    return jnp.cos(ang), jnp.sin(ang)


def _limb_angle(c):
    shape = (-1,) + (1,) * c.ndim
    hi = jnp.arange(EXTENDED // 8, dtype=I32).reshape(shape)
    lo = (2 * jnp.arange(8, dtype=I32) + 1).reshape(shape)
    ch, sh = _angle((16 * hi * c[None]) % CYCLE)
    cl, sl = _angle((lo * c[None]) % CYCLE)
    cos = ch[:, None] * cl[None] - sh[:, None] * sl[None]
    sin = sh[:, None] * cl[None] + ch[:, None] * sl[None]
    return cos.reshape((EXTENDED,) + c.shape), sin.reshape((EXTENDED,) + c.shape)


def _twiddle(p, q):
    cp, sp = _limb_angle(p % CYCLE)
    cq, sq = _limb_angle(q % CYCLE)
    cp, sp, cq, sq = lax.optimization_barrier((cp, sp, cq, sq))
    return 1.0 + 0.5 * (cp * cq - sp * sq)


def twiddle_tables(me, rows, cols, nc):
    rows_l, cols_l = rows // nc, cols // nc
    fine = jnp.arange(8, dtype=I32)[None, :, None]
    coarse = (8 * jnp.arange(rows // 8, dtype=I32))[:, None, None]
    bcol = (me * cols_l + jnp.arange(cols_l, dtype=I32))[None, None, :]
    w_col = _twiddle(coarse * bcol, fine * bcol).reshape(EXTENDED, rows, cols_l)
    coarse = (me * rows_l + 8 * jnp.arange(rows_l // 8, dtype=I32))[:, None, None]
    ball = jnp.arange(cols, dtype=I32)[None, None, :]
    w_row = _twiddle(coarse * ball, fine * ball).reshape(EXTENDED, rows_l, cols)
    v_row = _twiddle(coarse * cols + ball, fine * cols).reshape(EXTENDED, rows_l, cols)
    return w_col, w_row, v_row


SMEM_SPEC = pl.BlockSpec(memory_space=pltpu.SMEM)


def _split_store(me_ref, first, second, own_ref, send_ref):
    top = me_ref[0] == 0

    @pl.when(top)
    def _():
        own_ref[...] = first
        send_ref[...] = second

    @pl.when(jnp.logical_not(top))
    def _():
        own_ref[...] = second
        send_ref[...] = first


def _inv_row_kernel(me_ref, y_ref, w_ref, ft_ref, own_ref, send_ref, h_ref):
    ft = ft_ref[...]
    n, rows, _ = y_ref.shape
    for l in range(n):
        h = jnp.dot(ft, y_ref[l], preferred_element_type=F32)
        h_ref[l] = (h / w_ref[l]).astype(BF16)
    half = rows // 2
    _split_store(me_ref, h_ref[:, :half, :], h_ref[:, half:, :], own_ref, send_ref)


def inv_row(me_arr, y, w_col, ft, e0):
    n, rows, cols_l = y.shape
    eb0 = e0 // BLK
    blk = pl.BlockSpec((BLK, rows, cols_l), lambda i: (i, 0, 0))
    out = pl.BlockSpec((BLK, rows // 2, cols_l), lambda i: (i, 0, 0))
    return pl.pallas_call(
        _inv_row_kernel,
        grid=(n // BLK,),
        in_specs=[
            SMEM_SPEC,
            blk,
            pl.BlockSpec((BLK, rows, cols_l), lambda i: (i + eb0, 0, 0)),
            pl.BlockSpec((rows, rows), lambda i: (0, 0)),
        ],
        out_specs=[out, out],
        out_shape=[jax.ShapeDtypeStruct((n, rows // 2, cols_l), BF16)] * 2,
        scratch_shapes=[pltpu.VMEM((BLK, rows, cols_l), BF16)],
    )(me_arr, y, w_col, ft)


def _inv_col_kernel(own_ref, recv_ref, v_ref, fo_ref, fr_ref, out_ref):
    n, rows_l, half = own_ref.shape
    a = own_ref[...].reshape(n * rows_l, half)
    b = recv_ref[...].reshape(n * rows_l, half)
    x = jnp.dot(a, fo_ref[...], preferred_element_type=F32)
    x = x + jnp.dot(b, fr_ref[...], preferred_element_type=F32)
    x = x.reshape(n, rows_l, -1)
    out_ref[...] = (x / v_ref[...]).astype(BF16)


def inv_col(own, recv, v_row, f_own, f_oth, e0):
    n, rows_l, half = own.shape
    cols = 2 * half
    eb0 = e0 // BLK
    blk = pl.BlockSpec((BLK, rows_l, half), lambda i: (i, 0, 0))
    return pl.pallas_call(
        _inv_col_kernel,
        grid=(n // BLK,),
        in_specs=[
            blk,
            blk,
            pl.BlockSpec((BLK, rows_l, cols), lambda i: (i + eb0, 0, 0)),
            pl.BlockSpec((half, cols), lambda i: (0, 0)),
            pl.BlockSpec((half, cols), lambda i: (0, 0)),
        ],
        out_specs=pl.BlockSpec((BLK, rows_l, cols), lambda i: (i, 0, 0)),
        out_shape=jax.ShapeDtypeStruct((n, rows_l, cols), BF16),
    )(own, recv, v_row, f_own, f_oth)


def _fwd_col_kernel(me_ref, x_ref, v_ref, w_ref, ft_ref, own_ref, send_ref):
    n, rows_l, cols = x_ref.shape
    g = (x_ref[...].astype(F32) * v_ref[...]).astype(BF16)
    h = jnp.dot(g.reshape(n * rows_l, cols), ft_ref[...], preferred_element_type=F32)
    h = (h.reshape(n, rows_l, cols) * w_ref[...]).astype(BF16)
    half = cols // 2
    _split_store(me_ref, h[:, :, :half], h[:, :, half:], own_ref, send_ref)


def fwd_col(me_arr, x, v_row, w_row, ft, table_block):
    groups, n, rows_l, cols = x.shape
    half = cols // 2
    xs = pl.BlockSpec((None, BLK, rows_l, cols), lambda j, t: (j, t, 0, 0))
    ts = pl.BlockSpec((BLK, rows_l, cols), lambda j, t: (table_block(j, t), 0, 0))
    os = pl.BlockSpec((None, BLK, rows_l, half), lambda j, t: (j, t, 0, 0))
    return pl.pallas_call(
        _fwd_col_kernel,
        grid=(groups, n // BLK),
        in_specs=[SMEM_SPEC, xs, ts, ts, pl.BlockSpec((cols, cols), lambda j, t: (0, 0))],
        out_specs=[os, os],
        out_shape=[jax.ShapeDtypeStruct((groups, n, rows_l, half), BF16)] * 2,
    )(me_arr, x, v_row, w_row, ft)


def _product_kernel(eb0, g_ref, fo_ref, fr_ref, cip_ref, key_ref, *rest):
    halves = rest[: 2 * DIGITS]
    out_ref, acc_ref = rest[2 * DIGITS :]
    eb = pl.program_id(0) + eb0
    fo = fo_ref[...]
    fr = fr_ref[...]
    acc_ref[...] = jnp.zeros_like(acc_ref)
    n = acc_ref.shape[0]
    for gv in range(2):
        for j in range(DIGITS):
            own_ref, recv_ref = halves[2 * j], halves[2 * j + 1]
            kd = (j - gv) % DIGITS

            @pl.when(jnp.logical_and(g_ref[0] == gv, eb == j))
            def _():
                acc_ref[...] += cip_ref[...].astype(F32) * key_ref[kd].astype(F32)

            @pl.when(jnp.logical_and(g_ref[0] == gv, eb != j))
            def _():
                for l in range(n):
                    y = jnp.dot(fo, own_ref[l], preferred_element_type=F32)
                    y = (y + jnp.dot(fr, recv_ref[l], preferred_element_type=F32)).astype(BF16)
                    acc_ref[l] += y.astype(F32) * key_ref[kd, l].astype(F32)

    out_ref[...] = acc_ref[...].astype(BF16)


def product(cip, key, g_arr, own2, recv2, f_own, f_oth, eb0, nblocks):
    _, rows, cols_l = cip.shape
    rows_l = rows // 2

    def lifted_block(j):
        def index(i):
            eb = i + eb0
            tb = jnp.where(eb < j, eb, eb - 1)
            return (j, jnp.clip(tb, 0, DIGITS - 1), 0, 0)

        return pl.BlockSpec((None, BLK, rows_l, cols_l), index)

    half_specs = []
    half_args = []
    for j in range(DIGITS):
        half_specs += [lifted_block(j), lifted_block(j)]
        half_args += [own2, recv2]
    return pl.pallas_call(
        lambda *refs: _product_kernel(eb0, *refs),
        grid=(nblocks,),
        in_specs=[
            SMEM_SPEC,
            pl.BlockSpec((rows, rows_l), lambda i: (0, 0)),
            pl.BlockSpec((rows, rows_l), lambda i: (0, 0)),
            pl.BlockSpec(
                (BLK, rows, cols_l), lambda i: (jnp.minimum(i + eb0, DIGITS - 1), 0, 0)
            ),
            pl.BlockSpec((DIGITS, BLK, rows, cols_l), lambda i: (0, i + eb0, 0, 0)),
        ]
        + half_specs,
        out_specs=pl.BlockSpec((BLK, rows, cols_l), lambda i: (i, 0, 0)),
        out_shape=jax.ShapeDtypeStruct((nblocks * BLK, rows, cols_l), BF16),
        scratch_shapes=[pltpu.VMEM((BLK, rows, cols_l), F32)],
    )(g_arr, f_own, f_oth, cip, key, *half_args)


def _final_kernel(fo_ref, fr_ref, own_ref, recv_ref, prod_ref, s_ref, out_ref):
    fo = fo_ref[...]
    fr = fr_ref[...]
    for l in range(own_ref.shape[0]):
        y = jnp.dot(fo, own_ref[l], preferred_element_type=F32)
        y = (y + jnp.dot(fr, recv_ref[l], preferred_element_type=F32)).astype(BF16)
        diff = prod_ref[l].astype(F32) - y.astype(F32)
        out_ref[l] = (diff * s_ref[l]).astype(BF16)


def final(own4, recv4, prod, scale, f_own, f_oth):
    n, rows, cols_l = prod.shape
    rows_l = rows // 2
    hs = pl.BlockSpec((BLK, rows_l, cols_l), lambda i: (i, 0, 0))
    return pl.pallas_call(
        _final_kernel,
        grid=(n // BLK,),
        in_specs=[
            pl.BlockSpec((rows, rows_l), lambda i: (0, 0)),
            pl.BlockSpec((rows, rows_l), lambda i: (0, 0)),
            hs,
            hs,
            pl.BlockSpec((BLK, rows, cols_l), lambda i: (i, 0, 0)),
            pl.BlockSpec((BLK, 1, cols_l), lambda i: (i, 0, 0)),
        ],
        out_specs=pl.BlockSpec((BLK, rows, cols_l), lambda i: (i, 0, 0)),
        out_shape=jax.ShapeDtypeStruct((n, rows, cols_l), BF16),
    )(f_own, f_oth, own4, recv4, prod, scale)


def snake_ring(n):
    if n % 2:
        return list(range(n))
    outer = n // 2
    return [2 * a for a in range(outer)] + [2 * a + 1 for a in reversed(range(outer))]


def ring_setup(shard):
    n = lax.axis_size("limb")
    me_l = lax.axis_index("limb")
    g = lax.axis_index("grp")
    order = snake_ring(n)
    pos = [0] * n
    for i, l in enumerate(order):
        pos[l] = i
    p = jnp.array(pos, I32)[me_l]
    piece = lax.dynamic_slice_in_dim(shard, g, 2, axis=0)
    width = shard.shape[1]
    full = jnp.zeros((DIGITS, n * width) + shard.shape[2:], shard.dtype)
    full = lax.dynamic_update_slice(full, piece, (0, me_l * width, 0, 0))
    own_side = lax.dynamic_slice_in_dim(shard, 2 - 2 * g, 1, axis=0)
    full = lax.dynamic_update_slice(full, own_side, (2, me_l * width, 0, 0))
    order_arr = jnp.array(order, I32)
    return dict(
        full=full,
        width=width,
        src=[order_arr[(p - k) % n] * width for k in range(n)],
        n=n,
        g=g,
        cw=[(order[i], order[(i + 1) % n]) for i in range(n)],
        ccw=[(order[i], order[(i - 1) % n]) for i in range(n)],
        a=piece,
        b=piece,
        s=0,
        fresh=[],
        pending=[],
    )


def ring_steps(st):
    return st["n"] // 2


def _to_partner(x, g):
    return lax.ppermute(lax.dynamic_slice_in_dim(x, g, 1, axis=0), "grp", [(0, 1), (1, 0)])


def ring_step(st):
    n = st["n"]
    st["s"] += 1
    if 2 * st["s"] < n:
        st["a"] = lax.ppermute(st["a"], "limb", st["cw"])
        st["b"] = lax.ppermute(st["b"], "limb", st["ccw"])
        st["fresh"] = [st["a"], st["b"]]
    else:
        h = st["a"].shape[2] // 2
        a = lax.ppermute(st["a"][:, :, :h], "limb", st["cw"])
        b = lax.ppermute(st["b"][:, :, h:], "limb", st["ccw"])
        st["fresh"] = [jnp.concatenate([a, b], axis=2)]


def _settle(st, x):
    fresh, pending = st["fresh"], st["pending"]
    fresh, pending, st["full"], x = lax.optimization_barrier((fresh, pending, st["full"], x))
    _place(st, st["s"], fresh, 0)
    _place(st, st["s"] - 1, pending, 2)
    if len(fresh) == 2:
        st["a"], st["b"] = fresh
    st["pending"] = [_to_partner(jnp.concatenate(fresh, axis=1), st["g"])]
    st["fresh"] = []
    return x


def _place(st, s, pieces, digit):
    if s < 1 or not pieces:
        return
    n, w = st["n"], st["width"]
    if len(pieces) == 2:
        parts = [(pieces[0], s), (pieces[1], -s)]
    elif pieces[0].shape[1] == 2 * w:
        parts = [(pieces[0][:, :w], s), (pieces[0][:, w:], -s)]
    else:
        parts = [(pieces[0], s)]
    for part, k in parts:
        st["full"] = lax.dynamic_update_slice(st["full"], part, (digit, st["src"][k % n], 0, 0))


def ring_hold(st, x):
    if st["s"] >= ring_steps(st):
        return x
    x = _settle(st, x)
    ring_step(st)
    return x


def ring_finish(st, x):
    while st["s"] < ring_steps(st):
        x = _settle(st, x)
        ring_step(st)
    if st["fresh"]:
        x = _settle(st, x)
    _place(st, st["s"], st["pending"], 2)
    return st["full"], x

def swap(x):
    return lax.ppermute(x, "coef", perm=[(0, 1), (1, 0)])


def body(cipher, switch_key, raise_table, lower_table, special_inverse):
    nc = lax.axis_size("coef")
    me = lax.axis_index("coef")
    me_arr = jnp.reshape(me, (1,)).astype(I32)
    other = 1 - me
    _, limbs, rows, cols_l = cipher.shape
    cols = cols_l * nc
    rows_l = rows // nc

    ring = ring_setup(switch_key[0])
    if ring_steps(ring):
        ring_step(ring)

    f_rows = cosine_table(rows)
    f_cols = cosine_table(cols)
    ft_rows = f_rows.T
    ft_cols = f_cols.T
    fc_own = lax.dynamic_slice_in_dim(f_cols, me * cols_l, cols_l, axis=0)
    fc_oth = lax.dynamic_slice_in_dim(f_cols, other * cols_l, cols_l, axis=0)
    fr_own = lax.dynamic_slice_in_dim(f_rows, me * rows_l, rows_l, axis=1)
    fr_oth = lax.dynamic_slice_in_dim(f_rows, other * rows_l, rows_l, axis=1)
    w_col, w_row, v_row = twiddle_tables(me, rows, cols, nc)

    ct = cipher[0]
    own1, send1 = inv_row(me_arr, ct, w_col, ft_rows, 0)
    own1 = ring_hold(ring, own1)
    coeffs = inv_col(own1, swap(send1), v_row, fc_own, fc_oth, 0)

    coeffs = ring_hold(ring, coeffs)
    blocks = coeffs.reshape(DIGITS, DIGIT_LIMBS, rows_l, cols)
    raised = lax.dot_general(
        raise_table, blocks, (((2,), (1,)), ((0,), (0,))), preferred_element_type=F32
    ).astype(BF16)

    raised = ring_hold(ring, raised)
    own2, send2 = fwd_col(
        me_arr, raised, v_row, w_row, ft_cols, lambda j, t: jnp.where(t >= j, t + 1, t)
    )
    key, (own2, send2) = ring_finish(ring, (own2, send2))
    recv2 = swap(send2)
    g_arr = jnp.reshape(ring["g"], (1,)).astype(I32)

    prod_special = product(ct, key, g_arr, own2, recv2, fr_own, fr_oth, DIGITS, 1)
    prod_cipher = product(ct, key, g_arr, own2, recv2, fr_own, fr_oth, 0, DIGITS)

    own3, send3 = inv_row(me_arr, prod_special, w_col, ft_rows, limbs)
    special = inv_col(own3, swap(send3), v_row, fc_own, fc_oth, limbs)
    lowered = lax.dot_general(
        lower_table, special, (((1,), (0,)), ((), ())), preferred_element_type=F32
    )
    lowered = lowered.astype(BF16)[None]
    own4, send4 = fwd_col(me_arr, lowered, v_row, w_row, ft_cols, lambda j, t: t)
    scale = jnp.broadcast_to(special_inverse[:, None, None], (limbs, 1, cols_l))
    result = final(own4[0], swap(send4)[0], prod_cipher, scale, fr_own, fr_oth)
    return result[None, None]


def solution(mesh):
    in_specs = (
        P(("grp", "limb"), None, None, "coef"),
        P(None, None, "limb", None, "coef"),
        P(),
        P(),
        P(),
    )
    out_specs = P(None, ("grp", "limb"), None, None, "coef")
    return jax.shard_map(body, mesh=mesh, in_specs=in_specs, out_specs=out_specs, check_vma=False)
```

```python
import math

import jax
import ml_dtypes
import numpy as np
import jax.numpy as jnp
from jax import lax
from jax.experimental import pallas as pl
from jax.experimental.pallas import tpu as pltpu
from jax.sharding import PartitionSpec as P

LIMBS = 48
DIGITS = 3
DIGIT_LIMBS = 16
EXTENDED = 64
CYCLE = 32768
BLK = 16

F32 = jnp.float32
BF16 = jnp.bfloat16
I32 = jnp.int32


def cosine_table(size):
    freq = np.arange(size, dtype=np.float64)[:, None]
    place = np.arange(size, dtype=np.float64)[None, :]
    norm = np.where(freq == 0, math.sqrt(1.0 / size), math.sqrt(2.0 / size))
    return (norm * np.cos(math.pi * (2.0 * place + 1.0) * freq / (2.0 * size))).astype(
        ml_dtypes.bfloat16
    )


def _angle(phase):
    ang = (2.0 * math.pi / CYCLE) * phase.astype(F32)
    return jnp.cos(ang), jnp.sin(ang)


def _limb_angle(c):
    shape = (-1,) + (1,) * c.ndim
    hi = jnp.arange(EXTENDED // 8, dtype=I32).reshape(shape)
    lo = (2 * jnp.arange(8, dtype=I32) + 1).reshape(shape)
    ch, sh = _angle((16 * hi * c[None]) % CYCLE)
    cl, sl = _angle((lo * c[None]) % CYCLE)
    cos = ch[:, None] * cl[None] - sh[:, None] * sl[None]
    sin = sh[:, None] * cl[None] + ch[:, None] * sl[None]
    return cos.reshape((EXTENDED,) + c.shape), sin.reshape((EXTENDED,) + c.shape)


def _twiddle(p, q):
    cp, sp = _limb_angle(p % CYCLE)
    cq, sq = _limb_angle(q % CYCLE)
    cp, sp, cq, sq = lax.optimization_barrier((cp, sp, cq, sq))
    return 1.0 + 0.5 * (cp * cq - sp * sq)


def col_table(me, rows, cols, nc):
    cols_l = cols // nc
    fine = jnp.arange(8, dtype=I32)[None, :, None]
    coarse = (8 * jnp.arange(rows // 8, dtype=I32))[:, None, None]
    bcol = (me * cols_l + jnp.arange(cols_l, dtype=I32))[None, None, :]
    return _twiddle(coarse * bcol, fine * bcol).reshape(EXTENDED, rows, cols_l)


def row_tables(me, rows, cols, nc):
    rows_l = rows // nc
    fine = jnp.arange(8, dtype=I32)[None, :, None]
    coarse = (me * rows_l + 8 * jnp.arange(rows_l // 8, dtype=I32))[:, None, None]
    ball = jnp.arange(cols, dtype=I32)[None, None, :]
    w_row = _twiddle(coarse * ball, fine * ball).reshape(EXTENDED, rows_l, cols)
    v_row = _twiddle(coarse * cols + ball, fine * cols).reshape(EXTENDED, rows_l, cols)
    return w_row, v_row


SMEM_SPEC = pl.BlockSpec(memory_space=pltpu.SMEM)


def _split_store(me_ref, first, second, own_ref, send_ref):
    top = me_ref[0] == 0

    @pl.when(top)
    def _():
        own_ref[...] = first
        send_ref[...] = second

    @pl.when(jnp.logical_not(top))
    def _():
        own_ref[...] = second
        send_ref[...] = first


def _inv_row_kernel(me_ref, y_ref, w_ref, ft_ref, own_ref, send_ref, h_ref):
    ft = ft_ref[...]
    n, rows, _ = y_ref.shape
    for l in range(n):
        h = jnp.dot(ft, y_ref[l], preferred_element_type=F32)
        h_ref[l] = (h / w_ref[l]).astype(BF16)
    half = rows // 2
    _split_store(me_ref, h_ref[:, :half, :], h_ref[:, half:, :], own_ref, send_ref)


def inv_row(me_arr, y, w_col, ft, e0):
    n, rows, cols_l = y.shape
    eb0 = e0 // BLK
    blk = pl.BlockSpec((BLK, rows, cols_l), lambda i: (i, 0, 0))
    out = pl.BlockSpec((BLK, rows // 2, cols_l), lambda i: (i, 0, 0))
    return pl.pallas_call(
        _inv_row_kernel,
        grid=(n // BLK,),
        in_specs=[
            SMEM_SPEC,
            blk,
            pl.BlockSpec((BLK, rows, cols_l), lambda i: (i + eb0, 0, 0)),
            pl.BlockSpec((rows, rows), lambda i: (0, 0)),
        ],
        out_specs=[out, out],
        out_shape=[jax.ShapeDtypeStruct((n, rows // 2, cols_l), BF16)] * 2,
        scratch_shapes=[pltpu.VMEM((BLK, rows, cols_l), BF16)],
    )(me_arr, y, w_col, ft)


def _inv_col_kernel(own_ref, recv_ref, v_ref, fo_ref, fr_ref, out_ref):
    n, rows_l, half = own_ref.shape
    a = own_ref[...].reshape(n * rows_l, half)
    b = recv_ref[...].reshape(n * rows_l, half)
    x = jnp.dot(a, fo_ref[...], preferred_element_type=F32)
    x = x + jnp.dot(b, fr_ref[...], preferred_element_type=F32)
    x = x.reshape(n, rows_l, -1)
    out_ref[...] = (x / v_ref[...]).astype(BF16)


def inv_col(own, recv, v_row, f_own, f_oth, e0):
    n, rows_l, half = own.shape
    cols = 2 * half
    eb0 = e0 // BLK
    blk = pl.BlockSpec((BLK, rows_l, half), lambda i: (i, 0, 0))
    return pl.pallas_call(
        _inv_col_kernel,
        grid=(n // BLK,),
        in_specs=[
            blk,
            blk,
            pl.BlockSpec((BLK, rows_l, cols), lambda i: (i + eb0, 0, 0)),
            pl.BlockSpec((half, cols), lambda i: (0, 0)),
            pl.BlockSpec((half, cols), lambda i: (0, 0)),
        ],
        out_specs=pl.BlockSpec((BLK, rows_l, cols), lambda i: (i, 0, 0)),
        out_shape=jax.ShapeDtypeStruct((n, rows_l, cols), BF16),
    )(own, recv, v_row, f_own, f_oth)


def _fwd_col_kernel(me_ref, x_ref, v_ref, w_ref, ft_ref, own_ref, send_ref):
    n, rows_l, cols = x_ref.shape
    g = (x_ref[...].astype(F32) * v_ref[...]).astype(BF16)
    h = jnp.dot(g.reshape(n * rows_l, cols), ft_ref[...], preferred_element_type=F32)
    h = (h.reshape(n, rows_l, cols) * w_ref[...]).astype(BF16)
    half = cols // 2
    _split_store(me_ref, h[:, :, :half], h[:, :, half:], own_ref, send_ref)


def fwd_col(me_arr, x, v_row, w_row, ft, table_block):
    groups, n, rows_l, cols = x.shape
    half = cols // 2
    xs = pl.BlockSpec((None, BLK, rows_l, cols), lambda j, t: (j, t, 0, 0))
    ts = pl.BlockSpec((BLK, rows_l, cols), lambda j, t: (table_block(j, t), 0, 0))
    os = pl.BlockSpec((None, BLK, rows_l, half), lambda j, t: (j, t, 0, 0))
    return pl.pallas_call(
        _fwd_col_kernel,
        grid=(groups, n // BLK),
        in_specs=[SMEM_SPEC, xs, ts, ts, pl.BlockSpec((cols, cols), lambda j, t: (0, 0))],
        out_specs=[os, os],
        out_shape=[jax.ShapeDtypeStruct((groups, n, rows_l, half), BF16)] * 2,
    )(me_arr, x, v_row, w_row, ft)


def _product_kernel(eb0, g_ref, fo_ref, fr_ref, cip_ref, key_ref, *rest):
    halves = rest[: 2 * DIGITS]
    out_ref, acc_ref = rest[2 * DIGITS :]
    eb = pl.program_id(0) + eb0
    fo = fo_ref[...]
    fr = fr_ref[...]
    acc_ref[...] = jnp.zeros_like(acc_ref)
    n = acc_ref.shape[0]
    for gv in range(2):
        for j in range(DIGITS):
            own_ref, recv_ref = halves[2 * j], halves[2 * j + 1]
            kd = (j - gv) % DIGITS

            @pl.when(jnp.logical_and(g_ref[0] == gv, eb == j))
            def _():
                acc_ref[...] += cip_ref[...].astype(F32) * key_ref[kd].astype(F32)

            @pl.when(jnp.logical_and(g_ref[0] == gv, eb != j))
            def _():
                for l in range(n):
                    y = jnp.dot(fo, own_ref[l], preferred_element_type=F32)
                    y = (y + jnp.dot(fr, recv_ref[l], preferred_element_type=F32)).astype(BF16)
                    acc_ref[l] += y.astype(F32) * key_ref[kd, l].astype(F32)

    out_ref[...] = acc_ref[...].astype(BF16)


def product(cip, key, g_arr, own2, recv2, f_own, f_oth, eb0, nblocks):
    _, rows, cols_l = cip.shape
    rows_l = rows // 2

    def lifted_block(j):
        def index(i):
            eb = i + eb0
            tb = jnp.where(eb < j, eb, eb - 1)
            return (j, jnp.clip(tb, 0, DIGITS - 1), 0, 0)

        return pl.BlockSpec((None, BLK, rows_l, cols_l), index)

    half_specs = []
    half_args = []
    for j in range(DIGITS):
        half_specs += [lifted_block(j), lifted_block(j)]
        half_args += [own2, recv2]
    return pl.pallas_call(
        lambda *refs: _product_kernel(eb0, *refs),
        grid=(nblocks,),
        in_specs=[
            SMEM_SPEC,
            pl.BlockSpec((rows, rows_l), lambda i: (0, 0)),
            pl.BlockSpec((rows, rows_l), lambda i: (0, 0)),
            pl.BlockSpec(
                (BLK, rows, cols_l), lambda i: (jnp.minimum(i + eb0, DIGITS - 1), 0, 0)
            ),
            pl.BlockSpec((DIGITS, BLK, rows, cols_l), lambda i: (0, i + eb0, 0, 0)),
        ]
        + half_specs,
        out_specs=pl.BlockSpec((BLK, rows, cols_l), lambda i: (i, 0, 0)),
        out_shape=jax.ShapeDtypeStruct((nblocks * BLK, rows, cols_l), BF16),
        scratch_shapes=[pltpu.VMEM((BLK, rows, cols_l), F32)],
    )(g_arr, f_own, f_oth, cip, key, *half_args)


def _final_kernel(fo_ref, fr_ref, own_ref, recv_ref, prod_ref, s_ref, out_ref):
    fo = fo_ref[...]
    fr = fr_ref[...]
    for l in range(own_ref.shape[0]):
        y = jnp.dot(fo, own_ref[l], preferred_element_type=F32)
        y = (y + jnp.dot(fr, recv_ref[l], preferred_element_type=F32)).astype(BF16)
        diff = prod_ref[l].astype(F32) - y.astype(F32)
        out_ref[l] = (diff * s_ref[l]).astype(BF16)


def final(own4, recv4, prod, scale, f_own, f_oth):
    n, rows, cols_l = prod.shape
    rows_l = rows // 2
    hs = pl.BlockSpec((BLK, rows_l, cols_l), lambda i: (i, 0, 0))
    return pl.pallas_call(
        _final_kernel,
        grid=(n // BLK,),
        in_specs=[
            pl.BlockSpec((rows, rows_l), lambda i: (0, 0)),
            pl.BlockSpec((rows, rows_l), lambda i: (0, 0)),
            hs,
            hs,
            pl.BlockSpec((BLK, rows, cols_l), lambda i: (i, 0, 0)),
            pl.BlockSpec((BLK, 1, cols_l), lambda i: (i, 0, 0)),
        ],
        out_specs=pl.BlockSpec((BLK, rows, cols_l), lambda i: (i, 0, 0)),
        out_shape=jax.ShapeDtypeStruct((n, rows, cols_l), BF16),
    )(f_own, f_oth, own4, recv4, prod, scale)


def snake_ring(n):
    if n % 2:
        return list(range(n))
    outer = n // 2
    return [2 * a for a in range(outer)] + [2 * a + 1 for a in reversed(range(outer))]


def ring_setup(shard):
    n = lax.axis_size("limb")
    me_l = lax.axis_index("limb")
    g = lax.axis_index("grp")
    order = snake_ring(n)
    pos = [0] * n
    for i, l in enumerate(order):
        pos[l] = i
    p = jnp.array(pos, I32)[me_l]
    piece = lax.dynamic_slice_in_dim(shard, g, 2, axis=0)
    width = shard.shape[1]
    full = jnp.zeros((DIGITS, n * width) + shard.shape[2:], shard.dtype)
    full = lax.dynamic_update_slice(full, piece, (0, me_l * width, 0, 0))
    own_side = lax.dynamic_slice_in_dim(shard, 2 - 2 * g, 1, axis=0)
    full = lax.dynamic_update_slice(full, own_side, (2, me_l * width, 0, 0))
    order_arr = jnp.array(order, I32)
    return dict(
        full=full,
        width=width,
        src=[order_arr[(p - k) % n] * width for k in range(n)],
        n=n,
        g=g,
        cw=[(order[i], order[(i + 1) % n]) for i in range(n)],
        ccw=[(order[i], order[(i - 1) % n]) for i in range(n)],
        a=piece,
        b=piece,
        s=0,
        fresh=[],
        pending=[],
    )


def ring_steps(st):
    return st["n"] // 2


def _to_partner(x, g):
    return lax.ppermute(lax.dynamic_slice_in_dim(x, g, 1, axis=0), "grp", [(0, 1), (1, 0)])


def ring_step(st):
    n = st["n"]
    st["s"] += 1
    if 2 * st["s"] < n:
        st["a"] = lax.ppermute(st["a"], "limb", st["cw"])
        st["b"] = lax.ppermute(st["b"], "limb", st["ccw"])
        st["fresh"] = [st["a"], st["b"]]
    else:
        h = st["a"].shape[2] // 2
        a = lax.ppermute(st["a"][:, :, :h], "limb", st["cw"])
        b = lax.ppermute(st["b"][:, :, h:], "limb", st["ccw"])
        st["fresh"] = [jnp.concatenate([a, b], axis=2)]


def _settle(st, x):
    fresh, pending = st["fresh"], st["pending"]
    fresh, pending, st["full"], x = lax.optimization_barrier((fresh, pending, st["full"], x))
    _place(st, st["s"], fresh, 0)
    _place(st, st["s"] - 1, pending, 2)
    if len(fresh) == 2:
        st["a"], st["b"] = fresh
    st["pending"] = [_to_partner(jnp.concatenate(fresh, axis=1), st["g"])]
    st["fresh"] = []
    return x


def _place(st, s, pieces, digit):
    if s < 1 or not pieces:
        return
    n, w = st["n"], st["width"]
    if len(pieces) == 2:
        parts = [(pieces[0], s), (pieces[1], -s)]
    elif pieces[0].shape[1] == 2 * w:
        parts = [(pieces[0][:, :w], s), (pieces[0][:, w:], -s)]
    else:
        parts = [(pieces[0], s)]
    for part, k in parts:
        st["full"] = lax.dynamic_update_slice(st["full"], part, (digit, st["src"][k % n], 0, 0))


def ring_hold(st, x):
    if st["s"] >= ring_steps(st):
        return x
    x = _settle(st, x)
    ring_step(st)
    return x


def ring_finish(st, x):
    while st["s"] < ring_steps(st):
        x = _settle(st, x)
        ring_step(st)
    if st["fresh"]:
        x = _settle(st, x)
    _place(st, st["s"], st["pending"], 2)
    return st["full"], x

def swap(x):
    return lax.ppermute(x, "coef", perm=[(0, 1), (1, 0)])


def body(cipher, switch_key, raise_table, lower_table, special_inverse):
    nc = lax.axis_size("coef")
    me = lax.axis_index("coef")
    me_arr = jnp.reshape(me, (1,)).astype(I32)
    other = 1 - me
    _, limbs, rows, cols_l = cipher.shape
    cols = cols_l * nc
    rows_l = rows // nc

    ring = ring_setup(switch_key[0])
    if ring_steps(ring):
        ring_step(ring)

    f_rows = cosine_table(rows)
    f_cols = cosine_table(cols)
    ft_rows = f_rows.T
    ft_cols = f_cols.T
    fc_own = lax.dynamic_slice_in_dim(f_cols, me * cols_l, cols_l, axis=0)
    fc_oth = lax.dynamic_slice_in_dim(f_cols, other * cols_l, cols_l, axis=0)
    fr_own = lax.dynamic_slice_in_dim(f_rows, me * rows_l, rows_l, axis=1)
    fr_oth = lax.dynamic_slice_in_dim(f_rows, other * rows_l, rows_l, axis=1)
    w_col = col_table(me, rows, cols, nc)

    ct = cipher[0]
    own1, send1 = inv_row(me_arr, ct, w_col, ft_rows, 0)
    own1, me_late = ring_hold(ring, (own1, me))
    w_row, v_row = row_tables(me_late, rows, cols, nc)
    coeffs = inv_col(own1, swap(send1), v_row, fc_own, fc_oth, 0)

    coeffs = ring_hold(ring, coeffs)
    blocks = coeffs.reshape(DIGITS, DIGIT_LIMBS, rows_l, cols)
    raised = lax.dot_general(
        raise_table, blocks, (((2,), (1,)), ((0,), (0,))), preferred_element_type=F32
    ).astype(BF16)

    raised = ring_hold(ring, raised)
    own2, send2 = fwd_col(
        me_arr, raised, v_row, w_row, ft_cols, lambda j, t: jnp.where(t >= j, t + 1, t)
    )
    key, (own2, send2) = ring_finish(ring, (own2, send2))
    recv2 = swap(send2)
    g_arr = jnp.reshape(ring["g"], (1,)).astype(I32)

    prod_special = product(ct, key, g_arr, own2, recv2, fr_own, fr_oth, DIGITS, 1)
    prod_cipher = product(ct, key, g_arr, own2, recv2, fr_own, fr_oth, 0, DIGITS)

    own3, send3 = inv_row(me_arr, prod_special, w_col, ft_rows, limbs)
    special = inv_col(own3, swap(send3), v_row, fc_own, fc_oth, limbs)
    lowered = lax.dot_general(
        lower_table, special, (((1,), (0,)), ((), ())), preferred_element_type=F32
    )
    lowered = lowered.astype(BF16)[None]
    own4, send4 = fwd_col(me_arr, lowered, v_row, w_row, ft_cols, lambda j, t: t)
    scale = jnp.broadcast_to(special_inverse[:, None, None], (limbs, 1, cols_l))
    result = final(own4[0], swap(send4)[0], prod_cipher, scale, fr_own, fr_oth)
    return result[None, None]


def solution(mesh):
    in_specs = (
        P(("grp", "limb"), None, None, "coef"),
        P(None, None, "limb", None, "coef"),
        P(),
        P(),
        P(),
    )
    out_specs = P(None, ("grp", "limb"), None, None, "coef")
    return jax.shard_map(body, mesh=mesh, in_specs=in_specs, out_specs=out_specs, check_vma=False)
```

```python
import math

import jax
import ml_dtypes
import numpy as np
import jax.numpy as jnp
from jax import lax
from jax.experimental import pallas as pl
from jax.experimental.pallas import tpu as pltpu
from jax.sharding import PartitionSpec as P

LIMBS = 48
DIGITS = 3
DIGIT_LIMBS = 16
EXTENDED = 64
CYCLE = 32768
BLK = 16

F32 = jnp.float32
BF16 = jnp.bfloat16
I32 = jnp.int32


def cosine_table(size):
    freq = np.arange(size, dtype=np.float64)[:, None]
    place = np.arange(size, dtype=np.float64)[None, :]
    norm = np.where(freq == 0, math.sqrt(1.0 / size), math.sqrt(2.0 / size))
    return (norm * np.cos(math.pi * (2.0 * place + 1.0) * freq / (2.0 * size))).astype(
        ml_dtypes.bfloat16
    )


def _angle(phase):
    ang = (2.0 * math.pi / CYCLE) * phase.astype(F32)
    return jnp.cos(ang), jnp.sin(ang)


def _limb_angle(c):
    shape = (-1,) + (1,) * c.ndim
    hi = jnp.arange(EXTENDED // 8, dtype=I32).reshape(shape)
    lo = (2 * jnp.arange(8, dtype=I32) + 1).reshape(shape)
    ch, sh = _angle((16 * hi * c[None]) % CYCLE)
    cl, sl = _angle((lo * c[None]) % CYCLE)
    cos = ch[:, None] * cl[None] - sh[:, None] * sl[None]
    sin = sh[:, None] * cl[None] + ch[:, None] * sl[None]
    return cos.reshape((EXTENDED,) + c.shape), sin.reshape((EXTENDED,) + c.shape)


def _twiddle(p, q):
    cp, sp = _limb_angle(p % CYCLE)
    cq, sq = _limb_angle(q % CYCLE)
    cp, sp, cq, sq = lax.optimization_barrier((cp, sp, cq, sq))
    return 1.0 + 0.5 * (cp * cq - sp * sq)


def twiddle_tables(me, rows, cols, nc):
    rows_l, cols_l = rows // nc, cols // nc
    fine = jnp.arange(8, dtype=I32)[None, :, None]
    coarse = (8 * jnp.arange(rows // 8, dtype=I32))[:, None, None]
    bcol = (me * cols_l + jnp.arange(cols_l, dtype=I32))[None, None, :]
    w_col = _twiddle(coarse * bcol, fine * bcol).reshape(EXTENDED, rows, cols_l)
    coarse = (me * rows_l + 8 * jnp.arange(rows_l // 8, dtype=I32))[:, None, None]
    ball = jnp.arange(cols, dtype=I32)[None, None, :]
    w_row = _twiddle(coarse * ball, fine * ball).reshape(EXTENDED, rows_l, cols)
    v_row = _twiddle(coarse * cols + ball, fine * cols).reshape(EXTENDED, rows_l, cols)
    return w_col, w_row, v_row


SMEM_SPEC = pl.BlockSpec(memory_space=pltpu.SMEM)


def _split_store(me_ref, first, second, own_ref, send_ref):
    top = me_ref[0] == 0

    @pl.when(top)
    def _():
        own_ref[...] = first
        send_ref[...] = second

    @pl.when(jnp.logical_not(top))
    def _():
        own_ref[...] = second
        send_ref[...] = first


def _inv_row_kernel(me_ref, y_ref, w_ref, ft_ref, own_ref, send_ref, h_ref):
    ft = ft_ref[...]
    n, rows, _ = y_ref.shape
    for l in range(n):
        h = jnp.dot(ft, y_ref[l], preferred_element_type=F32)
        h_ref[l] = (h / w_ref[l]).astype(BF16)
    half = rows // 2
    _split_store(me_ref, h_ref[:, :half, :], h_ref[:, half:, :], own_ref, send_ref)


def inv_row(me_arr, y, w_col, ft, e0):
    n, rows, cols_l = y.shape
    eb0 = e0 // BLK
    blk = pl.BlockSpec((BLK, rows, cols_l), lambda i: (i, 0, 0))
    out = pl.BlockSpec((BLK, rows // 2, cols_l), lambda i: (i, 0, 0))
    return pl.pallas_call(
        _inv_row_kernel,
        grid=(n // BLK,),
        in_specs=[
            SMEM_SPEC,
            blk,
            pl.BlockSpec((BLK, rows, cols_l), lambda i: (i + eb0, 0, 0)),
            pl.BlockSpec((rows, rows), lambda i: (0, 0)),
        ],
        out_specs=[out, out],
        out_shape=[jax.ShapeDtypeStruct((n, rows // 2, cols_l), BF16)] * 2,
        scratch_shapes=[pltpu.VMEM((BLK, rows, cols_l), BF16)],
    )(me_arr, y, w_col, ft)


def _inv_col_kernel(own_ref, recv_ref, v_ref, fo_ref, fr_ref, out_ref):
    n, rows_l, half = own_ref.shape
    a = own_ref[...].reshape(n * rows_l, half)
    b = recv_ref[...].reshape(n * rows_l, half)
    x = jnp.dot(a, fo_ref[...], preferred_element_type=F32)
    x = x + jnp.dot(b, fr_ref[...], preferred_element_type=F32)
    x = x.reshape(n, rows_l, -1)
    out_ref[...] = (x / v_ref[...]).astype(BF16)


def inv_col(own, recv, v_row, f_own, f_oth, e0):
    n, rows_l, half = own.shape
    cols = 2 * half
    eb0 = e0 // BLK
    blk = pl.BlockSpec((BLK, rows_l, half), lambda i: (i, 0, 0))
    return pl.pallas_call(
        _inv_col_kernel,
        grid=(n // BLK,),
        in_specs=[
            blk,
            blk,
            pl.BlockSpec((BLK, rows_l, cols), lambda i: (i + eb0, 0, 0)),
            pl.BlockSpec((half, cols), lambda i: (0, 0)),
            pl.BlockSpec((half, cols), lambda i: (0, 0)),
        ],
        out_specs=pl.BlockSpec((BLK, rows_l, cols), lambda i: (i, 0, 0)),
        out_shape=jax.ShapeDtypeStruct((n, rows_l, cols), BF16),
    )(own, recv, v_row, f_own, f_oth)


def _fwd_col_kernel(sj_ref, st_ref, se_ref, me_ref, x_ref, v_ref, w_ref, ft_ref, own_ref, send_ref):
    n, rows_l, cols = x_ref.shape
    g = (x_ref[...].astype(F32) * v_ref[...]).astype(BF16)
    h = jnp.dot(g.reshape(n * rows_l, cols), ft_ref[...], preferred_element_type=F32)
    h = (h.reshape(n, rows_l, cols) * w_ref[...]).astype(BF16)
    half = cols // 2
    _split_store(me_ref, h[:, :, :half], h[:, :, half:], own_ref, send_ref)


def fwd_col(me_arr, x, v_row, w_row, ft, steps):
    groups, n, rows_l, cols = x.shape
    half = cols // 2
    sj, st, se = (jnp.array([step[k] for step in steps], I32) for k in range(3))
    xs = pl.BlockSpec((None, BLK, rows_l, cols), lambda i, a, b, c: (a[i], b[i], 0, 0))
    ts = pl.BlockSpec((BLK, rows_l, cols), lambda i, a, b, c: (c[i], 0, 0))
    os = pl.BlockSpec((None, BLK, rows_l, half), lambda i, a, b, c: (a[i], b[i], 0, 0))
    grid_spec = pltpu.PrefetchScalarGridSpec(
        num_scalar_prefetch=3,
        grid=(len(steps),),
        in_specs=[
            SMEM_SPEC,
            xs,
            ts,
            ts,
            pl.BlockSpec((cols, cols), lambda i, a, b, c: (0, 0)),
        ],
        out_specs=[os, os],
    )
    return pl.pallas_call(
        _fwd_col_kernel,
        grid_spec=grid_spec,
        out_shape=[jax.ShapeDtypeStruct((groups, n, rows_l, half), BF16)] * 2,
    )(sj, st, se, me_arr, x, v_row, w_row, ft)


def _product_kernel(eb0, fo_ref, fr_ref, cip_ref, key_ref, *rest):
    halves = rest[: 2 * DIGITS]
    out_ref, acc_ref = rest[2 * DIGITS :]
    eb = pl.program_id(0) + eb0
    fo = fo_ref[...]
    fr = fr_ref[...]
    acc_ref[...] = jnp.zeros_like(acc_ref)
    n = acc_ref.shape[0]
    for j in range(DIGITS):
        own_ref, recv_ref = halves[2 * j], halves[2 * j + 1]

        @pl.when(eb == j)
        def _():
            acc_ref[...] += cip_ref[...].astype(F32) * key_ref[j].astype(F32)

        @pl.when(eb != j)
        def _():
            for l in range(n):
                y = jnp.dot(fo, own_ref[l], preferred_element_type=F32)
                y = (y + jnp.dot(fr, recv_ref[l], preferred_element_type=F32)).astype(BF16)
                acc_ref[l] += y.astype(F32) * key_ref[j, l].astype(F32)

    out_ref[...] = acc_ref[...].astype(BF16)


def product(cip, key, own2, recv2, f_own, f_oth, eb0, nblocks):
    _, rows, cols_l = cip.shape
    rows_l = rows // 2

    def lifted_block(j):
        def index(i):
            eb = i + eb0
            tb = jnp.where(eb < j, eb, eb - 1)
            return (j, jnp.clip(tb, 0, DIGITS - 1), 0, 0)

        return pl.BlockSpec((None, BLK, rows_l, cols_l), index)

    half_specs = []
    half_args = []
    for j in range(DIGITS):
        half_specs += [lifted_block(j), lifted_block(j)]
        half_args += [own2, recv2]
    return pl.pallas_call(
        lambda *refs: _product_kernel(eb0, *refs),
        grid=(nblocks,),
        in_specs=[
            pl.BlockSpec((rows, rows_l), lambda i: (0, 0)),
            pl.BlockSpec((rows, rows_l), lambda i: (0, 0)),
            pl.BlockSpec(
                (BLK, rows, cols_l), lambda i: (jnp.minimum(i + eb0, DIGITS - 1), 0, 0)
            ),
            pl.BlockSpec((DIGITS, BLK, rows, cols_l), lambda i: (0, i + eb0, 0, 0)),
        ]
        + half_specs,
        out_specs=pl.BlockSpec((BLK, rows, cols_l), lambda i: (i, 0, 0)),
        out_shape=jax.ShapeDtypeStruct((nblocks * BLK, rows, cols_l), BF16),
        scratch_shapes=[pltpu.VMEM((BLK, rows, cols_l), F32)],
    )(f_own, f_oth, cip, key, *half_args)


def _final_kernel(fo_ref, fr_ref, own_ref, recv_ref, prod_ref, s_ref, out_ref):
    fo = fo_ref[...]
    fr = fr_ref[...]
    n = own_ref.shape[0]
    base = pl.program_id(0) * n
    for l in range(n):
        y = jnp.dot(fo, own_ref[l], preferred_element_type=F32)
        y = (y + jnp.dot(fr, recv_ref[l], preferred_element_type=F32)).astype(BF16)
        diff = prod_ref[l].astype(F32) - y.astype(F32)
        out_ref[l] = (diff * s_ref[base + l]).astype(BF16)


def final(own4, recv4, prod, scale, f_own, f_oth):
    n, rows, cols_l = prod.shape
    rows_l = rows // 2
    hs = pl.BlockSpec((BLK, rows_l, cols_l), lambda i: (i, 0, 0))
    return pl.pallas_call(
        _final_kernel,
        grid=(n // BLK,),
        in_specs=[
            pl.BlockSpec((rows, rows_l), lambda i: (0, 0)),
            pl.BlockSpec((rows, rows_l), lambda i: (0, 0)),
            hs,
            hs,
            pl.BlockSpec((BLK, rows, cols_l), lambda i: (i, 0, 0)),
            SMEM_SPEC,
        ],
        out_specs=pl.BlockSpec((BLK, rows, cols_l), lambda i: (i, 0, 0)),
        out_shape=jax.ShapeDtypeStruct((n, rows, cols_l), BF16),
    )(f_own, f_oth, own4, recv4, prod, scale)


def snake_ring(n):
    if n % 2:
        return list(range(n))
    outer = n // 2
    return [2 * a for a in range(outer)] + [2 * a + 1 for a in reversed(range(outer))]


def ring_setup(shard):
    n = lax.axis_size("limb")
    me_l = lax.axis_index("limb")
    order = snake_ring(n)
    pos = [0] * n
    for i, l in enumerate(order):
        pos[l] = i
    width = shard.shape[1]
    full = jnp.zeros((shard.shape[0], n * width) + shard.shape[2:], shard.dtype)
    full = lax.dynamic_update_slice_in_dim(full, shard, me_l * width, axis=1)
    return dict(
        n=n,
        order=jnp.array(order, I32),
        p=jnp.array(pos, I32)[me_l],
        cw=[(order[i], order[(i + 1) % n]) for i in range(n)],
        ccw=[(order[i], order[(i - 1) % n]) for i in range(n)],
        width=width,
        full=full,
        a=shard,
        b=shard,
        s=0,
    )


def ring_steps(st):
    return st["n"] // 2


def ring_step(st):
    n, width, order, p = st["n"], st["width"], st["order"], st["p"]
    st["s"] += 1
    s = st["s"]
    if 2 * s < n:
        st["a"] = lax.ppermute(st["a"], "limb", st["cw"])
        st["b"] = lax.ppermute(st["b"], "limb", st["ccw"])
        st["full"] = lax.dynamic_update_slice_in_dim(
            st["full"], st["a"], order[(p - s) % n] * width, axis=1
        )
        st["full"] = lax.dynamic_update_slice_in_dim(
            st["full"], st["b"], order[(p + s) % n] * width, axis=1
        )
    else:
        h = st["a"].shape[2] // 2
        a = lax.ppermute(st["a"][:, :, :h], "limb", st["cw"])
        b = lax.ppermute(st["b"][:, :, h:], "limb", st["ccw"])
        src = order[(p + s) % n] * width
        st["full"] = lax.dynamic_update_slice_in_dim(
            st["full"], jnp.concatenate([a, b], axis=2), src, axis=1
        )


def ring_hold(st, x):
    if st["s"] >= ring_steps(st):
        return x
    st["a"], st["b"], x = lax.optimization_barrier((st["a"], st["b"], x))
    ring_step(st)
    return x


def ring_finish(st):
    while st["s"] < ring_steps(st):
        ring_step(st)
    return st["full"]

def swap(x):
    return lax.ppermute(x, "coef", perm=[(0, 1), (1, 0)])


def body(cipher, switch_key, raise_table, lower_table, special_inverse):
    nc = lax.axis_size("coef")
    me = lax.axis_index("coef")
    me_arr = jnp.reshape(me, (1,)).astype(I32)
    other = 1 - me
    _, limbs, rows, cols_l = cipher.shape
    cols = cols_l * nc
    rows_l = rows // nc

    ring = ring_setup(switch_key[0])
    if ring_steps(ring):
        ring_step(ring)

    f_rows = cosine_table(rows)
    f_cols = cosine_table(cols)
    ft_rows = f_rows.T
    ft_cols = f_cols.T
    fc_own = lax.dynamic_slice_in_dim(f_cols, me * cols_l, cols_l, axis=0)
    fc_oth = lax.dynamic_slice_in_dim(f_cols, other * cols_l, cols_l, axis=0)
    fr_own = lax.dynamic_slice_in_dim(f_rows, me * rows_l, rows_l, axis=1)
    fr_oth = lax.dynamic_slice_in_dim(f_rows, other * rows_l, rows_l, axis=1)
    w_col, w_row, v_row = twiddle_tables(me, rows, cols, nc)

    ct = cipher[0]
    own1, send1 = inv_row(me_arr, ct, w_col, ft_rows, 0)
    own1 = ring_hold(ring, own1)
    coeffs = inv_col(own1, swap(send1), v_row, fc_own, fc_oth, 0)

    blocks = coeffs.reshape(DIGITS, DIGIT_LIMBS, rows_l, cols)
    raised = lax.dot_general(
        raise_table, blocks, (((2,), (1,)), ((0,), (0,))), preferred_element_type=F32
    ).astype(BF16)

    raised = ring_hold(ring, raised)
    digit_steps = []
    for eb in range(EXTENDED // BLK):
        for j in range(DIGITS):
            if j != eb:
                digit_steps.append((j, eb if eb < j else eb - 1, eb))
    own2, send2 = fwd_col(me_arr, raised, v_row, w_row, ft_cols, digit_steps)
    own2, send2 = ring_hold(ring, (own2, send2))
    recv2 = swap(send2)
    key = ring_finish(ring)

    prod_special = product(ct, key, own2, recv2, fr_own, fr_oth, DIGITS, 1)
    prod_cipher = product(ct, key, own2, recv2, fr_own, fr_oth, 0, DIGITS)

    own3, send3 = inv_row(me_arr, prod_special, w_col, ft_rows, limbs)
    special = inv_col(own3, swap(send3), v_row, fc_own, fc_oth, limbs)
    lowered = lax.dot_general(
        lower_table, special, (((1,), (0,)), ((), ())), preferred_element_type=F32
    )
    lowered = lowered.astype(BF16)[None]
    own4, send4 = fwd_col(
        me_arr, lowered, v_row, w_row, ft_cols, [(0, t, t) for t in range(limbs // BLK)]
    )
    scale = special_inverse
    result = final(own4[0], swap(send4)[0], prod_cipher, scale, fr_own, fr_oth)
    return result[None, None]


def solution(mesh):
    in_specs = (
        P(("grp", "limb"), None, None, "coef"),
        P(None, None, "limb", None, "coef"),
        P(),
        P(),
        P(),
    )
    out_specs = P(None, ("grp", "limb"), None, None, "coef")
    return jax.shard_map(body, mesh=mesh, in_specs=in_specs, out_specs=out_specs, check_vma=False)
```

```python
import math

import jax
import ml_dtypes
import numpy as np
import jax.numpy as jnp
from jax import lax
from jax.experimental import pallas as pl
from jax.experimental.pallas import tpu as pltpu
from jax.sharding import PartitionSpec as P

LIMBS = 48
DIGITS = 3
DIGIT_LIMBS = 16
EXTENDED = 64
CYCLE = 32768
BLK = 16

F32 = jnp.float32
BF16 = jnp.bfloat16
I32 = jnp.int32


def cosine_table(size):
    freq = np.arange(size, dtype=np.float64)[:, None]
    place = np.arange(size, dtype=np.float64)[None, :]
    norm = np.where(freq == 0, math.sqrt(1.0 / size), math.sqrt(2.0 / size))
    return (norm * np.cos(math.pi * (2.0 * place + 1.0) * freq / (2.0 * size))).astype(
        ml_dtypes.bfloat16
    )


def _angle(phase):
    ang = (2.0 * math.pi / CYCLE) * phase.astype(F32)
    return jnp.cos(ang), jnp.sin(ang)


def _limb_angle(c):
    shape = (-1,) + (1,) * c.ndim
    hi = jnp.arange(EXTENDED // 8, dtype=I32).reshape(shape)
    lo = (2 * jnp.arange(8, dtype=I32) + 1).reshape(shape)
    ch, sh = _angle((16 * hi * c[None]) % CYCLE)
    cl, sl = _angle((lo * c[None]) % CYCLE)
    cos = ch[:, None] * cl[None] - sh[:, None] * sl[None]
    sin = sh[:, None] * cl[None] + ch[:, None] * sl[None]
    return cos.reshape((EXTENDED,) + c.shape), sin.reshape((EXTENDED,) + c.shape)


def _twiddle(p, q):
    cp, sp = _limb_angle(p % CYCLE)
    cq, sq = _limb_angle(q % CYCLE)
    cp, sp, cq, sq = lax.optimization_barrier((cp, sp, cq, sq))
    return 1.0 + 0.5 * (cp * cq - sp * sq)


def twiddle_tables(me, rows, cols, nc):
    rows_l, cols_l = rows // nc, cols // nc
    fine = jnp.arange(8, dtype=I32)[None, :, None]
    coarse = (8 * jnp.arange(rows // 8, dtype=I32))[:, None, None]
    bcol = (me * cols_l + jnp.arange(cols_l, dtype=I32))[None, None, :]
    w_col = _twiddle(coarse * bcol, fine * bcol).reshape(EXTENDED, rows, cols_l)
    coarse = (me * rows_l + 8 * jnp.arange(rows_l // 8, dtype=I32))[:, None, None]
    ball = jnp.arange(cols, dtype=I32)[None, None, :]
    w_row = _twiddle(coarse * ball, fine * ball).reshape(EXTENDED, rows_l, cols)
    v_row = _twiddle(coarse * cols + ball, fine * cols).reshape(EXTENDED, rows_l, cols)
    return w_col, w_row, v_row


SMEM_SPEC = pl.BlockSpec(memory_space=pltpu.SMEM)


def _split_store(me_ref, first, second, own_ref, send_ref):
    top = me_ref[0] == 0

    @pl.when(top)
    def _():
        own_ref[...] = first
        send_ref[...] = second

    @pl.when(jnp.logical_not(top))
    def _():
        own_ref[...] = second
        send_ref[...] = first


def _inv_row_kernel(me_ref, y_ref, w_ref, ft_ref, own_ref, send_ref, h_ref):
    ft = ft_ref[...]
    n, rows, _ = y_ref.shape
    for l in range(n):
        h = jnp.dot(ft, y_ref[l], preferred_element_type=F32)
        h_ref[l] = (h / w_ref[l]).astype(BF16)
    half = rows // 2
    _split_store(me_ref, h_ref[:, :half, :], h_ref[:, half:, :], own_ref, send_ref)


def inv_row(me_arr, y, w_col, ft, e0):
    n, rows, cols_l = y.shape
    eb0 = e0 // BLK
    blk = pl.BlockSpec((BLK, rows, cols_l), lambda i: (i, 0, 0))
    out = pl.BlockSpec((BLK, rows // 2, cols_l), lambda i: (i, 0, 0))
    return pl.pallas_call(
        _inv_row_kernel,
        grid=(n // BLK,),
        in_specs=[
            SMEM_SPEC,
            blk,
            pl.BlockSpec((BLK, rows, cols_l), lambda i: (i + eb0, 0, 0)),
            pl.BlockSpec((rows, rows), lambda i: (0, 0)),
        ],
        out_specs=[out, out],
        out_shape=[jax.ShapeDtypeStruct((n, rows // 2, cols_l), BF16)] * 2,
        scratch_shapes=[pltpu.VMEM((BLK, rows, cols_l), BF16)],
    )(me_arr, y, w_col, ft)


def _inv_col_kernel(own_ref, recv_ref, v_ref, fo_ref, fr_ref, out_ref):
    n, rows_l, half = own_ref.shape
    a = own_ref[...].reshape(n * rows_l, half)
    b = recv_ref[...].reshape(n * rows_l, half)
    x = jnp.dot(a, fo_ref[...], preferred_element_type=F32)
    x = x + jnp.dot(b, fr_ref[...], preferred_element_type=F32)
    x = x.reshape(n, rows_l, -1)
    out_ref[...] = (x / v_ref[...]).astype(BF16)


def inv_col(own, recv, v_row, f_own, f_oth, e0):
    n, rows_l, half = own.shape
    cols = 2 * half
    eb0 = e0 // BLK
    blk = pl.BlockSpec((BLK, rows_l, half), lambda i: (i, 0, 0))
    return pl.pallas_call(
        _inv_col_kernel,
        grid=(n // BLK,),
        in_specs=[
            blk,
            blk,
            pl.BlockSpec((BLK, rows_l, cols), lambda i: (i + eb0, 0, 0)),
            pl.BlockSpec((half, cols), lambda i: (0, 0)),
            pl.BlockSpec((half, cols), lambda i: (0, 0)),
        ],
        out_specs=pl.BlockSpec((BLK, rows_l, cols), lambda i: (i, 0, 0)),
        out_shape=jax.ShapeDtypeStruct((n, rows_l, cols), BF16),
    )(own, recv, v_row, f_own, f_oth)


def _fwd_col_kernel(sj_ref, st_ref, se_ref, me_ref, x_ref, v_ref, w_ref, ft_ref, *rest):
    own_ref, send_ref = rest[-2:]
    n, rows_l, cols = x_ref.shape
    g = (x_ref[...].astype(F32) * v_ref[...]).astype(BF16)
    h = jnp.dot(g.reshape(n * rows_l, cols), ft_ref[...], preferred_element_type=F32)
    h = (h.reshape(n, rows_l, cols) * w_ref[...]).astype(BF16)
    half = cols // 2
    _split_store(me_ref, h[:, :, :half], h[:, :, half:], own_ref, send_ref)


def fwd_col(me_arr, x, v_row, w_row, ft, steps, into=None):
    groups, n, rows_l, cols = x.shape
    half = cols // 2
    sj, st, se = (jnp.array([step[k] for step in steps], I32) for k in range(3))
    xs = pl.BlockSpec((None, BLK, rows_l, cols), lambda i, a, b, c: (a[i], b[i], 0, 0))
    ts = pl.BlockSpec((BLK, rows_l, cols), lambda i, a, b, c: (c[i], 0, 0))
    os = pl.BlockSpec((None, BLK, rows_l, half), lambda i, a, b, c: (a[i], b[i], 0, 0))
    grid_spec = pltpu.PrefetchScalarGridSpec(
        num_scalar_prefetch=3,
        grid=(len(steps),),
        in_specs=[
            SMEM_SPEC,
            xs,
            ts,
            ts,
            pl.BlockSpec((cols, cols), lambda i, a, b, c: (0, 0)),
        ]
        + ([pl.BlockSpec(memory_space=pl.ANY)] * 2 if into else []),
        out_specs=[os, os],
    )
    return pl.pallas_call(
        _fwd_col_kernel,
        grid_spec=grid_spec,
        out_shape=[jax.ShapeDtypeStruct((groups, n, rows_l, half), BF16)] * 2,
        input_output_aliases={8: 0, 9: 1} if into else {},
        cost_estimate=pl.CostEstimate(
            flops=2 * len(steps) * BLK * rows_l * cols * cols,
            transcendentals=0,
            bytes_accessed=len(steps) * BLK * rows_l * cols * 12,
        ),
    )(sj, st, se, me_arr, x, v_row, w_row, ft, *(into or ()))


def _product_kernel(eb0, fo_ref, fr_ref, cip_ref, key_ref, *rest):
    halves = rest[: 2 * DIGITS]
    out_ref, acc_ref = rest[2 * DIGITS :]
    eb = pl.program_id(0) + eb0
    f = jnp.concatenate([fo_ref[...], fr_ref[...]], axis=1)
    acc_ref[...] = jnp.zeros_like(acc_ref)
    n = acc_ref.shape[0]
    for j in range(DIGITS):
        own_ref, recv_ref = halves[2 * j], halves[2 * j + 1]

        @pl.when(eb == j)
        def _():
            acc_ref[...] += cip_ref[...].astype(F32) * key_ref[j].astype(F32)

        @pl.when(eb != j)
        def _():
            for l in range(n):
                h = jnp.concatenate([own_ref[l], recv_ref[l]], axis=0)
                y = jnp.dot(f, h, preferred_element_type=F32).astype(BF16)
                acc_ref[l] += y.astype(F32) * key_ref[j, l].astype(F32)

    out_ref[...] = acc_ref[...].astype(BF16)


def product(cip, key, own2, recv2, f_own, f_oth, eb0, nblocks):
    _, rows, cols_l = cip.shape
    rows_l = rows // 2

    def lifted_block(j):
        def index(i):
            eb = i + eb0
            tb = jnp.where(eb < j, eb, eb - 1)
            return (j, jnp.clip(tb, 0, DIGITS - 1), 0, 0)

        return pl.BlockSpec((None, BLK, rows_l, cols_l), index)

    half_specs = []
    half_args = []
    for j in range(DIGITS):
        half_specs += [lifted_block(j), lifted_block(j)]
        half_args += [own2, recv2]
    return pl.pallas_call(
        lambda *refs: _product_kernel(eb0, *refs),
        grid=(nblocks,),
        in_specs=[
            pl.BlockSpec((rows, rows_l), lambda i: (0, 0)),
            pl.BlockSpec((rows, rows_l), lambda i: (0, 0)),
            pl.BlockSpec(
                (BLK, rows, cols_l), lambda i: (jnp.minimum(i + eb0, DIGITS - 1), 0, 0)
            ),
            pl.BlockSpec((DIGITS, BLK, rows, cols_l), lambda i: (0, i + eb0, 0, 0)),
        ]
        + half_specs,
        out_specs=pl.BlockSpec((BLK, rows, cols_l), lambda i: (i, 0, 0)),
        out_shape=jax.ShapeDtypeStruct((nblocks * BLK, rows, cols_l), BF16),
        scratch_shapes=[pltpu.VMEM((BLK, rows, cols_l), F32)],
    )(f_own, f_oth, cip, key, *half_args)


def _final_kernel(fo_ref, fr_ref, own_ref, recv_ref, prod_ref, s_ref, out_ref):
    f = jnp.concatenate([fo_ref[...], fr_ref[...]], axis=1)
    n = own_ref.shape[0]
    base = pl.program_id(0) * n
    for l in range(n):
        h = jnp.concatenate([own_ref[l], recv_ref[l]], axis=0)
        y = jnp.dot(f, h, preferred_element_type=F32).astype(BF16)
        diff = prod_ref[l].astype(F32) - y.astype(F32)
        out_ref[l] = (diff * s_ref[base + l]).astype(BF16)


def final(own4, recv4, prod, scale, f_own, f_oth):
    n, rows, cols_l = prod.shape
    rows_l = rows // 2
    hs = pl.BlockSpec((BLK, rows_l, cols_l), lambda i: (i, 0, 0))
    return pl.pallas_call(
        _final_kernel,
        grid=(n // BLK,),
        in_specs=[
            pl.BlockSpec((rows, rows_l), lambda i: (0, 0)),
            pl.BlockSpec((rows, rows_l), lambda i: (0, 0)),
            hs,
            hs,
            pl.BlockSpec((BLK, rows, cols_l), lambda i: (i, 0, 0)),
            SMEM_SPEC,
        ],
        out_specs=pl.BlockSpec((BLK, rows, cols_l), lambda i: (i, 0, 0)),
        out_shape=jax.ShapeDtypeStruct((n, rows, cols_l), BF16),
    )(f_own, f_oth, own4, recv4, prod, scale)


def snake_ring(n):
    if n % 2:
        return list(range(n))
    outer = n // 2
    return [2 * a for a in range(outer)] + [2 * a + 1 for a in reversed(range(outer))]


def ring_setup(shard):
    n = lax.axis_size("limb")
    me_l = lax.axis_index("limb")
    order = snake_ring(n)
    pos = [0] * n
    for i, l in enumerate(order):
        pos[l] = i
    width = shard.shape[1]
    full = jnp.zeros((shard.shape[0], n * width) + shard.shape[2:], shard.dtype)
    full = lax.dynamic_update_slice_in_dim(full, shard, me_l * width, axis=1)
    return dict(
        n=n,
        order=jnp.array(order, I32),
        p=jnp.array(pos, I32)[me_l],
        cw=[(order[i], order[(i + 1) % n]) for i in range(n)],
        ccw=[(order[i], order[(i - 1) % n]) for i in range(n)],
        width=width,
        full=full,
        a=shard,
        b=shard,
        s=0,
    )


def ring_steps(st):
    return st["n"] // 2


def ring_step(st):
    n, width, order, p = st["n"], st["width"], st["order"], st["p"]
    st["s"] += 1
    s = st["s"]
    if 2 * s < n:
        st["a"] = lax.ppermute(st["a"], "limb", st["cw"])
        st["b"] = lax.ppermute(st["b"], "limb", st["ccw"])
        st["full"] = lax.dynamic_update_slice_in_dim(
            st["full"], st["a"], order[(p - s) % n] * width, axis=1
        )
        st["full"] = lax.dynamic_update_slice_in_dim(
            st["full"], st["b"], order[(p + s) % n] * width, axis=1
        )
    else:
        if st.get("halved"):
            a = lax.ppermute(st["a"], "limb", st["cw"])
            b = lax.ppermute(st["b"], "limb", st["ccw"])
        else:
            h = st["a"].shape[2] // 2
            a = lax.ppermute(st["a"][:, :, :h], "limb", st["cw"])
            b = lax.ppermute(st["b"][:, :, h:], "limb", st["ccw"])
        src = order[(p + s) % n] * width
        st["full"] = lax.dynamic_update_slice_in_dim(
            st["full"], jnp.concatenate([a, b], axis=2), src, axis=1
        )


def ring_hold(st, x):
    if st["s"] >= ring_steps(st):
        return x
    if 2 * (st["s"] + 1) >= st["n"]:
        h = st["a"].shape[2] // 2
        st["a"], st["b"] = st["a"][:, :, :h], st["b"][:, :, h:]
        st["halved"] = True
    st["a"], st["b"], st["full"], x = lax.optimization_barrier((st["a"], st["b"], st["full"], x))
    ring_step(st)
    return x


def ring_finish(st):
    while st["s"] < ring_steps(st):
        ring_step(st)
    return st["full"]

def swap(x):
    return lax.ppermute(x, "coef", perm=[(0, 1), (1, 0)])


def body(cipher, switch_key, raise_table, lower_table, special_inverse):
    nc = lax.axis_size("coef")
    me = lax.axis_index("coef")
    me_arr = jnp.reshape(me, (1,)).astype(I32)
    other = 1 - me
    _, limbs, rows, cols_l = cipher.shape
    cols = cols_l * nc
    rows_l = rows // nc

    ring = ring_setup(switch_key[0])
    if ring_steps(ring):
        ring_step(ring)

    f_rows = cosine_table(rows)
    f_cols = cosine_table(cols)
    ft_rows = f_rows.T
    ft_cols = f_cols.T
    fc_own = lax.dynamic_slice_in_dim(f_cols, me * cols_l, cols_l, axis=0)
    fc_oth = lax.dynamic_slice_in_dim(f_cols, other * cols_l, cols_l, axis=0)
    fr_own = lax.dynamic_slice_in_dim(f_rows, me * rows_l, rows_l, axis=1)
    fr_oth = lax.dynamic_slice_in_dim(f_rows, other * rows_l, rows_l, axis=1)
    w_col, w_row, v_row = twiddle_tables(me, rows, cols, nc)

    ct = cipher[0]
    own1, send1 = inv_row(me_arr, ct, w_col, ft_rows, 0)
    own1 = ring_hold(ring, own1)
    coeffs = inv_col(own1, swap(send1), v_row, fc_own, fc_oth, 0)

    blocks = coeffs.reshape(DIGITS, DIGIT_LIMBS, rows_l, cols)
    raised = lax.dot_general(
        raise_table, blocks, (((2,), (1,)), ((0,), (0,))), preferred_element_type=F32
    ).astype(BF16)

    raised = ring_hold(ring, raised)
    digit_steps = []
    for eb in range(EXTENDED // BLK):
        for j in range(DIGITS):
            if j != eb:
                digit_steps.append((j, eb if eb < j else eb - 1, eb))
    cut = len(digit_steps) // 2
    first = fwd_col(me_arr, raised, v_row, w_row, ft_cols, digit_steps[:cut])
    first = ring_hold(ring, first)
    own2, send2 = fwd_col(me_arr, raised, v_row, w_row, ft_cols, digit_steps[cut:], first)
    recv2 = swap(send2)
    key = ring_finish(ring)

    prod_special = product(ct, key, own2, recv2, fr_own, fr_oth, DIGITS, 1)
    prod_cipher = product(ct, key, own2, recv2, fr_own, fr_oth, 0, DIGITS)

    own3, send3 = inv_row(me_arr, prod_special, w_col, ft_rows, limbs)
    special = inv_col(own3, swap(send3), v_row, fc_own, fc_oth, limbs)
    lowered = lax.dot_general(
        lower_table, special, (((1,), (0,)), ((), ())), preferred_element_type=F32
    )
    lowered = lowered.astype(BF16)[None]
    own4, send4 = fwd_col(
        me_arr, lowered, v_row, w_row, ft_cols, [(0, t, t) for t in range(limbs // BLK)]
    )
    scale = special_inverse
    result = final(own4[0], swap(send4)[0], prod_cipher, scale, fr_own, fr_oth)
    return result[None, None]


def solution(mesh):
    in_specs = (
        P(("grp", "limb"), None, None, "coef"),
        P(None, None, "limb", None, "coef"),
        P(),
        P(),
        P(),
    )
    out_specs = P(None, ("grp", "limb"), None, None, "coef")
    return jax.shard_map(body, mesh=mesh, in_specs=in_specs, out_specs=out_specs, check_vma=False)
```

```python
import math

import jax
import ml_dtypes
import numpy as np
import jax.numpy as jnp
from jax import lax
from jax.experimental import pallas as pl
from jax.experimental.pallas import tpu as pltpu
from jax.sharding import PartitionSpec as P

LIMBS = 48
DIGITS = 3
DIGIT_LIMBS = 16
EXTENDED = 64
CYCLE = 32768
BLK = 16

F32 = jnp.float32
BF16 = jnp.bfloat16
I32 = jnp.int32


def cosine_table(size):
    freq = np.arange(size, dtype=np.float64)[:, None]
    place = np.arange(size, dtype=np.float64)[None, :]
    norm = np.where(freq == 0, math.sqrt(1.0 / size), math.sqrt(2.0 / size))
    return (norm * np.cos(math.pi * (2.0 * place + 1.0) * freq / (2.0 * size))).astype(
        ml_dtypes.bfloat16
    )


def _angle(phase):
    ang = (2.0 * math.pi / CYCLE) * phase.astype(F32)
    return jnp.cos(ang), jnp.sin(ang)


def _limb_angle(c):
    shape = (-1,) + (1,) * c.ndim
    hi = jnp.arange(EXTENDED // 8, dtype=I32).reshape(shape)
    lo = (2 * jnp.arange(8, dtype=I32) + 1).reshape(shape)
    ch, sh = _angle((16 * hi * c[None]) % CYCLE)
    cl, sl = _angle((lo * c[None]) % CYCLE)
    cos = ch[:, None] * cl[None] - sh[:, None] * sl[None]
    sin = sh[:, None] * cl[None] + ch[:, None] * sl[None]
    return cos.reshape((EXTENDED,) + c.shape), sin.reshape((EXTENDED,) + c.shape)


def _twiddle(p, q):
    cp, sp = _limb_angle(p % CYCLE)
    cq, sq = _limb_angle(q % CYCLE)
    cp, sp, cq, sq = lax.optimization_barrier((cp, sp, cq, sq))
    return 1.0 + 0.5 * (cp * cq - sp * sq)


def twiddle_tables(me, rows, cols, nc):
    rows_l, cols_l = rows // nc, cols // nc
    fine = jnp.arange(8, dtype=I32)[None, :, None]
    coarse = (8 * jnp.arange(rows // 8, dtype=I32))[:, None, None]
    bcol = (me * cols_l + jnp.arange(cols_l, dtype=I32))[None, None, :]
    w_col = _twiddle(coarse * bcol, fine * bcol).reshape(EXTENDED, rows, cols_l)
    coarse = (me * rows_l + 8 * jnp.arange(rows_l // 8, dtype=I32))[:, None, None]
    ball = jnp.arange(cols, dtype=I32)[None, None, :]
    w_row = _twiddle(coarse * ball, fine * ball).reshape(EXTENDED, rows_l, cols)
    v_row = _twiddle(coarse * cols + ball, fine * cols).reshape(EXTENDED, rows_l, cols)
    return w_col, w_row, v_row


SMEM_SPEC = pl.BlockSpec(memory_space=pltpu.SMEM)


def _split_store(me_ref, first, second, own_ref, send_ref):
    top = me_ref[0] == 0

    @pl.when(top)
    def _():
        own_ref[...] = first
        send_ref[...] = second

    @pl.when(jnp.logical_not(top))
    def _():
        own_ref[...] = second
        send_ref[...] = first


def _inv_row_kernel(me_ref, y_ref, w_ref, ft_ref, own_ref, send_ref, h_ref):
    ft = ft_ref[...]
    n, rows, _ = y_ref.shape
    for l in range(n):
        h = jnp.dot(ft, y_ref[l], preferred_element_type=F32)
        h_ref[l] = (h / w_ref[l]).astype(BF16)
    half = rows // 2
    _split_store(me_ref, h_ref[:, :half, :], h_ref[:, half:, :], own_ref, send_ref)


def inv_row(me_arr, y, w_col, ft, e0):
    n, rows, cols_l = y.shape
    eb0 = e0 // BLK
    blk = pl.BlockSpec((BLK, rows, cols_l), lambda i: (i, 0, 0))
    out = pl.BlockSpec((BLK, rows // 2, cols_l), lambda i: (i, 0, 0))
    return pl.pallas_call(
        _inv_row_kernel,
        grid=(n // BLK,),
        in_specs=[
            SMEM_SPEC,
            blk,
            pl.BlockSpec((BLK, rows, cols_l), lambda i: (i + eb0, 0, 0)),
            pl.BlockSpec((rows, rows), lambda i: (0, 0)),
        ],
        out_specs=[out, out],
        out_shape=[jax.ShapeDtypeStruct((n, rows // 2, cols_l), BF16)] * 2,
        scratch_shapes=[pltpu.VMEM((BLK, rows, cols_l), BF16)],
    )(me_arr, y, w_col, ft)


def _inv_col_kernel(own_ref, recv_ref, v_ref, fo_ref, fr_ref, out_ref):
    n, rows_l, half = own_ref.shape
    a = own_ref[...].reshape(n * rows_l, half)
    b = recv_ref[...].reshape(n * rows_l, half)
    x = jnp.dot(a, fo_ref[...], preferred_element_type=F32)
    x = x + jnp.dot(b, fr_ref[...], preferred_element_type=F32)
    x = x.reshape(n, rows_l, -1)
    out_ref[...] = (x / v_ref[...]).astype(BF16)


def inv_col(own, recv, v_row, f_own, f_oth, e0):
    n, rows_l, half = own.shape
    cols = 2 * half
    eb0 = e0 // BLK
    blk = pl.BlockSpec((BLK, rows_l, half), lambda i: (i, 0, 0))
    return pl.pallas_call(
        _inv_col_kernel,
        grid=(n // BLK,),
        in_specs=[
            blk,
            blk,
            pl.BlockSpec((BLK, rows_l, cols), lambda i: (i + eb0, 0, 0)),
            pl.BlockSpec((half, cols), lambda i: (0, 0)),
            pl.BlockSpec((half, cols), lambda i: (0, 0)),
        ],
        out_specs=pl.BlockSpec((BLK, rows_l, cols), lambda i: (i, 0, 0)),
        out_shape=jax.ShapeDtypeStruct((n, rows_l, cols), BF16),
    )(own, recv, v_row, f_own, f_oth)


def _fwd_col_kernel(me_ref, x_ref, v_ref, w_ref, ft_ref, own_ref, send_ref):
    n, rows_l, cols = x_ref.shape
    g = (x_ref[...].astype(F32) * v_ref[...]).astype(BF16)
    h = jnp.dot(g.reshape(n * rows_l, cols), ft_ref[...], preferred_element_type=F32)
    h = (h.reshape(n, rows_l, cols) * w_ref[...]).astype(BF16)
    half = cols // 2
    _split_store(me_ref, h[:, :, :half], h[:, :, half:], own_ref, send_ref)


def fwd_col(me_arr, x, v_row, w_row, ft, table_block):
    groups, n, rows_l, cols = x.shape
    half = cols // 2
    xs = pl.BlockSpec((None, BLK, rows_l, cols), lambda j, t: (j, t, 0, 0))
    ts = pl.BlockSpec((BLK, rows_l, cols), lambda j, t: (table_block(j, t), 0, 0))
    os = pl.BlockSpec((None, BLK, rows_l, half), lambda j, t: (j, t, 0, 0))
    return pl.pallas_call(
        _fwd_col_kernel,
        grid=(groups, n // BLK),
        in_specs=[SMEM_SPEC, xs, ts, ts, pl.BlockSpec((cols, cols), lambda j, t: (0, 0))],
        out_specs=[os, os],
        out_shape=[jax.ShapeDtypeStruct((groups, n, rows_l, half), BF16)] * 2,
    )(me_arr, x, v_row, w_row, ft)


def _product_kernel(eb0, fo_ref, fr_ref, cip_ref, key_ref, *rest):
    halves = rest[: 2 * DIGITS]
    out_ref, acc_ref = rest[2 * DIGITS :]
    eb = pl.program_id(0) + eb0
    f = jnp.concatenate([fo_ref[...], fr_ref[...]], axis=1)
    acc_ref[...] = jnp.zeros_like(acc_ref)
    n = acc_ref.shape[0]
    for j in range(DIGITS):
        own_ref, recv_ref = halves[2 * j], halves[2 * j + 1]

        @pl.when(eb == j)
        def _():
            acc_ref[...] += cip_ref[...].astype(F32) * key_ref[j].astype(F32)

        @pl.when(eb != j)
        def _():
            for l in range(n):
                h = jnp.concatenate([own_ref[l], recv_ref[l]], axis=0)
                y = jnp.dot(f, h, preferred_element_type=F32).astype(BF16)
                acc_ref[l] += y.astype(F32) * key_ref[j, l].astype(F32)

    out_ref[...] = acc_ref[...].astype(BF16)


def product(cip, key, own2, recv2, f_own, f_oth, eb0, nblocks):
    _, rows, cols_l = cip.shape
    rows_l = rows // 2

    def lifted_block(j):
        def index(i):
            eb = i + eb0
            tb = jnp.where(eb < j, eb, eb - 1)
            return (j, jnp.clip(tb, 0, DIGITS - 1), 0, 0)

        return pl.BlockSpec((None, BLK, rows_l, cols_l), index)

    half_specs = []
    half_args = []
    for j in range(DIGITS):
        half_specs += [lifted_block(j), lifted_block(j)]
        half_args += [own2, recv2]
    return pl.pallas_call(
        lambda *refs: _product_kernel(eb0, *refs),
        grid=(nblocks,),
        in_specs=[
            pl.BlockSpec((rows, rows_l), lambda i: (0, 0)),
            pl.BlockSpec((rows, rows_l), lambda i: (0, 0)),
            pl.BlockSpec(
                (BLK, rows, cols_l), lambda i: (jnp.minimum(i + eb0, DIGITS - 1), 0, 0)
            ),
            pl.BlockSpec((DIGITS, BLK, rows, cols_l), lambda i: (0, i + eb0, 0, 0)),
        ]
        + half_specs,
        out_specs=pl.BlockSpec((BLK, rows, cols_l), lambda i: (i, 0, 0)),
        out_shape=jax.ShapeDtypeStruct((nblocks * BLK, rows, cols_l), BF16),
        scratch_shapes=[pltpu.VMEM((BLK, rows, cols_l), F32)],
    )(f_own, f_oth, cip, key, *half_args)


def _final_kernel(fo_ref, fr_ref, own_ref, recv_ref, prod_ref, s_ref, out_ref):
    f = jnp.concatenate([fo_ref[...], fr_ref[...]], axis=1)
    for l in range(own_ref.shape[0]):
        h = jnp.concatenate([own_ref[l], recv_ref[l]], axis=0)
        y = jnp.dot(f, h, preferred_element_type=F32).astype(BF16)
        diff = prod_ref[l].astype(F32) - y.astype(F32)
        out_ref[l] = (diff * s_ref[l]).astype(BF16)


def final(own4, recv4, prod, scale, f_own, f_oth):
    n, rows, cols_l = prod.shape
    rows_l = rows // 2
    hs = pl.BlockSpec((BLK, rows_l, cols_l), lambda i: (i, 0, 0))
    return pl.pallas_call(
        _final_kernel,
        grid=(n // BLK,),
        in_specs=[
            pl.BlockSpec((rows, rows_l), lambda i: (0, 0)),
            pl.BlockSpec((rows, rows_l), lambda i: (0, 0)),
            hs,
            hs,
            pl.BlockSpec((BLK, rows, cols_l), lambda i: (i, 0, 0)),
            pl.BlockSpec((BLK, 1, cols_l), lambda i: (i, 0, 0)),
        ],
        out_specs=pl.BlockSpec((BLK, rows, cols_l), lambda i: (i, 0, 0)),
        out_shape=jax.ShapeDtypeStruct((n, rows, cols_l), BF16),
    )(f_own, f_oth, own4, recv4, prod, scale)


def snake_ring(n):
    if n % 2:
        return list(range(n))
    outer = n // 2
    return [2 * a for a in range(outer)] + [2 * a + 1 for a in reversed(range(outer))]


def ring_setup(shard):
    n = lax.axis_size("limb")
    me_l = lax.axis_index("limb")
    order = snake_ring(n)
    pos = [0] * n
    for i, l in enumerate(order):
        pos[l] = i
    width = shard.shape[1]
    full = jnp.zeros((shard.shape[0], n * width) + shard.shape[2:], shard.dtype)
    full = lax.dynamic_update_slice_in_dim(full, shard, me_l * width, axis=1)
    return dict(
        n=n,
        order=jnp.array(order, I32),
        p=jnp.array(pos, I32)[me_l],
        cw=[(order[i], order[(i + 1) % n]) for i in range(n)],
        ccw=[(order[i], order[(i - 1) % n]) for i in range(n)],
        width=width,
        full=full,
        a=shard,
        b=shard,
        s=0,
    )


def ring_steps(st):
    return st["n"] // 2


def ring_step(st):
    n, width, order, p = st["n"], st["width"], st["order"], st["p"]
    st["s"] += 1
    s = st["s"]
    if 2 * s < n:
        st["a"] = lax.ppermute(st["a"], "limb", st["cw"])
        st["b"] = lax.ppermute(st["b"], "limb", st["ccw"])
        st["full"] = lax.dynamic_update_slice_in_dim(
            st["full"], st["a"], order[(p - s) % n] * width, axis=1
        )
        st["full"] = lax.dynamic_update_slice_in_dim(
            st["full"], st["b"], order[(p + s) % n] * width, axis=1
        )
    else:
        h = st["a"].shape[2] // 2
        a = lax.ppermute(st["a"][:, :, :h], "limb", st["cw"])
        b = lax.ppermute(st["b"][:, :, h:], "limb", st["ccw"])
        src = order[(p + s) % n] * width
        st["full"] = lax.dynamic_update_slice_in_dim(
            st["full"], jnp.concatenate([a, b], axis=2), src, axis=1
        )


def ring_hold(st, x):
    if st["s"] >= ring_steps(st):
        return x
    st["a"], st["b"], x = lax.optimization_barrier((st["a"], st["b"], x))
    ring_step(st)
    return x


def ring_finish(st):
    while st["s"] < ring_steps(st):
        ring_step(st)
    return st["full"]

def swap(x):
    return lax.ppermute(x, "coef", perm=[(0, 1), (1, 0)])


def body(cipher, switch_key, raise_table, lower_table, special_inverse):
    nc = lax.axis_size("coef")
    me = lax.axis_index("coef")
    me_arr = jnp.reshape(me, (1,)).astype(I32)
    other = 1 - me
    _, limbs, rows, cols_l = cipher.shape
    cols = cols_l * nc
    rows_l = rows // nc

    ring = ring_setup(switch_key[0])
    if ring_steps(ring):
        ring_step(ring)

    f_rows = cosine_table(rows)
    f_cols = cosine_table(cols)
    ft_rows = f_rows.T
    ft_cols = f_cols.T
    fc_own = lax.dynamic_slice_in_dim(f_cols, me * cols_l, cols_l, axis=0)
    fc_oth = lax.dynamic_slice_in_dim(f_cols, other * cols_l, cols_l, axis=0)
    fr_own = lax.dynamic_slice_in_dim(f_rows, me * rows_l, rows_l, axis=1)
    fr_oth = lax.dynamic_slice_in_dim(f_rows, other * rows_l, rows_l, axis=1)
    w_col, w_row, v_row = twiddle_tables(me, rows, cols, nc)

    ct = cipher[0]
    own1, send1 = inv_row(me_arr, ct, w_col, ft_rows, 0)
    own1 = ring_hold(ring, own1)
    coeffs = inv_col(own1, swap(send1), v_row, fc_own, fc_oth, 0)

    blocks = coeffs.reshape(DIGITS, DIGIT_LIMBS, rows_l, cols)
    raised = lax.dot_general(
        raise_table, blocks, (((2,), (1,)), ((0,), (0,))), preferred_element_type=F32
    ).astype(BF16)

    raised = ring_hold(ring, raised)
    own2, send2 = fwd_col(
        me_arr, raised, v_row, w_row, ft_cols, lambda j, t: jnp.where(t >= j, t + 1, t)
    )
    own2, send2 = ring_hold(ring, (own2, send2))
    recv2 = swap(send2)
    key = ring_finish(ring)

    prod_special = product(ct, key, own2, recv2, fr_own, fr_oth, DIGITS, 1)
    prod_cipher = product(ct, key, own2, recv2, fr_own, fr_oth, 0, DIGITS)

    own3, send3 = inv_row(me_arr, prod_special, w_col, ft_rows, limbs)
    special = inv_col(own3, swap(send3), v_row, fc_own, fc_oth, limbs)
    lowered = lax.dot_general(
        lower_table, special, (((1,), (0,)), ((), ())), preferred_element_type=F32
    )
    lowered = lowered.astype(BF16)[None]
    own4, send4 = fwd_col(me_arr, lowered, v_row, w_row, ft_cols, lambda j, t: t)
    scale = jnp.broadcast_to(special_inverse[:, None, None], (limbs, 1, cols_l))
    result = final(own4[0], swap(send4)[0], prod_cipher, scale, fr_own, fr_oth)
    return result[None, None]


def solution(mesh):
    in_specs = (
        P(("grp", "limb"), None, None, "coef"),
        P(None, None, "limb", None, "coef"),
        P(),
        P(),
        P(),
    )
    out_specs = P(None, ("grp", "limb"), None, None, "coef")
    return jax.shard_map(body, mesh=mesh, in_specs=in_specs, out_specs=out_specs, check_vma=False)
```

```python
import math

import jax
import ml_dtypes
import numpy as np
import jax.numpy as jnp
from jax import lax
from jax.experimental import pallas as pl
from jax.experimental.pallas import tpu as pltpu
from jax.sharding import PartitionSpec as P

LIMBS = 48
DIGITS = 3
DIGIT_LIMBS = 16
EXTENDED = 64
CYCLE = 32768
BLK = 16

F32 = jnp.float32
BF16 = jnp.bfloat16
I32 = jnp.int32


def cosine_table(size):
    freq = np.arange(size, dtype=np.float64)[:, None]
    place = np.arange(size, dtype=np.float64)[None, :]
    norm = np.where(freq == 0, math.sqrt(1.0 / size), math.sqrt(2.0 / size))
    return (norm * np.cos(math.pi * (2.0 * place + 1.0) * freq / (2.0 * size))).astype(
        ml_dtypes.bfloat16
    )


def _angle(phase):
    ang = (2.0 * math.pi / CYCLE) * phase.astype(F32)
    return jnp.cos(ang), jnp.sin(ang)


def _limb_angle(c):
    shape = (-1,) + (1,) * c.ndim
    hi = jnp.arange(EXTENDED // 8, dtype=I32).reshape(shape)
    lo = (2 * jnp.arange(8, dtype=I32) + 1).reshape(shape)
    ch, sh = _angle((16 * hi * c[None]) % CYCLE)
    cl, sl = _angle((lo * c[None]) % CYCLE)
    cos = ch[:, None] * cl[None] - sh[:, None] * sl[None]
    sin = sh[:, None] * cl[None] + ch[:, None] * sl[None]
    return cos.reshape((EXTENDED,) + c.shape), sin.reshape((EXTENDED,) + c.shape)


def _twiddle(p, q):
    cp, sp = _limb_angle(p % CYCLE)
    cq, sq = _limb_angle(q % CYCLE)
    cp, sp, cq, sq = lax.optimization_barrier((cp, sp, cq, sq))
    return 1.0 + 0.5 * (cp * cq - sp * sq)


def twiddle_tables(me, rows, cols, nc):
    rows_l, cols_l = rows // nc, cols // nc
    fine = jnp.arange(8, dtype=I32)[None, :, None]
    coarse = (8 * jnp.arange(rows // 8, dtype=I32))[:, None, None]
    bcol = (me * cols_l + jnp.arange(cols_l, dtype=I32))[None, None, :]
    w_col = _twiddle(coarse * bcol, fine * bcol).reshape(EXTENDED, rows, cols_l)
    coarse = (me * rows_l + 8 * jnp.arange(rows_l // 8, dtype=I32))[:, None, None]
    ball = jnp.arange(cols, dtype=I32)[None, None, :]
    w_row = _twiddle(coarse * ball, fine * ball).reshape(EXTENDED, rows_l, cols)
    v_row = _twiddle(coarse * cols + ball, fine * cols).reshape(EXTENDED, rows_l, cols)
    return w_col, w_row, v_row


SMEM_SPEC = pl.BlockSpec(memory_space=pltpu.SMEM)


def _split_store(me_ref, first, second, own_ref, send_ref):
    top = me_ref[0] == 0

    @pl.when(top)
    def _():
        own_ref[...] = first
        send_ref[...] = second

    @pl.when(jnp.logical_not(top))
    def _():
        own_ref[...] = second
        send_ref[...] = first


def _inv_row_kernel(me_ref, y_ref, w_ref, ft_ref, own_ref, send_ref, h_ref):
    ft = ft_ref[...]
    n, rows, _ = y_ref.shape
    for l in range(n):
        h = jnp.dot(ft, y_ref[l], preferred_element_type=F32)
        h_ref[l] = (h / w_ref[l]).astype(BF16)
    half = rows // 2
    _split_store(me_ref, h_ref[:, :half, :], h_ref[:, half:, :], own_ref, send_ref)


def inv_row(me_arr, y, w_col, ft, e0):
    n, rows, cols_l = y.shape
    eb0 = e0 // BLK
    blk = pl.BlockSpec((BLK, rows, cols_l), lambda i: (i, 0, 0))
    out = pl.BlockSpec((BLK, rows // 2, cols_l), lambda i: (i, 0, 0))
    return pl.pallas_call(
        _inv_row_kernel,
        grid=(n // BLK,),
        in_specs=[
            SMEM_SPEC,
            blk,
            pl.BlockSpec((BLK, rows, cols_l), lambda i: (i + eb0, 0, 0)),
            pl.BlockSpec((rows, rows), lambda i: (0, 0)),
        ],
        out_specs=[out, out],
        out_shape=[jax.ShapeDtypeStruct((n, rows // 2, cols_l), BF16)] * 2,
        scratch_shapes=[pltpu.VMEM((BLK, rows, cols_l), BF16)],
    )(me_arr, y, w_col, ft)


def _inv_col_kernel(own_ref, recv_ref, v_ref, fo_ref, fr_ref, out_ref):
    n, rows_l, half = own_ref.shape
    a = own_ref[...].reshape(n * rows_l, half)
    b = recv_ref[...].reshape(n * rows_l, half)
    f = jnp.concatenate([fo_ref[...], fr_ref[...]], axis=0)
    x = jnp.dot(jnp.concatenate([a, b], axis=1), f, preferred_element_type=F32)
    x = x.reshape(n, rows_l, -1)
    out_ref[...] = (x / v_ref[...]).astype(BF16)


def inv_col(own, recv, v_row, f_own, f_oth, e0):
    n, rows_l, half = own.shape
    cols = 2 * half
    eb0 = e0 // BLK
    blk = pl.BlockSpec((BLK, rows_l, half), lambda i: (i, 0, 0))
    return pl.pallas_call(
        _inv_col_kernel,
        grid=(n // BLK,),
        in_specs=[
            blk,
            blk,
            pl.BlockSpec((BLK, rows_l, cols), lambda i: (i + eb0, 0, 0)),
            pl.BlockSpec((half, cols), lambda i: (0, 0)),
            pl.BlockSpec((half, cols), lambda i: (0, 0)),
        ],
        out_specs=pl.BlockSpec((BLK, rows_l, cols), lambda i: (i, 0, 0)),
        out_shape=jax.ShapeDtypeStruct((n, rows_l, cols), BF16),
    )(own, recv, v_row, f_own, f_oth)


def _fwd_col_kernel(me_ref, x_ref, v_ref, w_ref, ft_ref, own_ref, send_ref):
    n, rows_l, cols = x_ref.shape
    g = (x_ref[...].astype(F32) * v_ref[...]).astype(BF16)
    h = jnp.dot(g.reshape(n * rows_l, cols), ft_ref[...], preferred_element_type=F32)
    h = (h.reshape(n, rows_l, cols) * w_ref[...]).astype(BF16)
    half = cols // 2
    _split_store(me_ref, h[:, :, :half], h[:, :, half:], own_ref, send_ref)


def fwd_col(me_arr, x, v_row, w_row, ft, table_block):
    groups, n, rows_l, cols = x.shape
    half = cols // 2
    xs = pl.BlockSpec((None, BLK, rows_l, cols), lambda j, t: (j, t, 0, 0))
    ts = pl.BlockSpec((BLK, rows_l, cols), lambda j, t: (table_block(j, t), 0, 0))
    os = pl.BlockSpec((None, BLK, rows_l, half), lambda j, t: (j, t, 0, 0))
    return pl.pallas_call(
        _fwd_col_kernel,
        grid=(groups, n // BLK),
        in_specs=[SMEM_SPEC, xs, ts, ts, pl.BlockSpec((cols, cols), lambda j, t: (0, 0))],
        out_specs=[os, os],
        out_shape=[jax.ShapeDtypeStruct((groups, n, rows_l, half), BF16)] * 2,
    )(me_arr, x, v_row, w_row, ft)


def _product_kernel(eb0, fo_ref, fr_ref, cip_ref, key_ref, *rest):
    halves = rest[: 2 * DIGITS]
    out_ref, acc_ref = rest[2 * DIGITS :]
    eb = pl.program_id(0) + eb0
    f = jnp.concatenate([fo_ref[...], fr_ref[...]], axis=1)
    acc_ref[...] = jnp.zeros_like(acc_ref)
    n = acc_ref.shape[0]
    for j in range(DIGITS):
        own_ref, recv_ref = halves[2 * j], halves[2 * j + 1]

        @pl.when(eb == j)
        def _():
            acc_ref[...] += cip_ref[...].astype(F32) * key_ref[j].astype(F32)

        @pl.when(eb != j)
        def _():
            for l in range(n):
                h = jnp.concatenate([own_ref[l], recv_ref[l]], axis=0)
                y = jnp.dot(f, h, preferred_element_type=F32).astype(BF16)
                acc_ref[l] += y.astype(F32) * key_ref[j, l].astype(F32)

    out_ref[...] = acc_ref[...].astype(BF16)


def product(cip, key, own2, recv2, f_own, f_oth, eb0, nblocks):
    _, rows, cols_l = cip.shape
    rows_l = rows // 2

    def lifted_block(j):
        def index(i):
            eb = i + eb0
            tb = jnp.where(eb < j, eb, eb - 1)
            return (j, jnp.clip(tb, 0, DIGITS - 1), 0, 0)

        return pl.BlockSpec((None, BLK, rows_l, cols_l), index)

    half_specs = []
    half_args = []
    for j in range(DIGITS):
        half_specs += [lifted_block(j), lifted_block(j)]
        half_args += [own2, recv2]
    return pl.pallas_call(
        lambda *refs: _product_kernel(eb0, *refs),
        grid=(nblocks,),
        in_specs=[
            pl.BlockSpec((rows, rows_l), lambda i: (0, 0)),
            pl.BlockSpec((rows, rows_l), lambda i: (0, 0)),
            pl.BlockSpec(
                (BLK, rows, cols_l), lambda i: (jnp.minimum(i + eb0, DIGITS - 1), 0, 0)
            ),
            pl.BlockSpec((DIGITS, BLK, rows, cols_l), lambda i: (0, i + eb0, 0, 0)),
        ]
        + half_specs,
        out_specs=pl.BlockSpec((BLK, rows, cols_l), lambda i: (i, 0, 0)),
        out_shape=jax.ShapeDtypeStruct((nblocks * BLK, rows, cols_l), BF16),
        scratch_shapes=[pltpu.VMEM((BLK, rows, cols_l), F32)],
    )(f_own, f_oth, cip, key, *half_args)


def _final_kernel(fo_ref, fr_ref, own_ref, recv_ref, prod_ref, s_ref, out_ref):
    f = jnp.concatenate([fo_ref[...], fr_ref[...]], axis=1)
    for l in range(own_ref.shape[0]):
        h = jnp.concatenate([own_ref[l], recv_ref[l]], axis=0)
        y = jnp.dot(f, h, preferred_element_type=F32).astype(BF16)
        diff = prod_ref[l].astype(F32) - y.astype(F32)
        out_ref[l] = (diff * s_ref[l]).astype(BF16)


def final(own4, recv4, prod, scale, f_own, f_oth):
    n, rows, cols_l = prod.shape
    rows_l = rows // 2
    hs = pl.BlockSpec((BLK, rows_l, cols_l), lambda i: (i, 0, 0))
    return pl.pallas_call(
        _final_kernel,
        grid=(n // BLK,),
        in_specs=[
            pl.BlockSpec((rows, rows_l), lambda i: (0, 0)),
            pl.BlockSpec((rows, rows_l), lambda i: (0, 0)),
            hs,
            hs,
            pl.BlockSpec((BLK, rows, cols_l), lambda i: (i, 0, 0)),
            pl.BlockSpec((BLK, 1, cols_l), lambda i: (i, 0, 0)),
        ],
        out_specs=pl.BlockSpec((BLK, rows, cols_l), lambda i: (i, 0, 0)),
        out_shape=jax.ShapeDtypeStruct((n, rows, cols_l), BF16),
    )(f_own, f_oth, own4, recv4, prod, scale)


def snake_ring(n):
    if n % 2:
        return list(range(n))
    outer = n // 2
    return [2 * a for a in range(outer)] + [2 * a + 1 for a in reversed(range(outer))]


def ring_setup(shard):
    n = lax.axis_size("limb")
    me_l = lax.axis_index("limb")
    order = snake_ring(n)
    pos = [0] * n
    for i, l in enumerate(order):
        pos[l] = i
    width = shard.shape[1]
    full = jnp.zeros((shard.shape[0], n * width) + shard.shape[2:], shard.dtype)
    full = lax.dynamic_update_slice_in_dim(full, shard, me_l * width, axis=1)
    return dict(
        n=n,
        order=jnp.array(order, I32),
        p=jnp.array(pos, I32)[me_l],
        cw=[(order[i], order[(i + 1) % n]) for i in range(n)],
        ccw=[(order[i], order[(i - 1) % n]) for i in range(n)],
        width=width,
        full=full,
        a=shard,
        b=shard,
        s=0,
    )


def ring_steps(st):
    return st["n"] // 2


def ring_step(st):
    n, width, order, p = st["n"], st["width"], st["order"], st["p"]
    st["s"] += 1
    s = st["s"]
    if 2 * s < n:
        st["a"] = lax.ppermute(st["a"], "limb", st["cw"])
        st["b"] = lax.ppermute(st["b"], "limb", st["ccw"])
        st["full"] = lax.dynamic_update_slice_in_dim(
            st["full"], st["a"], order[(p - s) % n] * width, axis=1
        )
        st["full"] = lax.dynamic_update_slice_in_dim(
            st["full"], st["b"], order[(p + s) % n] * width, axis=1
        )
    else:
        h = st["a"].shape[2] // 2
        a = lax.ppermute(st["a"][:, :, :h], "limb", st["cw"])
        b = lax.ppermute(st["b"][:, :, h:], "limb", st["ccw"])
        src = order[(p + s) % n] * width
        st["full"] = lax.dynamic_update_slice_in_dim(
            st["full"], jnp.concatenate([a, b], axis=2), src, axis=1
        )


def ring_hold(st, x):
    if st["s"] >= ring_steps(st):
        return x
    st["a"], st["b"], x = lax.optimization_barrier((st["a"], st["b"], x))
    ring_step(st)
    return x


def ring_finish(st):
    while st["s"] < ring_steps(st):
        ring_step(st)
    return st["full"]

def swap(x):
    return lax.ppermute(x, "coef", perm=[(0, 1), (1, 0)])


def body(cipher, switch_key, raise_table, lower_table, special_inverse):
    nc = lax.axis_size("coef")
    me = lax.axis_index("coef")
    me_arr = jnp.reshape(me, (1,)).astype(I32)
    other = 1 - me
    _, limbs, rows, cols_l = cipher.shape
    cols = cols_l * nc
    rows_l = rows // nc

    ring = ring_setup(switch_key[0])
    if ring_steps(ring):
        ring_step(ring)

    f_rows = cosine_table(rows)
    f_cols = cosine_table(cols)
    ft_rows = f_rows.T
    ft_cols = f_cols.T
    fc_own = lax.dynamic_slice_in_dim(f_cols, me * cols_l, cols_l, axis=0)
    fc_oth = lax.dynamic_slice_in_dim(f_cols, other * cols_l, cols_l, axis=0)
    fr_own = lax.dynamic_slice_in_dim(f_rows, me * rows_l, rows_l, axis=1)
    fr_oth = lax.dynamic_slice_in_dim(f_rows, other * rows_l, rows_l, axis=1)
    w_col, w_row, v_row = twiddle_tables(me, rows, cols, nc)

    ct = cipher[0]
    own1, send1 = inv_row(me_arr, ct, w_col, ft_rows, 0)
    own1 = ring_hold(ring, own1)
    coeffs = inv_col(own1, swap(send1), v_row, fc_own, fc_oth, 0)

    blocks = coeffs.reshape(DIGITS, DIGIT_LIMBS, rows_l, cols)
    raised = lax.dot_general(
        raise_table, blocks, (((2,), (1,)), ((0,), (0,))), preferred_element_type=F32
    ).astype(BF16)

    raised = ring_hold(ring, raised)
    own2, send2 = fwd_col(
        me_arr, raised, v_row, w_row, ft_cols, lambda j, t: jnp.where(t >= j, t + 1, t)
    )
    own2, send2 = ring_hold(ring, (own2, send2))
    recv2 = swap(send2)
    key = ring_finish(ring)

    prod_special = product(ct, key, own2, recv2, fr_own, fr_oth, DIGITS, 1)
    prod_cipher = product(ct, key, own2, recv2, fr_own, fr_oth, 0, DIGITS)

    own3, send3 = inv_row(me_arr, prod_special, w_col, ft_rows, limbs)
    special = inv_col(own3, swap(send3), v_row, fc_own, fc_oth, limbs)
    lowered = lax.dot_general(
        lower_table, special, (((1,), (0,)), ((), ())), preferred_element_type=F32
    )
    lowered = lowered.astype(BF16)[None]
    own4, send4 = fwd_col(me_arr, lowered, v_row, w_row, ft_cols, lambda j, t: t)
    scale = jnp.broadcast_to(special_inverse[:, None, None], (limbs, 1, cols_l))
    result = final(own4[0], swap(send4)[0], prod_cipher, scale, fr_own, fr_oth)
    return result[None, None]


def solution(mesh):
    in_specs = (
        P(("grp", "limb"), None, None, "coef"),
        P(None, None, "limb", None, "coef"),
        P(),
        P(),
        P(),
    )
    out_specs = P(None, ("grp", "limb"), None, None, "coef")
    return jax.shard_map(body, mesh=mesh, in_specs=in_specs, out_specs=out_specs, check_vma=False)
```

```python
import math

import jax
import ml_dtypes
import numpy as np
import jax.numpy as jnp
from jax import lax
from jax.experimental import pallas as pl
from jax.experimental.pallas import tpu as pltpu
from jax.sharding import PartitionSpec as P

LIMBS = 48
DIGITS = 3
DIGIT_LIMBS = 16
EXTENDED = 64
CYCLE = 32768
BLK = 16

F32 = jnp.float32
BF16 = jnp.bfloat16
I32 = jnp.int32


def cosine_table(size):
    freq = np.arange(size, dtype=np.float64)[:, None]
    place = np.arange(size, dtype=np.float64)[None, :]
    norm = np.where(freq == 0, math.sqrt(1.0 / size), math.sqrt(2.0 / size))
    return (norm * np.cos(math.pi * (2.0 * place + 1.0) * freq / (2.0 * size))).astype(
        ml_dtypes.bfloat16
    )


def _angle(phase):
    ang = (2.0 * math.pi / CYCLE) * phase.astype(F32)
    return jnp.cos(ang), jnp.sin(ang)


def _limb_angle(c):
    shape = (-1,) + (1,) * c.ndim
    hi = jnp.arange(EXTENDED // 8, dtype=I32).reshape(shape)
    lo = (2 * jnp.arange(8, dtype=I32) + 1).reshape(shape)
    ch, sh = _angle((16 * hi * c[None]) % CYCLE)
    cl, sl = _angle((lo * c[None]) % CYCLE)
    cos = ch[:, None] * cl[None] - sh[:, None] * sl[None]
    sin = sh[:, None] * cl[None] + ch[:, None] * sl[None]
    return cos.reshape((EXTENDED,) + c.shape), sin.reshape((EXTENDED,) + c.shape)


def _twiddle(p, q):
    cp, sp = _limb_angle(p % CYCLE)
    cq, sq = _limb_angle(q % CYCLE)
    cp, sp, cq, sq = lax.optimization_barrier((cp, sp, cq, sq))
    return 1.0 + 0.5 * (cp * cq - sp * sq)


def twiddle_tables(me, rows, cols, nc):
    rows_l, cols_l = rows // nc, cols // nc
    fine = jnp.arange(8, dtype=I32)[None, :, None]
    coarse = (8 * jnp.arange(rows // 8, dtype=I32))[:, None, None]
    bcol = (me * cols_l + jnp.arange(cols_l, dtype=I32))[None, None, :]
    w_col = _twiddle(coarse * bcol, fine * bcol).reshape(EXTENDED, rows, cols_l)
    coarse = (me * rows_l + 8 * jnp.arange(rows_l // 8, dtype=I32))[:, None, None]
    ball = jnp.arange(cols, dtype=I32)[None, None, :]
    w_row = _twiddle(coarse * ball, fine * ball).reshape(EXTENDED, rows_l, cols)
    v_row = _twiddle(coarse * cols + ball, fine * cols).reshape(EXTENDED, rows_l, cols)
    return w_col, w_row, v_row


SMEM_SPEC = pl.BlockSpec(memory_space=pltpu.SMEM)


def _split_store(me_ref, first, second, own_ref, send_ref):
    top = me_ref[0] == 0

    @pl.when(top)
    def _():
        own_ref[...] = first
        send_ref[...] = second

    @pl.when(jnp.logical_not(top))
    def _():
        own_ref[...] = second
        send_ref[...] = first


def _inv_row_kernel(me_ref, y_ref, w_ref, ft_ref, own_ref, send_ref, h_ref):
    ft = ft_ref[...]
    n, rows, _ = y_ref.shape
    for l in range(n):
        h = jnp.dot(ft, y_ref[l], preferred_element_type=F32)
        h_ref[l] = (h / w_ref[l]).astype(BF16)
    half = rows // 2
    _split_store(me_ref, h_ref[:, :half, :], h_ref[:, half:, :], own_ref, send_ref)


def inv_row(me_arr, y, w_col, ft, e0):
    n, rows, cols_l = y.shape
    eb0 = e0 // BLK
    blk = pl.BlockSpec((BLK, rows, cols_l), lambda i: (i, 0, 0))
    out = pl.BlockSpec((BLK, rows // 2, cols_l), lambda i: (i, 0, 0))
    return pl.pallas_call(
        _inv_row_kernel,
        grid=(n // BLK,),
        in_specs=[
            SMEM_SPEC,
            blk,
            pl.BlockSpec((BLK, rows, cols_l), lambda i: (i + eb0, 0, 0)),
            pl.BlockSpec((rows, rows), lambda i: (0, 0)),
        ],
        out_specs=[out, out],
        out_shape=[jax.ShapeDtypeStruct((n, rows // 2, cols_l), BF16)] * 2,
        scratch_shapes=[pltpu.VMEM((BLK, rows, cols_l), BF16)],
    )(me_arr, y, w_col, ft)


def _inv_col_kernel(own_ref, recv_ref, v_ref, fo_ref, fr_ref, out_ref):
    n, rows_l, half = own_ref.shape
    a = own_ref[...].reshape(n * rows_l, half)
    b = recv_ref[...].reshape(n * rows_l, half)
    f = jnp.concatenate([fo_ref[...], fr_ref[...]], axis=0)
    x = jnp.dot(jnp.concatenate([a, b], axis=1), f, preferred_element_type=F32)
    x = x.reshape(n, rows_l, -1)
    out_ref[...] = (x / v_ref[...]).astype(BF16)


def inv_col(own, recv, v_row, f_own, f_oth, e0):
    n, rows_l, half = own.shape
    cols = 2 * half
    eb0 = e0 // BLK
    blk = pl.BlockSpec((BLK, rows_l, half), lambda i: (i, 0, 0))
    return pl.pallas_call(
        _inv_col_kernel,
        grid=(n // BLK,),
        in_specs=[
            blk,
            blk,
            pl.BlockSpec((BLK, rows_l, cols), lambda i: (i + eb0, 0, 0)),
            pl.BlockSpec((half, cols), lambda i: (0, 0)),
            pl.BlockSpec((half, cols), lambda i: (0, 0)),
        ],
        out_specs=pl.BlockSpec((BLK, rows_l, cols), lambda i: (i, 0, 0)),
        out_shape=jax.ShapeDtypeStruct((n, rows_l, cols), BF16),
    )(own, recv, v_row, f_own, f_oth)


def _fwd_col_kernel(me_ref, x_ref, v_ref, w_ref, ft_ref, own_ref, send_ref):
    n, rows_l, cols = x_ref.shape
    g = (x_ref[...].astype(F32) * v_ref[...]).astype(BF16)
    h = jnp.dot(g.reshape(n * rows_l, cols), ft_ref[...], preferred_element_type=F32)
    h = (h.reshape(n, rows_l, cols) * w_ref[...]).astype(BF16)
    half = cols // 2
    _split_store(me_ref, h[:, :, :half], h[:, :, half:], own_ref, send_ref)


def fwd_col(me_arr, x, v_row, w_row, ft, table_block):
    groups, n, rows_l, cols = x.shape
    half = cols // 2
    xs = pl.BlockSpec((None, BLK, rows_l, cols), lambda j, t: (j, t, 0, 0))
    ts = pl.BlockSpec((BLK, rows_l, cols), lambda j, t: (table_block(j, t), 0, 0))
    os = pl.BlockSpec((None, BLK, rows_l, half), lambda j, t: (j, t, 0, 0))
    return pl.pallas_call(
        _fwd_col_kernel,
        grid=(groups, n // BLK),
        in_specs=[SMEM_SPEC, xs, ts, ts, pl.BlockSpec((cols, cols), lambda j, t: (0, 0))],
        out_specs=[os, os],
        out_shape=[jax.ShapeDtypeStruct((groups, n, rows_l, half), BF16)] * 2,
    )(me_arr, x, v_row, w_row, ft)


def _product_kernel(eb0, fo_ref, fr_ref, cip_ref, key_ref, *rest):
    halves = rest[: 2 * DIGITS]
    out_ref, acc_ref = rest[2 * DIGITS :]
    eb = pl.program_id(0) + eb0
    f = jnp.concatenate([fo_ref[...], fr_ref[...]], axis=1)
    acc_ref[...] = jnp.zeros_like(acc_ref)
    n = acc_ref.shape[0]
    for j in range(DIGITS):
        own_ref, recv_ref = halves[2 * j], halves[2 * j + 1]

        @pl.when(eb == j)
        def _():
            acc_ref[...] += cip_ref[...].astype(F32) * key_ref[j].astype(F32)

        @pl.when(eb != j)
        def _():
            for l in range(n):
                h = jnp.concatenate([own_ref[l], recv_ref[l]], axis=0)
                y = jnp.dot(f, h, preferred_element_type=F32).astype(BF16)
                acc_ref[l] += y.astype(F32) * key_ref[j, l].astype(F32)

    out_ref[...] = acc_ref[...].astype(BF16)


def product(cip, key, own2, recv2, f_own, f_oth, eb0, nblocks):
    _, rows, cols_l = cip.shape
    rows_l = rows // 2

    def lifted_block(j):
        def index(i):
            eb = i + eb0
            tb = jnp.where(eb < j, eb, eb - 1)
            return (j, jnp.clip(tb, 0, DIGITS - 1), 0, 0)

        return pl.BlockSpec((None, BLK, rows_l, cols_l), index)

    half_specs = []
    half_args = []
    for j in range(DIGITS):
        half_specs += [lifted_block(j), lifted_block(j)]
        half_args += [own2, recv2]
    return pl.pallas_call(
        lambda *refs: _product_kernel(eb0, *refs),
        grid=(nblocks,),
        in_specs=[
            pl.BlockSpec((rows, rows_l), lambda i: (0, 0)),
            pl.BlockSpec((rows, rows_l), lambda i: (0, 0)),
            pl.BlockSpec(
                (BLK, rows, cols_l), lambda i: (jnp.minimum(i + eb0, DIGITS - 1), 0, 0)
            ),
            pl.BlockSpec((DIGITS, BLK, rows, cols_l), lambda i: (0, i + eb0, 0, 0)),
        ]
        + half_specs,
        out_specs=pl.BlockSpec((BLK, rows, cols_l), lambda i: (i, 0, 0)),
        out_shape=jax.ShapeDtypeStruct((nblocks * BLK, rows, cols_l), BF16),
        scratch_shapes=[pltpu.VMEM((BLK, rows, cols_l), F32)],
    )(f_own, f_oth, cip, key, *half_args)


def _final_kernel(fo_ref, fr_ref, own_ref, recv_ref, prod_ref, s_ref, out_ref):
    f = jnp.concatenate([fo_ref[...], fr_ref[...]], axis=1)
    for l in range(own_ref.shape[0]):
        h = jnp.concatenate([own_ref[l], recv_ref[l]], axis=0)
        y = jnp.dot(f, h, preferred_element_type=F32).astype(BF16)
        diff = prod_ref[l].astype(F32) - y.astype(F32)
        out_ref[l] = (diff * s_ref[l]).astype(BF16)


def final(own4, recv4, prod, scale, f_own, f_oth):
    n, rows, cols_l = prod.shape
    rows_l = rows // 2
    hs = pl.BlockSpec((BLK, rows_l, cols_l), lambda i: (i, 0, 0))
    return pl.pallas_call(
        _final_kernel,
        grid=(n // BLK,),
        in_specs=[
            pl.BlockSpec((rows, rows_l), lambda i: (0, 0)),
            pl.BlockSpec((rows, rows_l), lambda i: (0, 0)),
            hs,
            hs,
            pl.BlockSpec((BLK, rows, cols_l), lambda i: (i, 0, 0)),
            pl.BlockSpec((BLK, 1, cols_l), lambda i: (i, 0, 0)),
        ],
        out_specs=pl.BlockSpec((BLK, rows, cols_l), lambda i: (i, 0, 0)),
        out_shape=jax.ShapeDtypeStruct((n, rows, cols_l), BF16),
    )(f_own, f_oth, own4, recv4, prod, scale)


def snake_ring(n):
    if n % 2:
        return list(range(n))
    outer = n // 2
    return [2 * a for a in range(outer)] + [2 * a + 1 for a in reversed(range(outer))]


def ring_setup(shard):
    n = lax.axis_size("limb")
    me_l = lax.axis_index("limb")
    order = snake_ring(n)
    pos = [0] * n
    for i, l in enumerate(order):
        pos[l] = i
    width = shard.shape[1]
    full = jnp.zeros((shard.shape[0], n * width) + shard.shape[2:], shard.dtype)
    full = lax.dynamic_update_slice_in_dim(full, shard, me_l * width, axis=1)
    return dict(
        n=n,
        order=jnp.array(order, I32),
        p=jnp.array(pos, I32)[me_l],
        cw=[(order[i], order[(i + 1) % n]) for i in range(n)],
        ccw=[(order[i], order[(i - 1) % n]) for i in range(n)],
        width=width,
        full=full,
        a=shard,
        b=shard,
        s=0,
    )


def ring_steps(st):
    return st["n"] // 2


def ring_step(st):
    n, width, order, p = st["n"], st["width"], st["order"], st["p"]
    st["s"] += 1
    s = st["s"]
    if 2 * s < n:
        st["a"] = lax.ppermute(st["a"], "limb", st["cw"])
        st["b"] = lax.ppermute(st["b"], "limb", st["ccw"])
        st["full"] = lax.dynamic_update_slice_in_dim(
            st["full"], st["a"], order[(p - s) % n] * width, axis=1
        )
        st["full"] = lax.dynamic_update_slice_in_dim(
            st["full"], st["b"], order[(p + s) % n] * width, axis=1
        )
    else:
        a = lax.ppermute(st["a"], "limb", st["cw"])
        src = order[(p + s) % n] * width
        st["full"] = lax.dynamic_update_slice_in_dim(st["full"], a, src, axis=1)


def ring_hold(st, x):
    if st["s"] >= ring_steps(st):
        return x
    st["a"], st["b"], x = lax.optimization_barrier((st["a"], st["b"], x))
    ring_step(st)
    return x


def ring_finish(st, x):
    while st["s"] < ring_steps(st):
        ring_step(st)
    st["full"], x = lax.optimization_barrier((st["full"], x))
    return st["full"], x

def swap(x):
    return lax.ppermute(x, "coef", perm=[(0, 1), (1, 0)])


def body(cipher, switch_key, raise_table, lower_table, special_inverse):
    nc = lax.axis_size("coef")
    me = lax.axis_index("coef")
    me_arr = jnp.reshape(me, (1,)).astype(I32)
    other = 1 - me
    _, limbs, rows, cols_l = cipher.shape
    cols = cols_l * nc
    rows_l = rows // nc

    ring = ring_setup(switch_key[0])
    if ring_steps(ring):
        ring_step(ring)

    f_rows = cosine_table(rows)
    f_cols = cosine_table(cols)
    ft_rows = f_rows.T
    ft_cols = f_cols.T
    fc_own = lax.dynamic_slice_in_dim(f_cols, me * cols_l, cols_l, axis=0)
    fc_oth = lax.dynamic_slice_in_dim(f_cols, other * cols_l, cols_l, axis=0)
    fr_own = lax.dynamic_slice_in_dim(f_rows, me * rows_l, rows_l, axis=1)
    fr_oth = lax.dynamic_slice_in_dim(f_rows, other * rows_l, rows_l, axis=1)
    w_col, w_row, v_row = twiddle_tables(me, rows, cols, nc)

    ct = cipher[0]
    own1, send1 = inv_row(me_arr, ct, w_col, ft_rows, 0)
    own1 = ring_hold(ring, own1)
    coeffs = inv_col(own1, swap(send1), v_row, fc_own, fc_oth, 0)

    coeffs = ring_hold(ring, coeffs)
    blocks = coeffs.reshape(DIGITS, DIGIT_LIMBS, rows_l, cols)
    raised = lax.dot_general(
        raise_table, blocks, (((2,), (1,)), ((0,), (0,))), preferred_element_type=F32
    ).astype(BF16)

    raised = ring_hold(ring, raised)
    own2, send2 = fwd_col(
        me_arr, raised, v_row, w_row, ft_cols, lambda j, t: jnp.where(t >= j, t + 1, t)
    )
    key, (own2, send2) = ring_finish(ring, (own2, send2))
    recv2 = swap(send2)

    prod_special = product(ct, key, own2, recv2, fr_own, fr_oth, DIGITS, 1)
    prod_cipher = product(ct, key, own2, recv2, fr_own, fr_oth, 0, DIGITS)

    own3, send3 = inv_row(me_arr, prod_special, w_col, ft_rows, limbs)
    special = inv_col(own3, swap(send3), v_row, fc_own, fc_oth, limbs)
    lowered = lax.dot_general(
        lower_table, special, (((1,), (0,)), ((), ())), preferred_element_type=F32
    )
    lowered = lowered.astype(BF16)[None]
    own4, send4 = fwd_col(me_arr, lowered, v_row, w_row, ft_cols, lambda j, t: t)
    scale = jnp.broadcast_to(special_inverse[:, None, None], (limbs, 1, cols_l))
    result = final(own4[0], swap(send4)[0], prod_cipher, scale, fr_own, fr_oth)
    return result[None, None]


def solution(mesh):
    in_specs = (
        P(("grp", "limb"), None, None, "coef"),
        P(None, None, "limb", None, "coef"),
        P(),
        P(),
        P(),
    )
    out_specs = P(None, ("grp", "limb"), None, None, "coef")
    return jax.shard_map(body, mesh=mesh, in_specs=in_specs, out_specs=out_specs, check_vma=False)
```

```python
import math

import jax
import ml_dtypes
import numpy as np
import jax.numpy as jnp
from jax import lax
from jax.experimental import pallas as pl
from jax.experimental.pallas import tpu as pltpu
from jax.sharding import PartitionSpec as P

LIMBS = 48
DIGITS = 3
DIGIT_LIMBS = 16
EXTENDED = 64
CYCLE = 32768
BLK = 16

F32 = jnp.float32
BF16 = jnp.bfloat16
I32 = jnp.int32


def cosine_table(size):
    freq = np.arange(size, dtype=np.float64)[:, None]
    place = np.arange(size, dtype=np.float64)[None, :]
    norm = np.where(freq == 0, math.sqrt(1.0 / size), math.sqrt(2.0 / size))
    return (norm * np.cos(math.pi * (2.0 * place + 1.0) * freq / (2.0 * size))).astype(
        ml_dtypes.bfloat16
    )


def _angle(phase):
    ang = (2.0 * math.pi / CYCLE) * phase.astype(F32)
    return jnp.cos(ang), jnp.sin(ang)


def _limb_angle(c):
    shape = (-1,) + (1,) * c.ndim
    hi = jnp.arange(EXTENDED // 8, dtype=I32).reshape(shape)
    lo = (2 * jnp.arange(8, dtype=I32) + 1).reshape(shape)
    ch, sh = _angle((16 * hi * c[None]) % CYCLE)
    cl, sl = _angle((lo * c[None]) % CYCLE)
    cos = ch[:, None] * cl[None] - sh[:, None] * sl[None]
    sin = sh[:, None] * cl[None] + ch[:, None] * sl[None]
    return cos.reshape((EXTENDED,) + c.shape), sin.reshape((EXTENDED,) + c.shape)


def _twiddle(p, q):
    cp, sp = _limb_angle(p % CYCLE)
    cq, sq = _limb_angle(q % CYCLE)
    cp, sp, cq, sq = lax.optimization_barrier((cp, sp, cq, sq))
    return 1.0 + 0.5 * (cp * cq - sp * sq)


def twiddle_tables(me, rows, cols, nc):
    rows_l, cols_l = rows // nc, cols // nc
    fine = jnp.arange(8, dtype=I32)[None, :, None]
    coarse = (8 * jnp.arange(rows // 8, dtype=I32))[:, None, None]
    bcol = (me * cols_l + jnp.arange(cols_l, dtype=I32))[None, None, :]
    w_col = _twiddle(coarse * bcol, fine * bcol).reshape(EXTENDED, rows, cols_l)
    coarse = (me * rows_l + 8 * jnp.arange(rows_l // 8, dtype=I32))[:, None, None]
    ball = jnp.arange(cols, dtype=I32)[None, None, :]
    w_row = _twiddle(coarse * ball, fine * ball).reshape(EXTENDED, rows_l, cols)
    v_row = _twiddle(coarse * cols + ball, fine * cols).reshape(EXTENDED, rows_l, cols)
    return w_col, w_row, v_row


SMEM_SPEC = pl.BlockSpec(memory_space=pltpu.SMEM)


def _split_store(me_ref, first, second, own_ref, send_ref):
    top = me_ref[0] == 0

    @pl.when(top)
    def _():
        own_ref[...] = first
        send_ref[...] = second

    @pl.when(jnp.logical_not(top))
    def _():
        own_ref[...] = second
        send_ref[...] = first


def _inv_row_kernel(me_ref, y_ref, w_ref, ft_ref, own_ref, send_ref, h_ref):
    ft = ft_ref[...]
    n, rows, _ = y_ref.shape
    for l in range(n):
        h = jnp.dot(ft, y_ref[l], preferred_element_type=F32)
        h_ref[l] = (h / w_ref[l]).astype(BF16)
    half = rows // 2
    _split_store(me_ref, h_ref[:, :half, :], h_ref[:, half:, :], own_ref, send_ref)


def inv_row(me_arr, y, w_col, ft, e0):
    n, rows, cols_l = y.shape
    eb0 = e0 // BLK
    blk = pl.BlockSpec((BLK, rows, cols_l), lambda i: (i, 0, 0))
    out = pl.BlockSpec((BLK, rows // 2, cols_l), lambda i: (i, 0, 0))
    return pl.pallas_call(
        _inv_row_kernel,
        grid=(n // BLK,),
        in_specs=[
            SMEM_SPEC,
            blk,
            pl.BlockSpec((BLK, rows, cols_l), lambda i: (i + eb0, 0, 0)),
            pl.BlockSpec((rows, rows), lambda i: (0, 0)),
        ],
        out_specs=[out, out],
        out_shape=[jax.ShapeDtypeStruct((n, rows // 2, cols_l), BF16)] * 2,
        scratch_shapes=[pltpu.VMEM((BLK, rows, cols_l), BF16)],
    )(me_arr, y, w_col, ft)


def _inv_col_kernel(own_ref, recv_ref, v_ref, fo_ref, fr_ref, out_ref):
    n, rows_l, half = own_ref.shape
    a = own_ref[...].reshape(n * rows_l, half)
    b = recv_ref[...].reshape(n * rows_l, half)
    f = jnp.concatenate([fo_ref[...], fr_ref[...]], axis=0)
    x = jnp.dot(jnp.concatenate([a, b], axis=1), f, preferred_element_type=F32)
    x = x.reshape(n, rows_l, -1)
    out_ref[...] = (x / v_ref[...]).astype(BF16)


def inv_col(own, recv, v_row, f_own, f_oth, e0):
    n, rows_l, half = own.shape
    cols = 2 * half
    eb0 = e0 // BLK
    blk = pl.BlockSpec((BLK, rows_l, half), lambda i: (i, 0, 0))
    return pl.pallas_call(
        _inv_col_kernel,
        grid=(n // BLK,),
        in_specs=[
            blk,
            blk,
            pl.BlockSpec((BLK, rows_l, cols), lambda i: (i + eb0, 0, 0)),
            pl.BlockSpec((half, cols), lambda i: (0, 0)),
            pl.BlockSpec((half, cols), lambda i: (0, 0)),
        ],
        out_specs=pl.BlockSpec((BLK, rows_l, cols), lambda i: (i, 0, 0)),
        out_shape=jax.ShapeDtypeStruct((n, rows_l, cols), BF16),
    )(own, recv, v_row, f_own, f_oth)


def _fwd_col_kernel(me_ref, x_ref, v_ref, w_ref, ft_ref, own_ref, send_ref):
    n, rows_l, cols = x_ref.shape
    g = (x_ref[...].astype(F32) * v_ref[...]).astype(BF16)
    h = jnp.dot(g.reshape(n * rows_l, cols), ft_ref[...], preferred_element_type=F32)
    h = (h.reshape(n, rows_l, cols) * w_ref[...]).astype(BF16)
    half = cols // 2
    _split_store(me_ref, h[:, :, :half], h[:, :, half:], own_ref, send_ref)


def fwd_col(me_arr, x, v_row, w_row, ft, table_block):
    groups, n, rows_l, cols = x.shape
    half = cols // 2
    xs = pl.BlockSpec((None, BLK, rows_l, cols), lambda j, t: (j, t, 0, 0))
    ts = pl.BlockSpec((BLK, rows_l, cols), lambda j, t: (table_block(j, t), 0, 0))
    os = pl.BlockSpec((None, BLK, rows_l, half), lambda j, t: (j, t, 0, 0))
    return pl.pallas_call(
        _fwd_col_kernel,
        grid=(groups, n // BLK),
        in_specs=[SMEM_SPEC, xs, ts, ts, pl.BlockSpec((cols, cols), lambda j, t: (0, 0))],
        out_specs=[os, os],
        out_shape=[jax.ShapeDtypeStruct((groups, n, rows_l, half), BF16)] * 2,
    )(me_arr, x, v_row, w_row, ft)


def _product_kernel(eb0, fo_ref, fr_ref, cip_ref, key_ref, *rest):
    halves = rest[: 2 * DIGITS]
    out_ref, acc_ref = rest[2 * DIGITS :]
    eb = pl.program_id(0) + eb0
    f = jnp.concatenate([fo_ref[...], fr_ref[...]], axis=1)
    acc_ref[...] = jnp.zeros_like(acc_ref)
    n = acc_ref.shape[0]
    for j in range(DIGITS):
        own_ref, recv_ref = halves[2 * j], halves[2 * j + 1]

        @pl.when(eb == j)
        def _():
            acc_ref[...] += cip_ref[...].astype(F32) * key_ref[j].astype(F32)

        @pl.when(eb != j)
        def _():
            for l in range(n):
                h = jnp.concatenate([own_ref[l], recv_ref[l]], axis=0)
                y = jnp.dot(f, h, preferred_element_type=F32).astype(BF16)
                acc_ref[l] += y.astype(F32) * key_ref[j, l].astype(F32)

    out_ref[...] = acc_ref[...].astype(BF16)


def product(cip, key, own2, recv2, f_own, f_oth, eb0, nblocks):
    _, rows, cols_l = cip.shape
    rows_l = rows // 2

    def lifted_block(j):
        def index(i):
            eb = i + eb0
            tb = jnp.where(eb < j, eb, eb - 1)
            return (j, jnp.clip(tb, 0, DIGITS - 1), 0, 0)

        return pl.BlockSpec((None, BLK, rows_l, cols_l), index)

    half_specs = []
    half_args = []
    for j in range(DIGITS):
        half_specs += [lifted_block(j), lifted_block(j)]
        half_args += [own2, recv2]
    return pl.pallas_call(
        lambda *refs: _product_kernel(eb0, *refs),
        grid=(nblocks,),
        in_specs=[
            pl.BlockSpec((rows, rows_l), lambda i: (0, 0)),
            pl.BlockSpec((rows, rows_l), lambda i: (0, 0)),
            pl.BlockSpec(
                (BLK, rows, cols_l), lambda i: (jnp.minimum(i + eb0, DIGITS - 1), 0, 0)
            ),
            pl.BlockSpec((DIGITS, BLK, rows, cols_l), lambda i: (0, i + eb0, 0, 0)),
        ]
        + half_specs,
        out_specs=pl.BlockSpec((BLK, rows, cols_l), lambda i: (i, 0, 0)),
        out_shape=jax.ShapeDtypeStruct((nblocks * BLK, rows, cols_l), BF16),
        scratch_shapes=[pltpu.VMEM((BLK, rows, cols_l), F32)],
    )(f_own, f_oth, cip, key, *half_args)


def _final_kernel(fo_ref, fr_ref, own_ref, recv_ref, prod_ref, s_ref, out_ref):
    f = jnp.concatenate([fo_ref[...], fr_ref[...]], axis=1)
    for l in range(own_ref.shape[0]):
        h = jnp.concatenate([own_ref[l], recv_ref[l]], axis=0)
        y = jnp.dot(f, h, preferred_element_type=F32).astype(BF16)
        diff = prod_ref[l].astype(F32) - y.astype(F32)
        out_ref[l] = (diff * s_ref[l]).astype(BF16)


def final(own4, recv4, prod, scale, f_own, f_oth):
    n, rows, cols_l = prod.shape
    rows_l = rows // 2
    hs = pl.BlockSpec((BLK, rows_l, cols_l), lambda i: (i, 0, 0))
    return pl.pallas_call(
        _final_kernel,
        grid=(n // BLK,),
        in_specs=[
            pl.BlockSpec((rows, rows_l), lambda i: (0, 0)),
            pl.BlockSpec((rows, rows_l), lambda i: (0, 0)),
            hs,
            hs,
            pl.BlockSpec((BLK, rows, cols_l), lambda i: (i, 0, 0)),
            pl.BlockSpec((BLK, 1, cols_l), lambda i: (i, 0, 0)),
        ],
        out_specs=pl.BlockSpec((BLK, rows, cols_l), lambda i: (i, 0, 0)),
        out_shape=jax.ShapeDtypeStruct((n, rows, cols_l), BF16),
    )(f_own, f_oth, own4, recv4, prod, scale)


def snake_ring(n):
    if n % 2:
        return list(range(n))
    outer = n // 2
    return [2 * a for a in range(outer)] + [2 * a + 1 for a in reversed(range(outer))]


def ring_setup(shard):
    n = lax.axis_size("limb")
    me_l = lax.axis_index("limb")
    order = snake_ring(n)
    pos = [0] * n
    for i, l in enumerate(order):
        pos[l] = i
    width = shard.shape[1]
    full = jnp.zeros((shard.shape[0], n * width) + shard.shape[2:], shard.dtype)
    full = lax.dynamic_update_slice_in_dim(full, shard, me_l * width, axis=1)
    return dict(
        n=n,
        order=jnp.array(order, I32),
        p=jnp.array(pos, I32)[me_l],
        cw=[(order[i], order[(i + 1) % n]) for i in range(n)],
        ccw=[(order[i], order[(i - 1) % n]) for i in range(n)],
        width=width,
        full=full,
        a=shard,
        b=shard,
        s=0,
    )


def ring_steps(st):
    return st["n"] // 2


def ring_step(st):
    n, width, order, p = st["n"], st["width"], st["order"], st["p"]
    st["s"] += 1
    s = st["s"]
    if 2 * s < n:
        st["a"] = lax.ppermute(st["a"], "limb", st["cw"])
        st["b"] = lax.ppermute(st["b"], "limb", st["ccw"])
        st["full"] = lax.dynamic_update_slice_in_dim(
            st["full"], st["a"], order[(p - s) % n] * width, axis=1
        )
        st["full"] = lax.dynamic_update_slice_in_dim(
            st["full"], st["b"], order[(p + s) % n] * width, axis=1
        )
    else:
        h = st["a"].shape[2] // 2
        a = lax.ppermute(st["a"][:, :, :h], "limb", st["cw"])
        b = lax.ppermute(st["b"][:, :, h:], "limb", st["ccw"])
        src = order[(p + s) % n] * width
        st["full"] = lax.dynamic_update_slice_in_dim(
            st["full"], jnp.concatenate([a, b], axis=2), src, axis=1
        )


def ring_hold(st, x):
    if st["s"] >= ring_steps(st):
        return x
    st["a"], st["b"], x = lax.optimization_barrier((st["a"], st["b"], x))
    ring_step(st)
    return x


def ring_finish(st, x):
    while st["s"] < ring_steps(st):
        ring_step(st)
    st["full"], x = lax.optimization_barrier((st["full"], x))
    return st["full"], x

def swap(x):
    return lax.ppermute(x, "coef", perm=[(0, 1), (1, 0)])


def body(cipher, switch_key, raise_table, lower_table, special_inverse):
    nc = lax.axis_size("coef")
    me = lax.axis_index("coef")
    me_arr = jnp.reshape(me, (1,)).astype(I32)
    other = 1 - me
    _, limbs, rows, cols_l = cipher.shape
    cols = cols_l * nc
    rows_l = rows // nc

    ring = ring_setup(switch_key[0])
    if ring_steps(ring):
        ring_step(ring)

    f_rows = cosine_table(rows)
    f_cols = cosine_table(cols)
    ft_rows = f_rows.T
    ft_cols = f_cols.T
    fc_own = lax.dynamic_slice_in_dim(f_cols, me * cols_l, cols_l, axis=0)
    fc_oth = lax.dynamic_slice_in_dim(f_cols, other * cols_l, cols_l, axis=0)
    fr_own = lax.dynamic_slice_in_dim(f_rows, me * rows_l, rows_l, axis=1)
    fr_oth = lax.dynamic_slice_in_dim(f_rows, other * rows_l, rows_l, axis=1)
    w_col, w_row, v_row = twiddle_tables(me, rows, cols, nc)

    ct = cipher[0]
    own1, send1 = inv_row(me_arr, ct, w_col, ft_rows, 0)
    own1 = ring_hold(ring, own1)
    coeffs = inv_col(own1, swap(send1), v_row, fc_own, fc_oth, 0)

    coeffs = ring_hold(ring, coeffs)
    blocks = coeffs.reshape(DIGITS, DIGIT_LIMBS, rows_l, cols)
    raised = lax.dot_general(
        raise_table, blocks, (((2,), (1,)), ((0,), (0,))), preferred_element_type=F32
    ).astype(BF16)

    raised = ring_hold(ring, raised)
    own2, send2 = fwd_col(
        me_arr, raised, v_row, w_row, ft_cols, lambda j, t: jnp.where(t >= j, t + 1, t)
    )
    key, (own2, send2) = ring_finish(ring, (own2, send2))
    recv2 = swap(send2)

    prod_special = product(ct, key, own2, recv2, fr_own, fr_oth, DIGITS, 1)
    prod_cipher = product(ct, key, own2, recv2, fr_own, fr_oth, 0, DIGITS)

    own3, send3 = inv_row(me_arr, prod_special, w_col, ft_rows, limbs)
    special = inv_col(own3, swap(send3), v_row, fc_own, fc_oth, limbs)
    lowered = lax.dot_general(
        lower_table, special, (((1,), (0,)), ((), ())), preferred_element_type=F32
    )
    lowered = lowered.astype(BF16)[None]
    own4, send4 = fwd_col(me_arr, lowered, v_row, w_row, ft_cols, lambda j, t: t)
    scale = jnp.broadcast_to(special_inverse[:, None, None], (limbs, 1, cols_l))
    result = final(own4[0], swap(send4)[0], prod_cipher, scale, fr_own, fr_oth)
    return result[None, None]


def solution(mesh):
    in_specs = (
        P(("grp", "limb"), None, None, "coef"),
        P(None, None, "limb", None, "coef"),
        P(),
        P(),
        P(),
    )
    out_specs = P(None, ("grp", "limb"), None, None, "coef")
    return jax.shard_map(body, mesh=mesh, in_specs=in_specs, out_specs=out_specs, check_vma=False)
```

```python
import math

import jax
import ml_dtypes
import numpy as np
import jax.numpy as jnp
from jax import lax
from jax.experimental import pallas as pl
from jax.experimental.pallas import tpu as pltpu
from jax.sharding import PartitionSpec as P

LIMBS = 48
DIGITS = 3
DIGIT_LIMBS = 16
EXTENDED = 64
CYCLE = 32768
BLK = 16

F32 = jnp.float32
BF16 = jnp.bfloat16
I32 = jnp.int32


def cosine_table(size):
    freq = np.arange(size, dtype=np.float64)[:, None]
    place = np.arange(size, dtype=np.float64)[None, :]
    norm = np.where(freq == 0, math.sqrt(1.0 / size), math.sqrt(2.0 / size))
    return (norm * np.cos(math.pi * (2.0 * place + 1.0) * freq / (2.0 * size))).astype(
        ml_dtypes.bfloat16
    )


def _angle(phase):
    ang = (2.0 * math.pi / CYCLE) * phase.astype(F32)
    return jnp.cos(ang), jnp.sin(ang)


def _limb_angle(c):
    shape = (-1,) + (1,) * c.ndim
    hi = jnp.arange(EXTENDED // 8, dtype=I32).reshape(shape)
    lo = (2 * jnp.arange(8, dtype=I32) + 1).reshape(shape)
    ch, sh = _angle((16 * hi * c[None]) % CYCLE)
    cl, sl = _angle((lo * c[None]) % CYCLE)
    cos = ch[:, None] * cl[None] - sh[:, None] * sl[None]
    sin = sh[:, None] * cl[None] + ch[:, None] * sl[None]
    return cos.reshape((EXTENDED,) + c.shape), sin.reshape((EXTENDED,) + c.shape)


def _twiddle(p, q):
    cp, sp = _limb_angle(p % CYCLE)
    cq, sq = _limb_angle(q % CYCLE)
    cp, sp, cq, sq = lax.optimization_barrier((cp, sp, cq, sq))
    return 1.0 + 0.5 * (cp * cq - sp * sq)


def twiddle_tables(me, rows, cols, nc):
    rows_l, cols_l = rows // nc, cols // nc
    fine = jnp.arange(8, dtype=I32)[None, :, None]
    coarse = (8 * jnp.arange(rows // 8, dtype=I32))[:, None, None]
    bcol = (me * cols_l + jnp.arange(cols_l, dtype=I32))[None, None, :]
    w_col = _twiddle(coarse * bcol, fine * bcol).reshape(EXTENDED, rows, cols_l)
    coarse = (me * rows_l + 8 * jnp.arange(rows_l // 8, dtype=I32))[:, None, None]
    ball = jnp.arange(cols, dtype=I32)[None, None, :]
    w_row = _twiddle(coarse * ball, fine * ball).reshape(EXTENDED, rows_l, cols)
    v_row = _twiddle(coarse * cols + ball, fine * cols).reshape(EXTENDED, rows_l, cols)
    return w_col, w_row, v_row


SMEM_SPEC = pl.BlockSpec(memory_space=pltpu.SMEM)


def _split_store(me_ref, first, second, own_ref, send_ref):
    top = me_ref[0] == 0

    @pl.when(top)
    def _():
        own_ref[...] = first
        send_ref[...] = second

    @pl.when(jnp.logical_not(top))
    def _():
        own_ref[...] = second
        send_ref[...] = first


def _inv_row_kernel(me_ref, y_ref, w_ref, ft_ref, own_ref, send_ref, h_ref):
    ft = ft_ref[...]
    n, rows, _ = y_ref.shape
    for l in range(n):
        h = jnp.dot(ft, y_ref[l], preferred_element_type=F32)
        h_ref[l] = (h / w_ref[l]).astype(BF16)
    half = rows // 2
    _split_store(me_ref, h_ref[:, :half, :], h_ref[:, half:, :], own_ref, send_ref)


def inv_row(me_arr, y, w_col, ft, e0):
    n, rows, cols_l = y.shape
    eb0 = e0 // BLK
    blk = pl.BlockSpec((BLK, rows, cols_l), lambda i: (i, 0, 0))
    out = pl.BlockSpec((BLK, rows // 2, cols_l), lambda i: (i, 0, 0))
    return pl.pallas_call(
        _inv_row_kernel,
        grid=(n // BLK,),
        in_specs=[
            SMEM_SPEC,
            blk,
            pl.BlockSpec((BLK, rows, cols_l), lambda i: (i + eb0, 0, 0)),
            pl.BlockSpec((rows, rows), lambda i: (0, 0)),
        ],
        out_specs=[out, out],
        out_shape=[jax.ShapeDtypeStruct((n, rows // 2, cols_l), BF16)] * 2,
        scratch_shapes=[pltpu.VMEM((BLK, rows, cols_l), BF16)],
    )(me_arr, y, w_col, ft)


def _inv_col_kernel(own_ref, recv_ref, v_ref, fo_ref, fr_ref, out_ref):
    n, rows_l, half = own_ref.shape
    a = own_ref[...].reshape(n * rows_l, half)
    b = recv_ref[...].reshape(n * rows_l, half)
    f = jnp.concatenate([fo_ref[...], fr_ref[...]], axis=0)
    x = jnp.dot(jnp.concatenate([a, b], axis=1), f, preferred_element_type=F32)
    x = x.reshape(n, rows_l, -1)
    out_ref[...] = (x / v_ref[...]).astype(BF16)


def inv_col(own, recv, v_row, f_own, f_oth, e0):
    n, rows_l, half = own.shape
    cols = 2 * half
    eb0 = e0 // BLK
    blk = pl.BlockSpec((BLK, rows_l, half), lambda i: (i, 0, 0))
    return pl.pallas_call(
        _inv_col_kernel,
        grid=(n // BLK,),
        in_specs=[
            blk,
            blk,
            pl.BlockSpec((BLK, rows_l, cols), lambda i: (i + eb0, 0, 0)),
            pl.BlockSpec((half, cols), lambda i: (0, 0)),
            pl.BlockSpec((half, cols), lambda i: (0, 0)),
        ],
        out_specs=pl.BlockSpec((BLK, rows_l, cols), lambda i: (i, 0, 0)),
        out_shape=jax.ShapeDtypeStruct((n, rows_l, cols), BF16),
    )(own, recv, v_row, f_own, f_oth)


def _fwd_col_kernel(me_ref, x_ref, v_ref, w_ref, ft_ref, own_ref, send_ref):
    n, rows_l, cols = x_ref.shape
    g = (x_ref[...].astype(F32) * v_ref[...]).astype(BF16)
    h = jnp.dot(g.reshape(n * rows_l, cols), ft_ref[...], preferred_element_type=F32)
    h = (h.reshape(n, rows_l, cols) * w_ref[...]).astype(BF16)
    half = cols // 2
    _split_store(me_ref, h[:, :, :half], h[:, :, half:], own_ref, send_ref)


def fwd_col(me_arr, x, v_row, w_row, ft, table_block):
    groups, n, rows_l, cols = x.shape
    half = cols // 2
    xs = pl.BlockSpec((None, BLK, rows_l, cols), lambda j, t: (j, t, 0, 0))
    ts = pl.BlockSpec((BLK, rows_l, cols), lambda j, t: (table_block(j, t), 0, 0))
    os = pl.BlockSpec((None, BLK, rows_l, half), lambda j, t: (j, t, 0, 0))
    return pl.pallas_call(
        _fwd_col_kernel,
        grid=(groups, n // BLK),
        in_specs=[SMEM_SPEC, xs, ts, ts, pl.BlockSpec((cols, cols), lambda j, t: (0, 0))],
        out_specs=[os, os],
        out_shape=[jax.ShapeDtypeStruct((groups, n, rows_l, half), BF16)] * 2,
    )(me_arr, x, v_row, w_row, ft)


def _fwd_col_steps_kernel(sj_ref, st_ref, se_ref, me_ref, x_ref, v_ref, w_ref, ft_ref, own_ref, send_ref):
    n, rows_l, cols = x_ref.shape
    g = (x_ref[...].astype(F32) * v_ref[...]).astype(BF16)
    h = jnp.dot(g.reshape(n * rows_l, cols), ft_ref[...], preferred_element_type=F32)
    h = (h.reshape(n, rows_l, cols) * w_ref[...]).astype(BF16)
    half = cols // 2
    _split_store(me_ref, h[:, :, :half], h[:, :, half:], own_ref, send_ref)


def fwd_col_steps(me_arr, x, v_row, w_row, ft, steps):
    groups, n, rows_l, cols = x.shape
    half = cols // 2
    sj, st, se = (jnp.array([step[k] for step in steps], I32) for k in range(3))
    xs = pl.BlockSpec((None, BLK, rows_l, cols), lambda i, a, b, c: (a[i], b[i], 0, 0))
    ts = pl.BlockSpec((BLK, rows_l, cols), lambda i, a, b, c: (c[i], 0, 0))
    os = pl.BlockSpec((None, BLK, rows_l, half), lambda i, a, b, c: (a[i], b[i], 0, 0))
    grid_spec = pltpu.PrefetchScalarGridSpec(
        num_scalar_prefetch=3,
        grid=(len(steps),),
        in_specs=[
            SMEM_SPEC,
            xs,
            ts,
            ts,
            pl.BlockSpec((cols, cols), lambda i, a, b, c: (0, 0)),
        ],
        out_specs=[os, os],
    )
    return pl.pallas_call(
        _fwd_col_steps_kernel,
        grid_spec=grid_spec,
        out_shape=[jax.ShapeDtypeStruct((groups, n, rows_l, half), BF16)] * 2,
    )(sj, st, se, me_arr, x, v_row, w_row, ft)


def _product_kernel(eb0, fo_ref, fr_ref, cip_ref, key_ref, *rest):
    halves = rest[: 2 * DIGITS]
    out_ref, acc_ref = rest[2 * DIGITS :]
    eb = pl.program_id(0) + eb0
    f = jnp.concatenate([fo_ref[...], fr_ref[...]], axis=1)
    acc_ref[...] = jnp.zeros_like(acc_ref)
    n = acc_ref.shape[0]
    for j in range(DIGITS):
        own_ref, recv_ref = halves[2 * j], halves[2 * j + 1]

        @pl.when(eb == j)
        def _():
            acc_ref[...] += cip_ref[...].astype(F32) * key_ref[j].astype(F32)

        @pl.when(eb != j)
        def _():
            for l in range(n):
                h = jnp.concatenate([own_ref[l], recv_ref[l]], axis=0)
                y = jnp.dot(f, h, preferred_element_type=F32).astype(BF16)
                acc_ref[l] += y.astype(F32) * key_ref[j, l].astype(F32)

    out_ref[...] = acc_ref[...].astype(BF16)


def product(cip, key, own2, recv2, f_own, f_oth, eb0, nblocks):
    _, rows, cols_l = cip.shape
    rows_l = rows // 2

    def lifted_block(j):
        def index(i):
            eb = i + eb0
            tb = jnp.where(eb < j, eb, eb - 1)
            return (j, jnp.clip(tb, 0, DIGITS - 1), 0, 0)

        return pl.BlockSpec((None, BLK, rows_l, cols_l), index)

    half_specs = []
    half_args = []
    for j in range(DIGITS):
        half_specs += [lifted_block(j), lifted_block(j)]
        half_args += [own2, recv2]
    return pl.pallas_call(
        lambda *refs: _product_kernel(eb0, *refs),
        grid=(nblocks,),
        in_specs=[
            pl.BlockSpec((rows, rows_l), lambda i: (0, 0)),
            pl.BlockSpec((rows, rows_l), lambda i: (0, 0)),
            pl.BlockSpec(
                (BLK, rows, cols_l), lambda i: (jnp.minimum(i + eb0, DIGITS - 1), 0, 0)
            ),
            pl.BlockSpec((DIGITS, BLK, rows, cols_l), lambda i: (0, i + eb0, 0, 0)),
        ]
        + half_specs,
        out_specs=pl.BlockSpec((BLK, rows, cols_l), lambda i: (i, 0, 0)),
        out_shape=jax.ShapeDtypeStruct((nblocks * BLK, rows, cols_l), BF16),
        scratch_shapes=[pltpu.VMEM((BLK, rows, cols_l), F32)],
    )(f_own, f_oth, cip, key, *half_args)


def _final_kernel(fo_ref, fr_ref, own_ref, recv_ref, prod_ref, s_ref, out_ref):
    f = jnp.concatenate([fo_ref[...], fr_ref[...]], axis=1)
    for l in range(own_ref.shape[0]):
        h = jnp.concatenate([own_ref[l], recv_ref[l]], axis=0)
        y = jnp.dot(f, h, preferred_element_type=F32).astype(BF16)
        diff = prod_ref[l].astype(F32) - y.astype(F32)
        out_ref[l] = (diff * s_ref[l]).astype(BF16)


def final(own4, recv4, prod, scale, f_own, f_oth):
    n, rows, cols_l = prod.shape
    rows_l = rows // 2
    hs = pl.BlockSpec((BLK, rows_l, cols_l), lambda i: (i, 0, 0))
    return pl.pallas_call(
        _final_kernel,
        grid=(n // BLK,),
        in_specs=[
            pl.BlockSpec((rows, rows_l), lambda i: (0, 0)),
            pl.BlockSpec((rows, rows_l), lambda i: (0, 0)),
            hs,
            hs,
            pl.BlockSpec((BLK, rows, cols_l), lambda i: (i, 0, 0)),
            pl.BlockSpec((BLK, 1, cols_l), lambda i: (i, 0, 0)),
        ],
        out_specs=pl.BlockSpec((BLK, rows, cols_l), lambda i: (i, 0, 0)),
        out_shape=jax.ShapeDtypeStruct((n, rows, cols_l), BF16),
    )(f_own, f_oth, own4, recv4, prod, scale)


def snake_ring(n):
    if n % 2:
        return list(range(n))
    outer = n // 2
    return [2 * a for a in range(outer)] + [2 * a + 1 for a in reversed(range(outer))]


def ring_setup(shard):
    n = lax.axis_size("limb")
    me_l = lax.axis_index("limb")
    order = snake_ring(n)
    pos = [0] * n
    for i, l in enumerate(order):
        pos[l] = i
    width = shard.shape[1]
    full = jnp.zeros((shard.shape[0], n * width) + shard.shape[2:], shard.dtype)
    full = lax.dynamic_update_slice_in_dim(full, shard, me_l * width, axis=1)
    return dict(
        n=n,
        order=jnp.array(order, I32),
        p=jnp.array(pos, I32)[me_l],
        cw=[(order[i], order[(i + 1) % n]) for i in range(n)],
        ccw=[(order[i], order[(i - 1) % n]) for i in range(n)],
        width=width,
        full=full,
        a=shard,
        b=shard,
        s=0,
    )


def ring_steps(st):
    return st["n"] // 2


def ring_step(st):
    n, width, order, p = st["n"], st["width"], st["order"], st["p"]
    st["s"] += 1
    s = st["s"]
    if 2 * s < n:
        st["a"] = lax.ppermute(st["a"], "limb", st["cw"])
        st["b"] = lax.ppermute(st["b"], "limb", st["ccw"])
        st["full"] = lax.dynamic_update_slice_in_dim(
            st["full"], st["a"], order[(p - s) % n] * width, axis=1
        )
        st["full"] = lax.dynamic_update_slice_in_dim(
            st["full"], st["b"], order[(p + s) % n] * width, axis=1
        )
    else:
        h = st["a"].shape[2] // 2
        a = lax.ppermute(st["a"][:, :, :h], "limb", st["cw"])
        b = lax.ppermute(st["b"][:, :, h:], "limb", st["ccw"])
        src = order[(p + s) % n] * width
        st["full"] = lax.dynamic_update_slice_in_dim(
            st["full"], jnp.concatenate([a, b], axis=2), src, axis=1
        )


def ring_hold(st, x):
    if st["s"] >= ring_steps(st):
        return x
    st["a"], st["b"], x = lax.optimization_barrier((st["a"], st["b"], x))
    ring_step(st)
    return x


def ring_finish(st, x):
    while st["s"] < ring_steps(st):
        ring_step(st)
    st["full"], x = lax.optimization_barrier((st["full"], x))
    return st["full"], x

def swap(x):
    return lax.ppermute(x, "coef", perm=[(0, 1), (1, 0)])


def body(cipher, switch_key, raise_table, lower_table, special_inverse):
    nc = lax.axis_size("coef")
    me = lax.axis_index("coef")
    me_arr = jnp.reshape(me, (1,)).astype(I32)
    other = 1 - me
    _, limbs, rows, cols_l = cipher.shape
    cols = cols_l * nc
    rows_l = rows // nc

    ring = ring_setup(switch_key[0])
    if ring_steps(ring):
        ring_step(ring)

    f_rows = cosine_table(rows)
    f_cols = cosine_table(cols)
    ft_rows = f_rows.T
    ft_cols = f_cols.T
    fc_own = lax.dynamic_slice_in_dim(f_cols, me * cols_l, cols_l, axis=0)
    fc_oth = lax.dynamic_slice_in_dim(f_cols, other * cols_l, cols_l, axis=0)
    fr_own = lax.dynamic_slice_in_dim(f_rows, me * rows_l, rows_l, axis=1)
    fr_oth = lax.dynamic_slice_in_dim(f_rows, other * rows_l, rows_l, axis=1)
    w_col, w_row, v_row = twiddle_tables(me, rows, cols, nc)

    ct = cipher[0]
    own1, send1 = inv_row(me_arr, ct, w_col, ft_rows, 0)
    own1 = ring_hold(ring, own1)
    coeffs = inv_col(own1, swap(send1), v_row, fc_own, fc_oth, 0)

    coeffs = ring_hold(ring, coeffs)
    blocks = coeffs.reshape(DIGITS, DIGIT_LIMBS, rows_l, cols)
    raised = lax.dot_general(
        raise_table, blocks, (((2,), (1,)), ((0,), (0,))), preferred_element_type=F32
    ).astype(BF16)

    raised = ring_hold(ring, raised)
    digit_steps = []
    for eb in range(EXTENDED // BLK):
        for j in range(DIGITS):
            if j != eb:
                digit_steps.append((j, eb if eb < j else eb - 1, eb))
    own2, send2 = fwd_col_steps(me_arr, raised, v_row, w_row, ft_cols, digit_steps)
    key, (own2, send2) = ring_finish(ring, (own2, send2))
    recv2 = swap(send2)

    prod_special = product(ct, key, own2, recv2, fr_own, fr_oth, DIGITS, 1)
    prod_cipher = product(ct, key, own2, recv2, fr_own, fr_oth, 0, DIGITS)

    own3, send3 = inv_row(me_arr, prod_special, w_col, ft_rows, limbs)
    special = inv_col(own3, swap(send3), v_row, fc_own, fc_oth, limbs)
    lowered = lax.dot_general(
        lower_table, special, (((1,), (0,)), ((), ())), preferred_element_type=F32
    )
    lowered = lowered.astype(BF16)[None]
    own4, send4 = fwd_col(me_arr, lowered, v_row, w_row, ft_cols, lambda j, t: t)
    scale = jnp.broadcast_to(special_inverse[:, None, None], (limbs, 1, cols_l))
    result = final(own4[0], swap(send4)[0], prod_cipher, scale, fr_own, fr_oth)
    return result[None, None]


def solution(mesh):
    in_specs = (
        P(("grp", "limb"), None, None, "coef"),
        P(None, None, "limb", None, "coef"),
        P(),
        P(),
        P(),
    )
    out_specs = P(None, ("grp", "limb"), None, None, "coef")
    return jax.shard_map(body, mesh=mesh, in_specs=in_specs, out_specs=out_specs, check_vma=False)
```

```python
import math

import jax
import ml_dtypes
import numpy as np
import jax.numpy as jnp
from jax import lax
from jax.experimental import pallas as pl
from jax.experimental.pallas import tpu as pltpu
from jax.sharding import PartitionSpec as P

LIMBS = 48
DIGITS = 3
DIGIT_LIMBS = 16
EXTENDED = 64
CYCLE = 32768
BLK = 16

F32 = jnp.float32
BF16 = jnp.bfloat16
I32 = jnp.int32


def cosine_table(size):
    freq = np.arange(size, dtype=np.float64)[:, None]
    place = np.arange(size, dtype=np.float64)[None, :]
    norm = np.where(freq == 0, math.sqrt(1.0 / size), math.sqrt(2.0 / size))
    return (norm * np.cos(math.pi * (2.0 * place + 1.0) * freq / (2.0 * size))).astype(
        ml_dtypes.bfloat16
    )


def _angle(phase):
    ang = (2.0 * math.pi / CYCLE) * phase.astype(F32)
    return jnp.cos(ang), jnp.sin(ang)


def _limb_angle(c):
    shape = (-1,) + (1,) * c.ndim
    hi = jnp.arange(EXTENDED // 8, dtype=I32).reshape(shape)
    lo = (2 * jnp.arange(8, dtype=I32) + 1).reshape(shape)
    ch, sh = _angle((16 * hi * c[None]) % CYCLE)
    cl, sl = _angle((lo * c[None]) % CYCLE)
    cos = ch[:, None] * cl[None] - sh[:, None] * sl[None]
    sin = sh[:, None] * cl[None] + ch[:, None] * sl[None]
    return cos.reshape((EXTENDED,) + c.shape), sin.reshape((EXTENDED,) + c.shape)


def _twiddle(p, q):
    cp, sp = _limb_angle(p % CYCLE)
    cq, sq = _limb_angle(q % CYCLE)
    cp, sp, cq, sq = lax.optimization_barrier((cp, sp, cq, sq))
    return 1.0 + 0.5 * (cp * cq - sp * sq)


def twiddle_tables(me, rows, cols, nc):
    rows_l, cols_l = rows // nc, cols // nc
    fine = jnp.arange(8, dtype=I32)[None, :, None]
    coarse = (8 * jnp.arange(rows // 8, dtype=I32))[:, None, None]
    bcol = (me * cols_l + jnp.arange(cols_l, dtype=I32))[None, None, :]
    w_col = _twiddle(coarse * bcol, fine * bcol).reshape(EXTENDED, rows, cols_l)
    coarse = (me * rows_l + 8 * jnp.arange(rows_l // 8, dtype=I32))[:, None, None]
    ball = jnp.arange(cols, dtype=I32)[None, None, :]
    w_row = _twiddle(coarse * ball, fine * ball).reshape(EXTENDED, rows_l, cols)
    v_row = _twiddle(coarse * cols + ball, fine * cols).reshape(EXTENDED, rows_l, cols)
    return w_col, w_row, v_row


SMEM_SPEC = pl.BlockSpec(memory_space=pltpu.SMEM)


def _split_store(me_ref, first, second, own_ref, send_ref):
    top = me_ref[0] == 0

    @pl.when(top)
    def _():
        own_ref[...] = first
        send_ref[...] = second

    @pl.when(jnp.logical_not(top))
    def _():
        own_ref[...] = second
        send_ref[...] = first


def _inv_row_kernel(me_ref, y_ref, w_ref, ft_ref, own_ref, send_ref, h_ref):
    ft = ft_ref[...]
    n, rows, _ = y_ref.shape
    for l in range(n):
        h = jnp.dot(ft, y_ref[l], preferred_element_type=F32)
        h_ref[l] = (h / w_ref[l]).astype(BF16)
    half = rows // 2
    _split_store(me_ref, h_ref[:, :half, :], h_ref[:, half:, :], own_ref, send_ref)


def inv_row(me_arr, y, w_col, ft, e0):
    n, rows, cols_l = y.shape
    eb0 = e0 // BLK
    blk = pl.BlockSpec((BLK, rows, cols_l), lambda i: (i, 0, 0))
    out = pl.BlockSpec((BLK, rows // 2, cols_l), lambda i: (i, 0, 0))
    return pl.pallas_call(
        _inv_row_kernel,
        grid=(n // BLK,),
        in_specs=[
            SMEM_SPEC,
            blk,
            pl.BlockSpec((BLK, rows, cols_l), lambda i: (i + eb0, 0, 0)),
            pl.BlockSpec((rows, rows), lambda i: (0, 0)),
        ],
        out_specs=[out, out],
        out_shape=[jax.ShapeDtypeStruct((n, rows // 2, cols_l), BF16)] * 2,
        scratch_shapes=[pltpu.VMEM((BLK, rows, cols_l), BF16)],
    )(me_arr, y, w_col, ft)


def _inv_col_kernel(own_ref, recv_ref, v_ref, fo_ref, fr_ref, out_ref):
    n, rows_l, half = own_ref.shape
    a = own_ref[...].reshape(n * rows_l, half)
    b = recv_ref[...].reshape(n * rows_l, half)
    f = jnp.concatenate([fo_ref[...], fr_ref[...]], axis=0)
    x = jnp.dot(jnp.concatenate([a, b], axis=1), f, preferred_element_type=F32)
    x = x.reshape(n, rows_l, -1)
    out_ref[...] = (x / v_ref[...]).astype(BF16)


def inv_col(own, recv, v_row, f_own, f_oth, e0):
    n, rows_l, half = own.shape
    cols = 2 * half
    eb0 = e0 // BLK
    blk = pl.BlockSpec((BLK, rows_l, half), lambda i: (i, 0, 0))
    return pl.pallas_call(
        _inv_col_kernel,
        grid=(n // BLK,),
        in_specs=[
            blk,
            blk,
            pl.BlockSpec((BLK, rows_l, cols), lambda i: (i + eb0, 0, 0)),
            pl.BlockSpec((half, cols), lambda i: (0, 0)),
            pl.BlockSpec((half, cols), lambda i: (0, 0)),
        ],
        out_specs=pl.BlockSpec((BLK, rows_l, cols), lambda i: (i, 0, 0)),
        out_shape=jax.ShapeDtypeStruct((n, rows_l, cols), BF16),
    )(own, recv, v_row, f_own, f_oth)


def _fwd_col_kernel(me_ref, x_ref, v_ref, w_ref, ft_ref, own_ref, send_ref):
    n, rows_l, cols = x_ref.shape
    g = (x_ref[...].astype(F32) * v_ref[...]).astype(BF16)
    h = jnp.dot(g.reshape(n * rows_l, cols), ft_ref[...], preferred_element_type=F32)
    h = (h.reshape(n, rows_l, cols) * w_ref[...]).astype(BF16)
    half = cols // 2
    _split_store(me_ref, h[:, :, :half], h[:, :, half:], own_ref, send_ref)


def fwd_col(me_arr, x, v_row, w_row, ft, table_block):
    groups, n, rows_l, cols = x.shape
    half = cols // 2
    xs = pl.BlockSpec((None, BLK, rows_l, cols), lambda j, t: (j, t, 0, 0))
    ts = pl.BlockSpec((BLK, rows_l, cols), lambda j, t: (table_block(j, t), 0, 0))
    os = pl.BlockSpec((None, BLK, rows_l, half), lambda j, t: (j, t, 0, 0))
    return pl.pallas_call(
        _fwd_col_kernel,
        grid=(groups, n // BLK),
        in_specs=[SMEM_SPEC, xs, ts, ts, pl.BlockSpec((cols, cols), lambda j, t: (0, 0))],
        out_specs=[os, os],
        out_shape=[jax.ShapeDtypeStruct((groups, n, rows_l, half), BF16)] * 2,
    )(me_arr, x, v_row, w_row, ft)


def _fwd_col_steps_kernel(sj_ref, st_ref, se_ref, me_ref, x_ref, v_ref, w_ref, ft_ref, own_ref, send_ref):
    n, rows_l, cols = x_ref.shape
    g = (x_ref[...].astype(F32) * v_ref[...]).astype(BF16)
    h = jnp.dot(g.reshape(n * rows_l, cols), ft_ref[...], preferred_element_type=F32)
    h = (h.reshape(n, rows_l, cols) * w_ref[...]).astype(BF16)
    half = cols // 2
    _split_store(me_ref, h[:, :, :half], h[:, :, half:], own_ref, send_ref)


def fwd_col_steps(me_arr, x, v_row, w_row, ft, steps):
    groups, n, rows_l, cols = x.shape
    half = cols // 2
    sj, st, se = (jnp.array([step[k] for step in steps], I32) for k in range(3))
    xs = pl.BlockSpec((None, BLK, rows_l, cols), lambda i, a, b, c: (a[i], b[i], 0, 0))
    ts = pl.BlockSpec((BLK, rows_l, cols), lambda i, a, b, c: (c[i], 0, 0))
    os = pl.BlockSpec((None, BLK, rows_l, half), lambda i, a, b, c: (a[i], b[i], 0, 0))
    grid_spec = pltpu.PrefetchScalarGridSpec(
        num_scalar_prefetch=3,
        grid=(len(steps),),
        in_specs=[
            SMEM_SPEC,
            xs,
            ts,
            ts,
            pl.BlockSpec((cols, cols), lambda i, a, b, c: (0, 0)),
        ],
        out_specs=[os, os],
    )
    return pl.pallas_call(
        _fwd_col_steps_kernel,
        grid_spec=grid_spec,
        out_shape=[jax.ShapeDtypeStruct((groups, n, rows_l, half), BF16)] * 2,
    )(sj, st, se, me_arr, x, v_row, w_row, ft)


def _product_kernel(eb0, fo_ref, fr_ref, cip_ref, key_ref, *rest):
    halves = rest[: 2 * DIGITS]
    out_ref, acc_ref = rest[2 * DIGITS :]
    eb = pl.program_id(0) + eb0
    f = jnp.concatenate([fo_ref[...], fr_ref[...]], axis=1)
    acc_ref[...] = jnp.zeros_like(acc_ref)
    n = acc_ref.shape[0]
    for j in range(DIGITS):
        own_ref, recv_ref = halves[2 * j], halves[2 * j + 1]

        @pl.when(eb == j)
        def _():
            acc_ref[...] += cip_ref[...].astype(F32) * key_ref[j].astype(F32)

        @pl.when(eb != j)
        def _():
            for l in range(n):
                h = jnp.concatenate([own_ref[l], recv_ref[l]], axis=0)
                y = jnp.dot(f, h, preferred_element_type=F32).astype(BF16)
                acc_ref[l] += y.astype(F32) * key_ref[j, l].astype(F32)

    out_ref[...] = acc_ref[...].astype(BF16)


def product(cip, key, own2, recv2, f_own, f_oth, eb0, nblocks):
    _, rows, cols_l = cip.shape
    rows_l = rows // 2

    def lifted_block(j):
        def index(i):
            eb = i + eb0
            tb = jnp.where(eb < j, eb, eb - 1)
            return (j, jnp.clip(tb, 0, DIGITS - 1), 0, 0)

        return pl.BlockSpec((None, BLK, rows_l, cols_l), index)

    half_specs = []
    half_args = []
    for j in range(DIGITS):
        half_specs += [lifted_block(j), lifted_block(j)]
        half_args += [own2, recv2]
    return pl.pallas_call(
        lambda *refs: _product_kernel(eb0, *refs),
        grid=(nblocks,),
        in_specs=[
            pl.BlockSpec((rows, rows_l), lambda i: (0, 0)),
            pl.BlockSpec((rows, rows_l), lambda i: (0, 0)),
            pl.BlockSpec(
                (BLK, rows, cols_l), lambda i: (jnp.minimum(i + eb0, DIGITS - 1), 0, 0)
            ),
            pl.BlockSpec((DIGITS, BLK, rows, cols_l), lambda i: (0, i + eb0, 0, 0)),
        ]
        + half_specs,
        out_specs=pl.BlockSpec((BLK, rows, cols_l), lambda i: (i, 0, 0)),
        out_shape=jax.ShapeDtypeStruct((nblocks * BLK, rows, cols_l), BF16),
        scratch_shapes=[pltpu.VMEM((BLK, rows, cols_l), F32)],
    )(f_own, f_oth, cip, key, *half_args)


def _final_kernel(fo_ref, fr_ref, own_ref, recv_ref, prod_ref, s_ref, out_ref):
    f = jnp.concatenate([fo_ref[...], fr_ref[...]], axis=1)
    for l in range(own_ref.shape[0]):
        h = jnp.concatenate([own_ref[l], recv_ref[l]], axis=0)
        y = jnp.dot(f, h, preferred_element_type=F32).astype(BF16)
        diff = prod_ref[l].astype(F32) - y.astype(F32)
        out_ref[l] = (diff * s_ref[l]).astype(BF16)


def final(own4, recv4, prod, scale, f_own, f_oth):
    n, rows, cols_l = prod.shape
    rows_l = rows // 2
    hs = pl.BlockSpec((BLK, rows_l, cols_l), lambda i: (i, 0, 0))
    return pl.pallas_call(
        _final_kernel,
        grid=(n // BLK,),
        in_specs=[
            pl.BlockSpec((rows, rows_l), lambda i: (0, 0)),
            pl.BlockSpec((rows, rows_l), lambda i: (0, 0)),
            hs,
            hs,
            pl.BlockSpec((BLK, rows, cols_l), lambda i: (i, 0, 0)),
            pl.BlockSpec((BLK, 1, cols_l), lambda i: (i, 0, 0)),
        ],
        out_specs=pl.BlockSpec((BLK, rows, cols_l), lambda i: (i, 0, 0)),
        out_shape=jax.ShapeDtypeStruct((n, rows, cols_l), BF16),
    )(f_own, f_oth, own4, recv4, prod, scale)


def snake_ring(n):
    if n % 2:
        return list(range(n))
    outer = n // 2
    return [2 * a for a in range(outer)] + [2 * a + 1 for a in reversed(range(outer))]


def ring_setup(shard):
    n = lax.axis_size("limb")
    me_l = lax.axis_index("limb")
    order = snake_ring(n)
    pos = [0] * n
    for i, l in enumerate(order):
        pos[l] = i
    width = shard.shape[1]
    full = jnp.zeros((shard.shape[0], n * width) + shard.shape[2:], shard.dtype)
    full = lax.dynamic_update_slice_in_dim(full, shard, me_l * width, axis=1)
    return dict(
        n=n,
        order=jnp.array(order, I32),
        p=jnp.array(pos, I32)[me_l],
        cw=[(order[i], order[(i + 1) % n]) for i in range(n)],
        ccw=[(order[i], order[(i - 1) % n]) for i in range(n)],
        width=width,
        full=full,
        a=shard,
        b=shard,
        s=0,
    )


def ring_steps(st):
    return st["n"] // 2


def ring_step(st):
    n, width, order, p = st["n"], st["width"], st["order"], st["p"]
    st["s"] += 1
    s = st["s"]
    if 2 * s < n:
        st["a"] = lax.ppermute(st["a"], "limb", st["cw"])
        st["b"] = lax.ppermute(st["b"], "limb", st["ccw"])
        st["full"] = lax.dynamic_update_slice_in_dim(
            st["full"], st["a"], order[(p - s) % n] * width, axis=1
        )
        st["full"] = lax.dynamic_update_slice_in_dim(
            st["full"], st["b"], order[(p + s) % n] * width, axis=1
        )
    else:
        h = st["a"].shape[2] // 2
        a = lax.ppermute(st["a"][:, :, :h], "limb", st["cw"])
        b = lax.ppermute(st["b"][:, :, h:], "limb", st["ccw"])
        src = order[(p + s) % n] * width
        st["full"] = lax.dynamic_update_slice(st["full"], a, (0, src, 0, 0))
        st["full"] = lax.dynamic_update_slice(st["full"], b, (0, src, h, 0))


def ring_hold(st, x):
    if st["s"] >= ring_steps(st):
        return x
    st["a"], st["b"], x = lax.optimization_barrier((st["a"], st["b"], x))
    ring_step(st)
    return x


def ring_finish(st, x):
    while st["s"] < ring_steps(st):
        ring_step(st)
    st["full"], x = lax.optimization_barrier((st["full"], x))
    return st["full"], x

def swap(x):
    return lax.ppermute(x, "coef", perm=[(0, 1), (1, 0)])


def body(cipher, switch_key, raise_table, lower_table, special_inverse):
    nc = lax.axis_size("coef")
    me = lax.axis_index("coef")
    me_arr = jnp.reshape(me, (1,)).astype(I32)
    other = 1 - me
    _, limbs, rows, cols_l = cipher.shape
    cols = cols_l * nc
    rows_l = rows // nc

    ring = ring_setup(switch_key[0])
    if ring_steps(ring):
        ring_step(ring)

    f_rows = cosine_table(rows)
    f_cols = cosine_table(cols)
    ft_rows = f_rows.T
    ft_cols = f_cols.T
    fc_own = lax.dynamic_slice_in_dim(f_cols, me * cols_l, cols_l, axis=0)
    fc_oth = lax.dynamic_slice_in_dim(f_cols, other * cols_l, cols_l, axis=0)
    fr_own = lax.dynamic_slice_in_dim(f_rows, me * rows_l, rows_l, axis=1)
    fr_oth = lax.dynamic_slice_in_dim(f_rows, other * rows_l, rows_l, axis=1)
    w_col, w_row, v_row = twiddle_tables(me, rows, cols, nc)

    ct = cipher[0]
    own1, send1 = inv_row(me_arr, ct, w_col, ft_rows, 0)
    own1 = ring_hold(ring, own1)
    coeffs = inv_col(own1, swap(send1), v_row, fc_own, fc_oth, 0)

    coeffs = ring_hold(ring, coeffs)
    blocks = coeffs.reshape(DIGITS, DIGIT_LIMBS, rows_l, cols)
    raised = lax.dot_general(
        raise_table, blocks, (((2,), (1,)), ((0,), (0,))), preferred_element_type=F32
    ).astype(BF16)

    raised = ring_hold(ring, raised)
    digit_steps = []
    for eb in range(EXTENDED // BLK):
        for j in range(DIGITS):
            if j != eb:
                digit_steps.append((j, eb if eb < j else eb - 1, eb))
    own2, send2 = fwd_col_steps(me_arr, raised, v_row, w_row, ft_cols, digit_steps)
    key, (own2, send2) = ring_finish(ring, (own2, send2))
    recv2 = swap(send2)

    prod_special = product(ct, key, own2, recv2, fr_own, fr_oth, DIGITS, 1)
    prod_cipher = product(ct, key, own2, recv2, fr_own, fr_oth, 0, DIGITS)

    own3, send3 = inv_row(me_arr, prod_special, w_col, ft_rows, limbs)
    special = inv_col(own3, swap(send3), v_row, fc_own, fc_oth, limbs)
    lowered = lax.dot_general(
        lower_table, special, (((1,), (0,)), ((), ())), preferred_element_type=F32
    )
    lowered = lowered.astype(BF16)[None]
    own4, send4 = fwd_col(me_arr, lowered, v_row, w_row, ft_cols, lambda j, t: t)
    scale = jnp.broadcast_to(special_inverse[:, None, None], (limbs, 1, cols_l))
    result = final(own4[0], swap(send4)[0], prod_cipher, scale, fr_own, fr_oth)
    return result[None, None]


def solution(mesh):
    in_specs = (
        P(("grp", "limb"), None, None, "coef"),
        P(None, None, "limb", None, "coef"),
        P(),
        P(),
        P(),
    )
    out_specs = P(None, ("grp", "limb"), None, None, "coef")
    return jax.shard_map(body, mesh=mesh, in_specs=in_specs, out_specs=out_specs, check_vma=False)
```
